128 devices in a mesh: px: 8 (over y, core), py: 16 (over z, x).
Axes of the slice: x: 4, y: 4, z: 4, core: 2. Of those that a mesh axis runs over, the one named last changes fastest.
Arguments:
- kappa: bfloat16 [301056, 128], P(('px', 'py')), may hold values from -6 to 6
- send_list: int32 [128, 128, 192], P(('px', 'py')), may hold values from 0 to 2351, as said below
- dest_slot: int32 [128, 128, 192], P(('px', 'py')), may hold values from 0 to 2047, as said below
- send_count: int32 [128, 128], P(('px', 'py')), may hold values from 0 to 192, as said below
Outputs:
- flexion: float32 [4, 4096, 8192], P(None, 'px', 'py')
The draws below stay inside these ranges and needn't reach their ends.
Inputs may be any that keep to these rules, and one draw needn't show every extreme that they name: For k < send_count[a, d], send_list[a, d, k] is a row of source a's own 2352 tiles; later entries are 0. Over all sources a and k < send_count[a, d], dest_slot[a, d, k] names every slot of patch d exactly once; later entries are 0. send_count[a, d] is nonzero only where d's patch row equals a's px index or is one less; it is a multiple of 4, and reaches 192 in every draw. Summed over the sources a whose px index is one more than d's patch row, it is exactly 512.
All inputs are finite; a program needn't handle non-finite values.
Results may differ from the reference program's by a relative error of at most 0.0065.
Values may be sent and summed in bfloat16 or wider, within the bound.
No kernel may reach another device: no remote copies, remote signals or barrier semaphores. Data moves between devices by JAX's collectives and lax.ppermute only.
A program may use at most 64 MiB of HBM per device.

```python
import math
import jax
import jax.numpy as jnp
from jax import lax

PATCH_ROWS = 512
PATCH_COLS = 512
TILE = 128
TILES_ROW = 4
SLOTS = 2048
BAND_ROWS = 384
CYCLE_TILES = 49
CYCLE_MOST = 48
TILE_DEV = 2352
CAP = 192
N_PX = 8
N_PY = 16


def band_lengths(key):
    collected = []
    for band_number in range(N_PX):
        total_rows = PATCH_ROWS if band_number == N_PX - 1 else BAND_ROWS
        extra_units = total_rows - CYCLE_MOST - (N_PY - 1)
        band_key = jax.random.fold_in(key, 1000 + band_number)
        first_key, second_key = jax.random.split(band_key)
        busiest = jax.random.randint(first_key, (), 0, N_PY)
        unit_order = jax.random.permutation(second_key, (N_PY - 1) * (CYCLE_MOST - 1))
        chosen = (unit_order < extra_units).astype(jnp.int32).reshape(N_PY - 1, CYCLE_MOST - 1)
        others = 1 + jnp.sum(chosen, axis=1)
        places = jnp.arange(N_PY, dtype=jnp.int32)
        shifted = jnp.clip(places - (places > busiest).astype(jnp.int32), 0, N_PY - 2)
        collected.append(jnp.where(places == busiest, CYCLE_MOST, others[shifted]))
    return jnp.stack(collected).astype(jnp.int32)


def routing(key):
    lengths = band_lengths(jax.random.fold_in(key, 77))
    starts = jnp.cumsum(lengths, axis=1) - lengths
    src_band = jnp.arange(N_PX, dtype=jnp.int32)[:, None, None, None, None]
    dst_band = jnp.arange(N_PX, dtype=jnp.int32)[None, None, :, None, None]
    dst_col = jnp.arange(N_PY, dtype=jnp.int32)[None, None, None, :, None]
    slot_pos = jnp.arange(CAP, dtype=jnp.int32)[None, None, None, None, :]
    length = lengths[:, :, None, None, None]
    start = starts[:, :, None, None, None]
    same_row = dst_band == src_band
    row_above = dst_band == src_band - 1
    rise_count = jnp.clip(jnp.minimum(start + length, TILE) - start, 0, None) * TILES_ROW
    count = jnp.where(same_row, length * TILES_ROW, jnp.where(row_above, rise_count, 0))
    count = jnp.broadcast_to(count, (N_PX, N_PY, N_PX, N_PY, 1))
    band_local = slot_pos // TILES_ROW
    column = slot_pos % TILES_ROW
    band_row = start + band_local
    local_row = band_local * CYCLE_TILES + dst_col * (TILES_ROW - 1) + column
    patch_row = jnp.where(same_row, band_row, band_row + BAND_ROWS)
    slot_value = patch_row * TILES_ROW + column
    live_mask = slot_pos < count
    devices = N_PX * N_PY
    lists = jnp.where(live_mask, local_row, 0).astype(jnp.int32).reshape(devices, devices, CAP)
    slots = jnp.where(live_mask, slot_value, 0).astype(jnp.int32).reshape(devices, devices, CAP)
    counts = count[..., 0].astype(jnp.int32).reshape(devices, devices)
    return (lists, slots, counts)


def draw_send_list(key, part):
    return routing(key)[0]


def draw_dest_slot(key, part):
    return routing(key)[1]


def draw_send_count(key, part):
    return routing(key)[2]


def level_of(stream_key, extent, cuts, low, top_value):
    factor_of = 1.0
    for dim, blocks in cuts:
        heights = jax.random.uniform(jax.random.fold_in(jax.random.fold_in(stream_key, 6), dim), (blocks,), jnp.float32, low / len(cuts), top_value / len(cuts))
        factor_of = factor_of * jnp.repeat(jnp.exp(heights), extent[dim] // blocks).reshape((-1,) + (1,) * (len(extent) - 1 - dim))
    return factor_of


def bell_draw(key, extent, scale, reach, shards=(), kind=jnp.bfloat16):
    values = jax.random.normal(key, extent, jnp.float32) * scale
    if len(shards) > 0:
        values = level_of(key, extent, shards, -0.22, 0.18) * values
    return jnp.clip(values, min=-reach, max=reach).astype(kind)


def setup_inputs(seed: int = 0) -> dict:
    key_of = jax.random.split(jax.random.key(seed), 5)
    kappa = bell_draw(key_of[0], (N_PX * N_PY * TILE_DEV, TILE), 1.0, 6.0, ((0, 128),))
    send_list = draw_send_list(jax.random.fold_in(key_of[4], 71), 0)
    dest_slot = draw_dest_slot(jax.random.fold_in(key_of[4], 71), 0)
    send_count = draw_send_count(jax.random.fold_in(key_of[4], 71), 0)
    return dict(kappa=kappa, send_list=send_list, dest_slot=dest_slot, send_count=send_count)


def dft_tables(length):
    positions = jnp.arange(length, dtype=jnp.int32)
    phases = (positions[:, None] * positions[None, :]) % length
    angles = phases.astype(jnp.float32) * (2.0 * math.pi / length)
    return jnp.cos(angles), jnp.sin(angles)


def wavenumbers(length):
    positions = jnp.arange(length, dtype=jnp.int32)
    signed = positions - length * (positions >= (length + 1) // 2).astype(jnp.int32)
    return signed.astype(jnp.float32) * (2.0 / length)


def flexion_fields(pixels):
    row_count = pixels.shape[0]
    col_count = pixels.shape[1]
    cos_cols, sin_cols = dft_tables(col_count)
    cos_rows, sin_rows = dft_tables(row_count)
    forward_cols = jnp.concatenate([cos_cols, sin_cols], axis=1).astype(jnp.bfloat16)
    halves = jnp.dot(pixels, forward_cols, preferred_element_type=jnp.float32)
    stacked = jnp.concatenate([halves[:, :col_count], halves[:, col_count:]], axis=0).astype(jnp.bfloat16)
    forward_rows = jnp.concatenate([jnp.concatenate([cos_rows, -sin_rows], axis=1), jnp.concatenate([-sin_rows, -cos_rows], axis=1)], axis=0).astype(jnp.bfloat16)
    spectrum = jnp.dot(forward_rows, stacked, preferred_element_type=jnp.float32)
    real_part = spectrum[:row_count]
    imag_part = spectrum[row_count:]
    across = wavenumbers(col_count)[None, :]
    down = wavenumbers(row_count)[:, None]
    scale = 1.0 / (row_count * col_count)
    power = across * across + down * down
    safe_power = jnp.where(power > 0, power, 1.0)
    cube_real = across * across * across - 3.0 * across * down * down
    cube_imag = 3.0 * across * across * down - down * down * down
    one_real = (-down * real_part - across * imag_part) * scale
    one_imag = (across * real_part - down * imag_part) * scale
    kernel_real = -cube_imag / safe_power
    kernel_imag = cube_real / safe_power
    three_real = (kernel_real * real_part - kernel_imag * imag_part) * scale
    three_imag = (kernel_real * imag_part + kernel_imag * real_part) * scale
    spectra = jnp.concatenate([jnp.concatenate([one_real, three_real], axis=1), jnp.concatenate([one_imag, three_imag], axis=1)], axis=0).astype(jnp.bfloat16)
    inverse_rows = jnp.concatenate([jnp.concatenate([cos_rows, -sin_rows], axis=1), jnp.concatenate([sin_rows, cos_rows], axis=1)], axis=0).astype(jnp.bfloat16)
    columns_done = jnp.dot(inverse_rows, spectra, preferred_element_type=jnp.float32).astype(jnp.bfloat16)
    arranged = jnp.concatenate([
        jnp.concatenate([columns_done[:row_count, :col_count], columns_done[row_count:, :col_count]], axis=1),
        jnp.concatenate([columns_done[:row_count, col_count:], columns_done[row_count:, col_count:]], axis=1)], axis=0)
    inverse_cols = jnp.concatenate([jnp.concatenate([cos_cols, sin_cols], axis=1), jnp.concatenate([-sin_cols, cos_cols], axis=1)], axis=0).astype(jnp.bfloat16)
    result = jnp.dot(arranged, inverse_cols, preferred_element_type=jnp.float32)
    return jnp.stack([result[:row_count, :col_count], result[:row_count, col_count:], result[row_count:, :col_count], result[row_count:, col_count:]]).astype(jnp.bfloat16)


def blend_edges(extended, has_top, has_bottom, has_left, has_right, width):
    values = extended.astype(jnp.float32)
    row_count = values.shape[1] - 2 * width
    col_count = values.shape[2] - 2 * width
    ramp = (jnp.arange(width, dtype=jnp.float32) + 0.5) / width
    top_weight = jnp.where(has_top, ramp, 1.0)[None, :, None]
    bottom_weight = jnp.where(has_bottom, ramp[::-1], 1.0)[None, :, None]
    middle = values[:, width:width + row_count, :]
    top_band = top_weight * middle[:, :width] + (1.0 - top_weight) * values[:, :width]
    bottom_band = bottom_weight * middle[:, row_count - width:] + (1.0 - bottom_weight) * values[:, row_count + width:]
    middle = jnp.concatenate([top_band, middle[:, width:row_count - width], bottom_band], axis=1)
    left_weight = jnp.where(has_left, ramp, 1.0)[None, None, :]
    right_weight = jnp.where(has_right, ramp[::-1], 1.0)[None, None, :]
    inner = middle[:, :, width:width + col_count]
    left_band = left_weight * inner[:, :, :width] + (1.0 - left_weight) * middle[:, :, :width]
    right_band = right_weight * inner[:, :, col_count - width:] + (1.0 - right_weight) * middle[:, :, col_count + width:]
    return jnp.concatenate([left_band, inner[:, :, width:col_count - width], right_band], axis=2)


def reference(kappa, send_list, dest_slot, send_count):
    devices = N_PX * N_PY
    tile_width = kappa.shape[1]
    tile_table = kappa.reshape(devices, TILE_DEV, tile_width)
    sources = jnp.arange(devices, dtype=jnp.int32)[:, None]
    slot_depth = jnp.arange(CAP, dtype=jnp.int32)[None, :]

    def one_patch(patch_number):
        chosen = send_list[:, patch_number, :]
        tile_values = tile_table[sources, chosen]
        live_mask = slot_depth < send_count[:, patch_number][:, None]
        target = jnp.where(live_mask, dest_slot[:, patch_number, :], SLOTS)
        patch_tiles = jnp.zeros((SLOTS, tile_width), kappa.dtype).at[target.reshape(-1)].set(tile_values.reshape(-1, tile_width), mode="drop")
        return flexion_fields(patch_tiles.reshape(PATCH_ROWS, PATCH_COLS))

    numbers = jnp.arange(devices, dtype=jnp.int32)
    fields = lax.map(one_patch, numbers)
    field_grid = fields.reshape(N_PX, N_PY, 4, PATCH_ROWS, PATCH_COLS)
    padded = jnp.pad(field_grid, ((1, 1), (1, 1), (0, 0), (0, 0), (0, 0)))

    def one_blend(patch_number):
        band_index = patch_number // N_PY
        column_index = patch_number % N_PY
        zero_index = jnp.zeros((), jnp.int32)
        neighbours = lax.dynamic_slice(padded, (band_index, column_index, zero_index, zero_index, zero_index), (3, 3, 4, PATCH_ROWS, PATCH_COLS))
        stacks = []
        for offset in range(3):
            stacks.append(jnp.concatenate([neighbours[0, offset, :, PATCH_ROWS - TILE:], neighbours[1, offset], neighbours[2, offset, :, :TILE]], axis=1))
        extended = jnp.concatenate([stacks[0][:, :, PATCH_COLS - TILE:], stacks[1], stacks[2][:, :, :TILE]], axis=2)
        return blend_edges(extended, band_index > 0, band_index < N_PX - 1, column_index > 0, column_index < N_PY - 1, TILE)

    blended = lax.map(one_blend, numbers)
    blended = blended.reshape(N_PX, N_PY, 4, PATCH_ROWS, PATCH_COLS).transpose(2, 0, 3, 1, 4)
    return blended.reshape(4, N_PX * PATCH_ROWS, N_PY * PATCH_COLS)
```

```python
import math

import jax
import ml_dtypes
import numpy as np
import jax.numpy as jnp
from jax import lax
from jax.sharding import PartitionSpec as P

PATCH_ROWS = 512
PATCH_COLS = 512


def shifted(shard, axis, by):
    size = lax.axis_size(axis)
    pairs = [(i, i + by) for i in range(size) if 0 <= i + by < size]
    return lax.ppermute(shard, axis, pairs)


def padded(block, sides, width):
    for axis, dim in sides:
        count = lax.axis_size(axis)
        forward = [(i, i + 1) for i in range(count - 1)]
        backward = [(target, source) for source, target in forward]
        low = lax.ppermute(
            lax.slice_in_dim(block, block.shape[dim] - width, None, axis=dim), axis, forward
        )
        high = lax.ppermute(lax.slice_in_dim(block, 0, width, axis=dim), axis, backward)
        block = jnp.concatenate([low, block, high], axis=dim)
    return block


def dft_tables(length):
    positions = np.arange(length, dtype=np.int64)
    phases = positions[:, None] * positions[None, :] % length
    angles = phases.astype(np.float32) * np.float32(2.0 * math.pi / length)
    return (np.cos(angles).astype(np.float32), np.sin(angles).astype(np.float32))


def table(values):
    return jnp.asarray(values.astype(ml_dtypes.bfloat16))


def wavenumbers(length):
    positions = jnp.arange(length, dtype=jnp.int32)
    signed = positions - length * (positions >= (length + 1) // 2).astype(jnp.int32)
    return signed.astype(jnp.float32) * (2.0 / length)


def dot32(a, b):
    return jnp.dot(a, b, preferred_element_type=jnp.float32)


def flexion_fields(pixels):
    row_count = pixels.shape[0]
    col_count = pixels.shape[1]
    assert row_count == col_count
    cos_np, sin_np = dft_tables(row_count)
    cosine, sine = table(cos_np), table(sin_np)
    n = row_count
    halves = jnp.concatenate([dot32(pixels, cosine), dot32(pixels, sine)], axis=1).astype(
        jnp.bfloat16
    )
    by_cos = dot32(cosine, halves)
    by_sin = dot32(sine, halves)
    real_part = by_cos[:, :n] - by_sin[:, n:]
    imag_part = -(by_sin[:, :n] + by_cos[:, n:])
    across = wavenumbers(col_count)[None, :]
    down = wavenumbers(row_count)[:, None]
    scale = 1.0 / (row_count * col_count)
    power = across * across + down * down
    safe_power = jnp.where(power > 0, power, 1.0)
    cube_real = across * across * across - 3.0 * across * down * down
    cube_imag = 3.0 * across * across * down - down * down * down
    one_real = (-down * real_part - across * imag_part) * scale
    one_imag = (across * real_part - down * imag_part) * scale
    kernel_real = -cube_imag / safe_power
    kernel_imag = cube_real / safe_power
    three_real = (kernel_real * real_part - kernel_imag * imag_part) * scale
    three_imag = (kernel_real * imag_part + kernel_imag * real_part) * scale
    spectra = jnp.concatenate([one_real, three_real, one_imag, three_imag], axis=1).astype(
        jnp.bfloat16
    )
    by_cos = dot32(cosine, spectra)
    by_sin = dot32(sine, spectra)
    columns_done = jnp.concatenate(
        [
            by_cos[:, : 2 * n] - by_sin[:, 2 * n :],
            by_sin[:, : 2 * n] + by_cos[:, 2 * n :],
        ],
        axis=1,
    ).astype(jnp.bfloat16)
    arranged = jnp.concatenate(
        [columns_done[:, k * n : (k + 1) * n] for k in range(4)], axis=0
    )
    by_cos = dot32(arranged, cosine)
    by_sin = dot32(arranged, sine)
    return jnp.stack(
        [
            by_cos[:n] - by_sin[2 * n : 3 * n],
            by_sin[:n] + by_cos[2 * n : 3 * n],
            by_cos[n : 2 * n] - by_sin[3 * n :],
            by_sin[n : 2 * n] + by_cos[3 * n :],
        ]
    ).astype(jnp.bfloat16)


def blend_edges(extended, has_top, has_bottom, has_left, has_right, width):
    values = extended.astype(jnp.float32)
    row_count = values.shape[1] - 2 * width
    col_count = values.shape[2] - 2 * width
    ramp = (jnp.arange(width, dtype=jnp.float32) + 0.5) / width
    top_weight = jnp.where(has_top, ramp, 1.0)[None, :, None]
    bottom_weight = jnp.where(has_bottom, ramp[::-1], 1.0)[None, :, None]
    middle = values[:, width : width + row_count, :]
    top_band = top_weight * middle[:, :width] + (1.0 - top_weight) * values[:, :width]
    bottom_band = (
        bottom_weight * middle[:, row_count - width :]
        + (1.0 - bottom_weight) * values[:, row_count + width :]
    )
    middle = jnp.concatenate([top_band, middle[:, width : row_count - width], bottom_band], axis=1)
    left_weight = jnp.where(has_left, ramp, 1.0)[None, None, :]
    right_weight = jnp.where(has_right, ramp[::-1], 1.0)[None, None, :]
    inner = middle[:, :, width : width + col_count]
    left_band = left_weight * inner[:, :, :width] + (1.0 - left_weight) * middle[:, :, :width]
    right_band = (
        right_weight * inner[:, :, col_count - width :]
        + (1.0 - right_weight) * middle[:, :, col_count + width :]
    )
    return jnp.concatenate([left_band, inner[:, :, width : col_count - width], right_band], axis=2)


def one_hot_rows(codes, count, values):
    picks = codes[None, :] == jnp.arange(1, count + 1, dtype=jnp.int32)[:, None]
    return jnp.dot(
        picks.astype(values.dtype), values, preferred_element_type=jnp.float32
    ).astype(values.dtype)


def on_device(kappa, send_list, dest_slot, send_count):
    tile_width = kappa.shape[1]
    rows_axis = lax.axis_size("px")
    cols_axis = lax.axis_size("py")
    band_index = lax.axis_index("px")
    column_index = lax.axis_index("py")
    tile_lists = send_list[0].reshape(rows_axis, cols_axis, -1)
    slot_lists = dest_slot[0].reshape(rows_axis, cols_axis, -1)
    pair_counts = send_count[0].reshape(rows_axis, cols_axis)
    slot_depth = tile_lists.shape[2]
    upper_band = jnp.maximum(band_index - 1, 0)
    picked_lists = jnp.stack([tile_lists[band_index], tile_lists[upper_band]], axis=1)
    picked_slots = jnp.stack([slot_lists[band_index], slot_lists[upper_band]], axis=1)
    upper_counts = jnp.where(band_index > 0, pair_counts[upper_band], 0)
    picked_counts = jnp.stack([pair_counts[band_index], upper_counts], axis=1)
    live_mask = jnp.arange(slot_depth, dtype=jnp.int32)[None, None, :] < picked_counts[:, :, None]
    slot_codes = jnp.where(live_mask, picked_slots + 1, 0)
    sent_picks = picked_lists.reshape(-1)[:, None] == jnp.arange(kappa.shape[0], dtype=jnp.int32)
    sent_values = jnp.dot(
        sent_picks.astype(kappa.dtype), kappa, preferred_element_type=jnp.float32
    ).astype(kappa.dtype)
    sent_values = sent_values.reshape(cols_axis, 2, slot_depth, tile_width)
    arrived = lax.all_to_all(sent_values, "py", 0, 0, tiled=True)
    arrived_codes = lax.all_to_all(slot_codes, "py", 0, 0, tiled=True)
    rise_total = PATCH_ROWS * PATCH_COLS // tile_width // 4
    rise_codes = arrived_codes[:, 1].reshape(-1)
    rise_live = rise_codes > 0
    rise_place = jnp.where(rise_live, jnp.cumsum(rise_live.astype(jnp.int32)), 0)
    packed_values = one_hot_rows(rise_place, rise_total, arrived[:, 1].reshape(-1, tile_width))
    packed_picks = rise_place[None, :] == jnp.arange(1, rise_total + 1, dtype=jnp.int32)[:, None]
    packed_codes = jnp.sum(jnp.where(packed_picks, rise_codes[None, :], 0), axis=1)
    raised_values, raised_codes = shifted((packed_values, packed_codes), "px", -1)
    all_values = jnp.concatenate(
        [arrived[:, 0].reshape(-1, tile_width), raised_values], axis=0
    )
    all_codes = jnp.concatenate([arrived_codes[:, 0].reshape(-1), raised_codes], axis=0)
    slot_total = PATCH_ROWS * PATCH_COLS // tile_width
    patch_tiles = one_hot_rows(all_codes, slot_total, all_values)
    fields = flexion_fields(patch_tiles.reshape(PATCH_ROWS, PATCH_COLS))
    extended = padded(fields, (("px", 1), ("py", 2)), tile_width)
    return blend_edges(
        extended,
        band_index > 0,
        band_index < rows_axis - 1,
        column_index > 0,
        column_index < cols_axis - 1,
        tile_width,
    )


def solution(mesh):
    placed = (
        P(("px", "py"), None),
        P(("px", "py"), None, None),
        P(("px", "py"), None, None),
        P(("px", "py"), None),
    )
    return jax.shard_map(
        on_device, mesh=mesh, in_specs=placed, out_specs=P(None, "px", "py"), check_vma=False
    )
```

```python
import math

import jax
import ml_dtypes
import numpy as np
import jax.numpy as jnp
from jax import lax
from jax.sharding import PartitionSpec as P

PATCH_ROWS = 512
PATCH_COLS = 512


def shifted(shard, axis, by):
    size = lax.axis_size(axis)
    pairs = [(i, i + by) for i in range(size) if 0 <= i + by < size]
    return lax.ppermute(shard, axis, pairs)


def padded(block, sides, width):
    for axis, dim in sides:
        count = lax.axis_size(axis)
        forward = [(i, i + 1) for i in range(count - 1)]
        backward = [(target, source) for source, target in forward]
        low = lax.ppermute(
            lax.slice_in_dim(block, block.shape[dim] - width, None, axis=dim), axis, forward
        )
        high = lax.ppermute(lax.slice_in_dim(block, 0, width, axis=dim), axis, backward)
        block = jnp.concatenate([low, block, high], axis=dim)
    return block


def dft_tables(length):
    positions = np.arange(length, dtype=np.int64)
    phases = positions[:, None] * positions[None, :] % length
    angles = phases.astype(np.float32) * np.float32(2.0 * math.pi / length)
    return (np.cos(angles).astype(np.float32), np.sin(angles).astype(np.float32))


def table(values):
    return jnp.asarray(values.astype(ml_dtypes.bfloat16))


def wavenumbers(length):
    positions = jnp.arange(length, dtype=jnp.int32)
    signed = positions - length * (positions >= (length + 1) // 2).astype(jnp.int32)
    return signed.astype(jnp.float32) * (2.0 / length)


def dot32(a, b):
    return jnp.dot(a, b, preferred_element_type=jnp.float32)


def flexion_fields(pixels):
    row_count = pixels.shape[0]
    col_count = pixels.shape[1]
    assert row_count == col_count
    cos_np, sin_np = dft_tables(row_count)
    cosine, sine = table(cos_np), table(sin_np)
    n = row_count
    halves = jnp.concatenate([dot32(pixels, cosine), dot32(pixels, sine)], axis=1).astype(
        jnp.bfloat16
    )
    by_cos = dot32(cosine, halves)
    by_sin = dot32(sine, halves)
    real_part = by_cos[:, :n] - by_sin[:, n:]
    imag_part = -(by_sin[:, :n] + by_cos[:, n:])
    across = wavenumbers(col_count)[None, :]
    down = wavenumbers(row_count)[:, None]
    scale = 1.0 / (row_count * col_count)
    power = across * across + down * down
    safe_power = jnp.where(power > 0, power, 1.0)
    cube_real = across * across * across - 3.0 * across * down * down
    cube_imag = 3.0 * across * across * down - down * down * down
    one_real = (-down * real_part - across * imag_part) * scale
    one_imag = (across * real_part - down * imag_part) * scale
    kernel_real = -cube_imag / safe_power
    kernel_imag = cube_real / safe_power
    three_real = (kernel_real * real_part - kernel_imag * imag_part) * scale
    three_imag = (kernel_real * imag_part + kernel_imag * real_part) * scale
    spectra = jnp.concatenate([one_real, three_real, one_imag, three_imag], axis=1).astype(
        jnp.bfloat16
    )
    by_cos = dot32(cosine, spectra)
    by_sin = dot32(sine, spectra)
    columns_done = jnp.concatenate(
        [
            by_cos[:, : 2 * n] - by_sin[:, 2 * n :],
            by_sin[:, : 2 * n] + by_cos[:, 2 * n :],
        ],
        axis=1,
    ).astype(jnp.bfloat16)
    arranged = jnp.concatenate(
        [columns_done[:, k * n : (k + 1) * n] for k in range(4)], axis=0
    )
    by_cos = dot32(arranged, cosine)
    by_sin = dot32(arranged, sine)
    return jnp.stack(
        [
            by_cos[:n] - by_sin[2 * n : 3 * n],
            by_sin[:n] + by_cos[2 * n : 3 * n],
            by_cos[n : 2 * n] - by_sin[3 * n :],
            by_sin[n : 2 * n] + by_cos[3 * n :],
        ]
    ).astype(jnp.bfloat16)


def blend_edges(extended, has_top, has_bottom, has_left, has_right, width):
    values = extended.astype(jnp.float32)
    row_count = values.shape[1] - 2 * width
    col_count = values.shape[2] - 2 * width
    ramp = (jnp.arange(width, dtype=jnp.float32) + 0.5) / width
    top_weight = jnp.where(has_top, ramp, 1.0)[None, :, None]
    bottom_weight = jnp.where(has_bottom, ramp[::-1], 1.0)[None, :, None]
    middle = values[:, width : width + row_count, :]
    top_band = top_weight * middle[:, :width] + (1.0 - top_weight) * values[:, :width]
    bottom_band = (
        bottom_weight * middle[:, row_count - width :]
        + (1.0 - bottom_weight) * values[:, row_count + width :]
    )
    middle = jnp.concatenate([top_band, middle[:, width : row_count - width], bottom_band], axis=1)
    left_weight = jnp.where(has_left, ramp, 1.0)[None, None, :]
    right_weight = jnp.where(has_right, ramp[::-1], 1.0)[None, None, :]
    inner = middle[:, :, width : width + col_count]
    left_band = left_weight * inner[:, :, :width] + (1.0 - left_weight) * middle[:, :, :width]
    right_band = (
        right_weight * inner[:, :, col_count - width :]
        + (1.0 - right_weight) * middle[:, :, col_count + width :]
    )
    return jnp.concatenate([left_band, inner[:, :, width : col_count - width], right_band], axis=2)


def one_hot_rows(codes, count, values):
    picks = codes[None, :] == jnp.arange(1, count + 1, dtype=jnp.int32)[:, None]
    return jnp.dot(picks.astype(values.dtype), values, preferred_element_type=jnp.float32)


def gathered_rows(table_rows, picks):
    chosen = picks.reshape(-1)[:, None] == jnp.arange(table_rows.shape[0], dtype=jnp.int32)
    values = jnp.dot(chosen.astype(table_rows.dtype), table_rows, preferred_element_type=jnp.float32)
    return values.astype(table_rows.dtype).reshape(picks.shape + table_rows.shape[1:])


CODE_SPLIT = 64
CODE_ROWS = 16


def with_codes(values, codes):
    depth, width = values.shape[1], values.shape[2]
    halves = jnp.concatenate([codes // CODE_SPLIT, codes % CODE_SPLIT], axis=1)
    code_rows = halves.reshape(values.shape[0], -1, width).astype(values.dtype)
    pad = jnp.zeros((values.shape[0], CODE_ROWS - code_rows.shape[1], width), values.dtype)
    return jnp.concatenate([values, code_rows, pad], axis=1)


def split_codes(payload, depth):
    width = payload.shape[2]
    used = 2 * depth // width
    halves = payload[:, depth : depth + used].reshape(payload.shape[0], 2 * depth)
    halves = halves.astype(jnp.int32)
    codes = halves[:, :depth] * CODE_SPLIT + halves[:, depth:]
    return payload[:, :depth].reshape(-1, width), codes.reshape(-1)


def sent_block(kappa, lists, slots, counts):
    depth = lists.shape[1]
    live = jnp.arange(depth, dtype=jnp.int32)[None, :] < counts[:, None]
    codes = jnp.where(live, slots + 1, 0)
    return with_codes(gathered_rows(kappa, lists), codes)


def diagonal(block, row_by, col_by):
    rows, cols = lax.axis_size("px"), lax.axis_size("py")
    pairs = [
        (i * cols + j, (i + row_by) * cols + j + col_by)
        for i in range(rows)
        for j in range(cols)
        if 0 <= i + row_by < rows and 0 <= j + col_by < cols
    ]
    return lax.ppermute(block, ("px", "py"), pairs)


def row_blend(own, above, below, top_weight, bottom_weight, width):
    count = own.shape[1]
    top = top_weight * own[:, :width] + (1.0 - top_weight) * above
    bottom = bottom_weight * own[:, count - width :] + (1.0 - bottom_weight) * below
    return jnp.concatenate([top, own[:, width : count - width], bottom], axis=1)


def on_device(kappa, send_list, dest_slot, send_count):
    tile_width = kappa.shape[1]
    rows_axis = lax.axis_size("px")
    cols_axis = lax.axis_size("py")
    band_index = lax.axis_index("px")
    column_index = lax.axis_index("py")
    tile_lists = send_list[0].reshape(rows_axis, cols_axis, -1)
    slot_lists = dest_slot[0].reshape(rows_axis, cols_axis, -1)
    pair_counts = send_count[0].reshape(rows_axis, cols_axis)
    slot_depth = tile_lists.shape[2]
    upper_band = jnp.maximum(band_index - 1, 0)
    upper_counts = jnp.where(band_index > 0, pair_counts[upper_band], 0)
    same_sent = sent_block(
        kappa, tile_lists[band_index], slot_lists[band_index], pair_counts[band_index]
    )
    same_arrived = lax.all_to_all(same_sent, "py", 0, 0, tiled=True)
    rise_sent = sent_block(kappa, tile_lists[upper_band], slot_lists[upper_band], upper_counts)
    rise_arrived = lax.all_to_all(rise_sent, "py", 0, 0, tiled=True)
    same_values, same_codes = split_codes(same_arrived, slot_depth)
    rise_values, rise_codes = split_codes(rise_arrived, slot_depth)
    rise_total = PATCH_ROWS * PATCH_COLS // tile_width // 4
    rise_live = rise_codes > 0
    rise_place = jnp.where(rise_live, jnp.cumsum(rise_live.astype(jnp.int32)), 0)
    packed_values = one_hot_rows(rise_place, rise_total, rise_values).astype(kappa.dtype)
    packed_picks = rise_place[None, :] == jnp.arange(1, rise_total + 1, dtype=jnp.int32)[:, None]
    packed_codes = jnp.sum(jnp.where(packed_picks, rise_codes[None, :], 0), axis=1)
    raised_values, raised_codes = shifted((packed_values, packed_codes), "px", -1)
    slot_total = PATCH_ROWS * PATCH_COLS // tile_width
    patch_tiles = (
        one_hot_rows(same_codes, slot_total, same_values)
        + one_hot_rows(raised_codes, slot_total, raised_values)
    ).astype(kappa.dtype)
    fields = flexion_fields(patch_tiles.reshape(PATCH_ROWS, PATCH_COLS))
    width = tile_width
    last = PATCH_ROWS - width
    above = shifted(fields[:, last:], "px", 1)
    below = shifted(fields[:, :width], "px", -1)
    left = shifted(fields[:, :, last:], "py", 1)
    right = shifted(fields[:, :, :width], "py", -1)
    above_left = diagonal(fields[:, last:, last:], 1, 1)
    above_right = diagonal(fields[:, last:, :width], 1, -1)
    below_left = diagonal(fields[:, :width, last:], -1, 1)
    below_right = diagonal(fields[:, :width, :width], -1, -1)
    ramp = (jnp.arange(width, dtype=jnp.float32) + 0.5) / width
    top_weight = jnp.where(band_index > 0, ramp, 1.0)[None, :, None]
    bottom_weight = jnp.where(band_index < rows_axis - 1, ramp[::-1], 1.0)[None, :, None]
    left_weight = jnp.where(column_index > 0, ramp, 1.0)[None, None, :]
    right_weight = jnp.where(column_index < cols_axis - 1, ramp[::-1], 1.0)[None, None, :]
    f32 = lambda x: x.astype(jnp.float32)
    inner = row_blend(f32(fields), f32(above), f32(below), top_weight, bottom_weight, width)
    left_strip = row_blend(
        f32(left), f32(above_left), f32(below_left), top_weight, bottom_weight, width
    )
    right_strip = row_blend(
        f32(right), f32(above_right), f32(below_right), top_weight, bottom_weight, width
    )
    col_count = inner.shape[2]
    left_band = left_weight * inner[:, :, :width] + (1.0 - left_weight) * left_strip
    right_band = right_weight * inner[:, :, col_count - width :] + (1.0 - right_weight) * right_strip
    return jnp.concatenate(
        [left_band, inner[:, :, width : col_count - width], right_band], axis=2
    )


def solution(mesh):
    placed = (
        P(("px", "py"), None),
        P(("px", "py"), None, None),
        P(("px", "py"), None, None),
        P(("px", "py"), None),
    )
    return jax.shard_map(
        on_device, mesh=mesh, in_specs=placed, out_specs=P(None, "px", "py"), check_vma=False
    )
```

```python
import math

import jax
import ml_dtypes
import numpy as np
import jax.numpy as jnp
from jax import lax
from jax.sharding import PartitionSpec as P

PATCH_ROWS = 512
PATCH_COLS = 512


def shifted(shard, axis, by):
    size = lax.axis_size(axis)
    pairs = [(i, i + by) for i in range(size) if 0 <= i + by < size]
    return lax.ppermute(shard, axis, pairs)


def padded(block, sides, width):
    for axis, dim in sides:
        count = lax.axis_size(axis)
        forward = [(i, i + 1) for i in range(count - 1)]
        backward = [(target, source) for source, target in forward]
        low = lax.ppermute(
            lax.slice_in_dim(block, block.shape[dim] - width, None, axis=dim), axis, forward
        )
        high = lax.ppermute(lax.slice_in_dim(block, 0, width, axis=dim), axis, backward)
        block = jnp.concatenate([low, block, high], axis=dim)
    return block


def dft_tables(length):
    positions = np.arange(length, dtype=np.int64)
    phases = positions[:, None] * positions[None, :] % length
    angles = phases.astype(np.float32) * np.float32(2.0 * math.pi / length)
    return (np.cos(angles).astype(np.float32), np.sin(angles).astype(np.float32))


def table(values):
    return jnp.asarray(values.astype(ml_dtypes.bfloat16))


def wavenumbers(length):
    positions = jnp.arange(length, dtype=jnp.int32)
    signed = positions - length * (positions >= (length + 1) // 2).astype(jnp.int32)
    return signed.astype(jnp.float32) * (2.0 / length)


def dot32(a, b):
    return jnp.dot(a, b, preferred_element_type=jnp.float32)


def flexion_fields(pixels):
    row_count = pixels.shape[0]
    col_count = pixels.shape[1]
    assert row_count == col_count
    cos_np, sin_np = dft_tables(row_count)
    cosine, sine = table(cos_np), table(sin_np)
    n = row_count
    halves = jnp.concatenate([dot32(pixels, cosine), dot32(pixels, sine)], axis=1).astype(
        jnp.bfloat16
    )
    by_cos = dot32(cosine, halves)
    by_sin = dot32(sine, halves)
    real_part = by_cos[:, :n] - by_sin[:, n:]
    imag_part = -(by_sin[:, :n] + by_cos[:, n:])
    across = wavenumbers(col_count)[None, :]
    down = wavenumbers(row_count)[:, None]
    scale = 1.0 / (row_count * col_count)
    power = across * across + down * down
    safe_power = jnp.where(power > 0, power, 1.0)
    cube_real = across * across * across - 3.0 * across * down * down
    cube_imag = 3.0 * across * across * down - down * down * down
    one_real = (-down * real_part - across * imag_part) * scale
    one_imag = (across * real_part - down * imag_part) * scale
    kernel_real = -cube_imag / safe_power
    kernel_imag = cube_real / safe_power
    three_real = (kernel_real * real_part - kernel_imag * imag_part) * scale
    three_imag = (kernel_real * imag_part + kernel_imag * real_part) * scale
    spectra = jnp.concatenate([one_real, three_real, one_imag, three_imag], axis=1).astype(
        jnp.bfloat16
    )
    by_cos = dot32(cosine, spectra)
    by_sin = dot32(sine, spectra)
    columns_done = jnp.concatenate(
        [
            by_cos[:, : 2 * n] - by_sin[:, 2 * n :],
            by_sin[:, : 2 * n] + by_cos[:, 2 * n :],
        ],
        axis=1,
    ).astype(jnp.bfloat16)
    arranged = jnp.concatenate(
        [columns_done[:, k * n : (k + 1) * n] for k in range(4)], axis=0
    )
    by_cos = dot32(arranged, cosine)
    by_sin = dot32(arranged, sine)
    return jnp.stack(
        [
            by_cos[:n] - by_sin[2 * n : 3 * n],
            by_sin[:n] + by_cos[2 * n : 3 * n],
            by_cos[n : 2 * n] - by_sin[3 * n :],
            by_sin[n : 2 * n] + by_cos[3 * n :],
        ]
    ).astype(jnp.bfloat16)


def blend_edges(extended, has_top, has_bottom, has_left, has_right, width):
    values = extended.astype(jnp.float32)
    row_count = values.shape[1] - 2 * width
    col_count = values.shape[2] - 2 * width
    ramp = (jnp.arange(width, dtype=jnp.float32) + 0.5) / width
    top_weight = jnp.where(has_top, ramp, 1.0)[None, :, None]
    bottom_weight = jnp.where(has_bottom, ramp[::-1], 1.0)[None, :, None]
    middle = values[:, width : width + row_count, :]
    top_band = top_weight * middle[:, :width] + (1.0 - top_weight) * values[:, :width]
    bottom_band = (
        bottom_weight * middle[:, row_count - width :]
        + (1.0 - bottom_weight) * values[:, row_count + width :]
    )
    middle = jnp.concatenate([top_band, middle[:, width : row_count - width], bottom_band], axis=1)
    left_weight = jnp.where(has_left, ramp, 1.0)[None, None, :]
    right_weight = jnp.where(has_right, ramp[::-1], 1.0)[None, None, :]
    inner = middle[:, :, width : width + col_count]
    left_band = left_weight * inner[:, :, :width] + (1.0 - left_weight) * middle[:, :, :width]
    right_band = (
        right_weight * inner[:, :, col_count - width :]
        + (1.0 - right_weight) * middle[:, :, col_count + width :]
    )
    return jnp.concatenate([left_band, inner[:, :, width : col_count - width], right_band], axis=2)


def one_hot_rows(codes, count, values):
    picks = codes[None, :] == jnp.arange(1, count + 1, dtype=jnp.int32)[:, None]
    return jnp.dot(picks.astype(values.dtype), values, preferred_element_type=jnp.float32)


def gathered_rows(table_rows, picks):
    chosen = picks.reshape(-1)[:, None] == jnp.arange(table_rows.shape[0], dtype=jnp.int32)
    values = jnp.dot(chosen.astype(table_rows.dtype), table_rows, preferred_element_type=jnp.float32)
    return values.astype(table_rows.dtype).reshape(picks.shape + table_rows.shape[1:])


CODE_SPLIT = 64
CODE_ROWS = 16


def with_codes(values, codes):
    depth, width = values.shape[1], values.shape[2]
    halves = jnp.concatenate([codes // CODE_SPLIT, codes % CODE_SPLIT], axis=1)
    code_rows = halves.reshape(values.shape[0], -1, width).astype(values.dtype)
    pad = jnp.zeros((values.shape[0], CODE_ROWS - code_rows.shape[1], width), values.dtype)
    return jnp.concatenate([values, code_rows, pad], axis=1)


def split_codes(payload, depth):
    width = payload.shape[2]
    used = 2 * depth // width
    halves = payload[:, depth : depth + used].reshape(payload.shape[0], 2 * depth)
    halves = halves.astype(jnp.int32)
    codes = halves[:, :depth] * CODE_SPLIT + halves[:, depth:]
    return payload[:, :depth].reshape(-1, width), codes.reshape(-1)


def sent_block(kappa, lists, slots, counts):
    depth = lists.shape[1]
    live = jnp.arange(depth, dtype=jnp.int32)[None, :] < counts[:, None]
    codes = jnp.where(live, slots + 1, 0)
    return with_codes(gathered_rows(kappa, lists), codes)


def diagonal(block, row_by, col_by):
    rows, cols = lax.axis_size("px"), lax.axis_size("py")
    pairs = [
        (i * cols + j, (i + row_by) * cols + j + col_by)
        for i in range(rows)
        for j in range(cols)
        if 0 <= i + row_by < rows and 0 <= j + col_by < cols
    ]
    return lax.ppermute(block, ("px", "py"), pairs)


def row_blend(own, above, below, top_weight, bottom_weight, width):
    count = own.shape[1]
    top = top_weight * own[:, :width] + (1.0 - top_weight) * above
    bottom = bottom_weight * own[:, count - width :] + (1.0 - bottom_weight) * below
    return jnp.concatenate([top, own[:, width : count - width], bottom], axis=1)


def on_device(kappa, send_list, dest_slot, send_count):
    tile_width = kappa.shape[1]
    rows_axis = lax.axis_size("px")
    cols_axis = lax.axis_size("py")
    band_index = lax.axis_index("px")
    column_index = lax.axis_index("py")
    tile_lists = send_list[0].reshape(rows_axis, cols_axis, -1)
    slot_lists = dest_slot[0].reshape(rows_axis, cols_axis, -1)
    pair_counts = send_count[0].reshape(rows_axis, cols_axis)
    slot_depth = tile_lists.shape[2]
    upper_band = jnp.maximum(band_index - 1, 0)
    upper_counts = jnp.where(band_index > 0, pair_counts[upper_band], 0)
    same_sent = sent_block(
        kappa, tile_lists[band_index], slot_lists[band_index], pair_counts[band_index]
    )
    rise_sent = sent_block(kappa, tile_lists[upper_band], slot_lists[upper_band], upper_counts)
    arrived = lax.all_to_all(jnp.stack([same_sent, rise_sent], axis=1), "py", 0, 0, tiled=True)
    same_values, same_codes = split_codes(arrived[:, 0], slot_depth)
    rise_values, rise_codes = split_codes(arrived[:, 1], slot_depth)
    rise_total = PATCH_ROWS * PATCH_COLS // tile_width // 4
    rise_live = rise_codes > 0
    rise_place = jnp.where(rise_live, jnp.cumsum(rise_live.astype(jnp.int32)), 0)
    packed_values = one_hot_rows(rise_place, rise_total, rise_values).astype(kappa.dtype)
    packed_picks = rise_place[None, :] == jnp.arange(1, rise_total + 1, dtype=jnp.int32)[:, None]
    packed_codes = jnp.sum(jnp.where(packed_picks, rise_codes[None, :], 0), axis=1)
    packed = with_codes(packed_values.reshape(1, rise_total, tile_width), packed_codes[None])
    raised_values, raised_codes = split_codes(shifted(packed, "px", -1), rise_total)
    slot_total = PATCH_ROWS * PATCH_COLS // tile_width
    patch_tiles = (
        one_hot_rows(same_codes, slot_total, same_values)
        + one_hot_rows(raised_codes, slot_total, raised_values)
    ).astype(kappa.dtype)
    fields = flexion_fields(patch_tiles.reshape(PATCH_ROWS, PATCH_COLS))
    width = tile_width
    last = PATCH_ROWS - width
    above = shifted(fields[:, last:], "px", 1)
    below = shifted(fields[:, :width], "px", -1)
    left = shifted(fields[:, :, last:], "py", 1)
    right = shifted(fields[:, :, :width], "py", -1)
    above_left = diagonal(fields[:, last:, last:], 1, 1)
    above_right = diagonal(fields[:, last:, :width], 1, -1)
    below_left = diagonal(fields[:, :width, last:], -1, 1)
    below_right = diagonal(fields[:, :width, :width], -1, -1)
    ramp = (jnp.arange(width, dtype=jnp.float32) + 0.5) / width
    top_weight = jnp.where(band_index > 0, ramp, 1.0)[None, :, None]
    bottom_weight = jnp.where(band_index < rows_axis - 1, ramp[::-1], 1.0)[None, :, None]
    left_weight = jnp.where(column_index > 0, ramp, 1.0)[None, None, :]
    right_weight = jnp.where(column_index < cols_axis - 1, ramp[::-1], 1.0)[None, None, :]
    f32 = lambda x: x.astype(jnp.float32)
    inner = row_blend(f32(fields), f32(above), f32(below), top_weight, bottom_weight, width)
    left_strip = row_blend(
        f32(left), f32(above_left), f32(below_left), top_weight, bottom_weight, width
    )
    right_strip = row_blend(
        f32(right), f32(above_right), f32(below_right), top_weight, bottom_weight, width
    )
    col_count = inner.shape[2]
    left_band = left_weight * inner[:, :, :width] + (1.0 - left_weight) * left_strip
    right_band = right_weight * inner[:, :, col_count - width :] + (1.0 - right_weight) * right_strip
    return jnp.concatenate(
        [left_band, inner[:, :, width : col_count - width], right_band], axis=2
    )


def solution(mesh):
    placed = (
        P(("px", "py"), None),
        P(("px", "py"), None, None),
        P(("px", "py"), None, None),
        P(("px", "py"), None),
    )
    return jax.shard_map(
        on_device, mesh=mesh, in_specs=placed, out_specs=P(None, "px", "py"), check_vma=False
    )
```

```python
import math

import jax
import jax.numpy as jnp
from jax import lax
from jax.sharding import PartitionSpec as P

PATCH_ROWS = 512
PATCH_COLS = 512


def shifted(shard, axis, by):
    size = lax.axis_size(axis)
    pairs = [(i, i + by) for i in range(size) if 0 <= i + by < size]
    return lax.ppermute(shard, axis, pairs)


def padded(block, sides, width):
    for axis, dim in sides:
        count = lax.axis_size(axis)
        forward = [(i, i + 1) for i in range(count - 1)]
        backward = [(target, source) for source, target in forward]
        low = lax.ppermute(
            lax.slice_in_dim(block, block.shape[dim] - width, None, axis=dim), axis, forward
        )
        high = lax.ppermute(lax.slice_in_dim(block, 0, width, axis=dim), axis, backward)
        block = jnp.concatenate([low, block, high], axis=dim)
    return block


def dft_tables(length):
    positions = jnp.arange(length, dtype=jnp.int32)
    phases = positions[:, None] * positions[None, :] % length
    angles = phases.astype(jnp.float32) * (2.0 * math.pi / length)
    return (jnp.cos(angles), jnp.sin(angles))


def wavenumbers(length):
    positions = jnp.arange(length, dtype=jnp.int32)
    signed = positions - length * (positions >= (length + 1) // 2).astype(jnp.int32)
    return signed.astype(jnp.float32) * (2.0 / length)


def dot32(a, b):
    return jnp.dot(a, b, preferred_element_type=jnp.float32)


def flexion_fields(pixels):
    row_count = pixels.shape[0]
    col_count = pixels.shape[1]
    assert row_count == col_count
    n = row_count
    cosine, sine = dft_tables(n)
    side_by_side = jnp.concatenate([cosine, sine], axis=1).astype(jnp.bfloat16)
    stacked = jnp.concatenate([cosine, sine], axis=0).astype(jnp.bfloat16)
    halves = dot32(pixels, side_by_side).astype(jnp.bfloat16)
    products = dot32(stacked, halves)
    real_part = products[:n, :n] - products[n:, n:]
    imag_part = -(products[n:, :n] + products[:n, n:])
    across = wavenumbers(col_count)[None, :]
    down = wavenumbers(row_count)[:, None]
    scale = 1.0 / (row_count * col_count)
    power = across * across + down * down
    safe_power = jnp.where(power > 0, power, 1.0)
    cube_real = across * across * across - 3.0 * across * down * down
    cube_imag = 3.0 * across * across * down - down * down * down
    one_real = (-down * real_part - across * imag_part) * scale
    one_imag = (across * real_part - down * imag_part) * scale
    kernel_real = -cube_imag / safe_power
    kernel_imag = cube_real / safe_power
    three_real = (kernel_real * real_part - kernel_imag * imag_part) * scale
    three_imag = (kernel_real * imag_part + kernel_imag * real_part) * scale
    spectra = jnp.concatenate([one_real, three_real, one_imag, three_imag], axis=1).astype(
        jnp.bfloat16
    )
    products = dot32(stacked, spectra)
    columns_done = jnp.concatenate(
        [
            products[:n, : 2 * n] - products[n:, 2 * n :],
            products[n:, : 2 * n] + products[:n, 2 * n :],
        ],
        axis=1,
    ).astype(jnp.bfloat16)
    arranged = jnp.concatenate(
        [columns_done[:, k * n : (k + 1) * n] for k in range(4)], axis=0
    )
    products = dot32(arranged, side_by_side)
    by_cos, by_sin = products[:, :n], products[:, n:]
    return jnp.stack(
        [
            by_cos[:n] - by_sin[2 * n : 3 * n],
            by_sin[:n] + by_cos[2 * n : 3 * n],
            by_cos[n : 2 * n] - by_sin[3 * n :],
            by_sin[n : 2 * n] + by_cos[3 * n :],
        ]
    ).astype(jnp.bfloat16)


def blend_edges(extended, has_top, has_bottom, has_left, has_right, width):
    values = extended.astype(jnp.float32)
    row_count = values.shape[1] - 2 * width
    col_count = values.shape[2] - 2 * width
    ramp = (jnp.arange(width, dtype=jnp.float32) + 0.5) / width
    top_weight = jnp.where(has_top, ramp, 1.0)[None, :, None]
    bottom_weight = jnp.where(has_bottom, ramp[::-1], 1.0)[None, :, None]
    middle = values[:, width : width + row_count, :]
    top_band = top_weight * middle[:, :width] + (1.0 - top_weight) * values[:, :width]
    bottom_band = (
        bottom_weight * middle[:, row_count - width :]
        + (1.0 - bottom_weight) * values[:, row_count + width :]
    )
    middle = jnp.concatenate([top_band, middle[:, width : row_count - width], bottom_band], axis=1)
    left_weight = jnp.where(has_left, ramp, 1.0)[None, None, :]
    right_weight = jnp.where(has_right, ramp[::-1], 1.0)[None, None, :]
    inner = middle[:, :, width : width + col_count]
    left_band = left_weight * inner[:, :, :width] + (1.0 - left_weight) * middle[:, :, :width]
    right_band = (
        right_weight * inner[:, :, col_count - width :]
        + (1.0 - right_weight) * middle[:, :, col_count + width :]
    )
    return jnp.concatenate([left_band, inner[:, :, width : col_count - width], right_band], axis=2)


def one_hot_rows(codes, count, values):
    picks = codes[None, :] == jnp.arange(1, count + 1, dtype=jnp.int32)[:, None]
    return jnp.dot(picks.astype(values.dtype), values, preferred_element_type=jnp.float32)


def gathered_rows(table_rows, picks):
    chosen = picks.reshape(-1)[:, None] == jnp.arange(table_rows.shape[0], dtype=jnp.int32)
    values = jnp.dot(chosen.astype(table_rows.dtype), table_rows, preferred_element_type=jnp.float32)
    return values.astype(table_rows.dtype).reshape(picks.shape + table_rows.shape[1:])


CODE_SPLIT = 64
CODE_ROWS = 16


def with_codes(values, codes):
    depth, width = values.shape[1], values.shape[2]
    halves = jnp.concatenate([codes // CODE_SPLIT, codes % CODE_SPLIT], axis=1)
    code_rows = halves.reshape(values.shape[0], -1, width).astype(values.dtype)
    pad = jnp.zeros((values.shape[0], CODE_ROWS - code_rows.shape[1], width), values.dtype)
    return jnp.concatenate([values, code_rows, pad], axis=1)


def split_codes(payload, depth):
    width = payload.shape[2]
    used = 2 * depth // width
    halves = payload[:, depth : depth + used].reshape(payload.shape[0], 2 * depth)
    halves = halves.astype(jnp.int32)
    codes = halves[:, :depth] * CODE_SPLIT + halves[:, depth:]
    return payload[:, :depth].reshape(-1, width), codes.reshape(-1)


def sent_block(kappa, lists, slots, counts):
    depth = lists.shape[1]
    live = jnp.arange(depth, dtype=jnp.int32)[None, :] < counts[:, None]
    codes = jnp.where(live, slots + 1, 0)
    return with_codes(gathered_rows(kappa, lists), codes)


def diagonal(block, row_by, col_by):
    rows, cols = lax.axis_size("px"), lax.axis_size("py")
    pairs = [
        (i * cols + j, (i + row_by) * cols + j + col_by)
        for i in range(rows)
        for j in range(cols)
        if 0 <= i + row_by < rows and 0 <= j + col_by < cols
    ]
    return lax.ppermute(block, ("px", "py"), pairs)


def row_blend(own, above, below, top_weight, bottom_weight, width):
    count = own.shape[1]
    top = top_weight * own[:, :width] + (1.0 - top_weight) * above
    bottom = bottom_weight * own[:, count - width :] + (1.0 - bottom_weight) * below
    return jnp.concatenate([top, own[:, width : count - width], bottom], axis=1)


def on_device(kappa, send_list, dest_slot, send_count):
    tile_width = kappa.shape[1]
    rows_axis = lax.axis_size("px")
    cols_axis = lax.axis_size("py")
    band_index = lax.axis_index("px")
    column_index = lax.axis_index("py")
    tile_lists = send_list[0].reshape(rows_axis, cols_axis, -1)
    slot_lists = dest_slot[0].reshape(rows_axis, cols_axis, -1)
    pair_counts = send_count[0].reshape(rows_axis, cols_axis)
    slot_depth = tile_lists.shape[2]
    upper_band = jnp.maximum(band_index - 1, 0)
    upper_counts = jnp.where(band_index > 0, pair_counts[upper_band], 0)
    same_sent = sent_block(
        kappa, tile_lists[band_index], slot_lists[band_index], pair_counts[band_index]
    )
    rise_sent = sent_block(kappa, tile_lists[upper_band], slot_lists[upper_band], upper_counts)
    arrived = lax.all_to_all(jnp.stack([same_sent, rise_sent], axis=1), "py", 0, 0, tiled=True)
    same_values, same_codes = split_codes(arrived[:, 0], slot_depth)
    rise_values, rise_codes = split_codes(arrived[:, 1], slot_depth)
    rise_total = PATCH_ROWS * PATCH_COLS // tile_width // 4
    rise_live = rise_codes > 0
    rise_place = jnp.where(rise_live, jnp.cumsum(rise_live.astype(jnp.int32)), 0)
    packed_values = one_hot_rows(rise_place, rise_total, rise_values).astype(kappa.dtype)
    packed_picks = rise_place[None, :] == jnp.arange(1, rise_total + 1, dtype=jnp.int32)[:, None]
    packed_codes = jnp.sum(jnp.where(packed_picks, rise_codes[None, :], 0), axis=1)
    packed = with_codes(packed_values.reshape(1, rise_total, tile_width), packed_codes[None])
    raised_values, raised_codes = split_codes(shifted(packed, "px", -1), rise_total)
    slot_total = PATCH_ROWS * PATCH_COLS // tile_width
    patch_tiles = (
        one_hot_rows(same_codes, slot_total, same_values)
        + one_hot_rows(raised_codes, slot_total, raised_values)
    ).astype(kappa.dtype)
    fields = flexion_fields(patch_tiles.reshape(PATCH_ROWS, PATCH_COLS))
    width = tile_width
    last = PATCH_ROWS - width
    above = shifted(fields[:, last:], "px", 1)
    below = shifted(fields[:, :width], "px", -1)
    left = shifted(fields[:, :, last:], "py", 1)
    right = shifted(fields[:, :, :width], "py", -1)
    above_left = diagonal(fields[:, last:, last:], 1, 1)
    above_right = diagonal(fields[:, last:, :width], 1, -1)
    below_left = diagonal(fields[:, :width, last:], -1, 1)
    below_right = diagonal(fields[:, :width, :width], -1, -1)
    ramp = (jnp.arange(width, dtype=jnp.float32) + 0.5) / width
    top_weight = jnp.where(band_index > 0, ramp, 1.0)[None, :, None]
    bottom_weight = jnp.where(band_index < rows_axis - 1, ramp[::-1], 1.0)[None, :, None]
    left_weight = jnp.where(column_index > 0, ramp, 1.0)[None, None, :]
    right_weight = jnp.where(column_index < cols_axis - 1, ramp[::-1], 1.0)[None, None, :]
    f32 = lambda x: x.astype(jnp.float32)
    inner = row_blend(f32(fields), f32(above), f32(below), top_weight, bottom_weight, width)
    left_strip = row_blend(
        f32(left), f32(above_left), f32(below_left), top_weight, bottom_weight, width
    )
    right_strip = row_blend(
        f32(right), f32(above_right), f32(below_right), top_weight, bottom_weight, width
    )
    col_count = inner.shape[2]
    left_band = left_weight * inner[:, :, :width] + (1.0 - left_weight) * left_strip
    right_band = right_weight * inner[:, :, col_count - width :] + (1.0 - right_weight) * right_strip
    return jnp.concatenate(
        [left_band, inner[:, :, width : col_count - width], right_band], axis=2
    )


def solution(mesh):
    placed = (
        P(("px", "py"), None),
        P(("px", "py"), None, None),
        P(("px", "py"), None, None),
        P(("px", "py"), None),
    )
    return jax.shard_map(
        on_device, mesh=mesh, in_specs=placed, out_specs=P(None, "px", "py"), check_vma=False
    )
```

```python
import math

import jax
import ml_dtypes
import numpy as np
import jax.numpy as jnp
from jax import lax
from jax.sharding import PartitionSpec as P

PATCH_ROWS = 512
PATCH_COLS = 512


def shifted(shard, axis, by):
    size = lax.axis_size(axis)
    pairs = [(i, i + by) for i in range(size) if 0 <= i + by < size]
    return lax.ppermute(shard, axis, pairs)


def padded(block, sides, width):
    for axis, dim in sides:
        count = lax.axis_size(axis)
        forward = [(i, i + 1) for i in range(count - 1)]
        backward = [(target, source) for source, target in forward]
        low = lax.ppermute(
            lax.slice_in_dim(block, block.shape[dim] - width, None, axis=dim), axis, forward
        )
        high = lax.ppermute(lax.slice_in_dim(block, 0, width, axis=dim), axis, backward)
        block = jnp.concatenate([low, block, high], axis=dim)
    return block


def dft_tables(length):
    positions = np.arange(length, dtype=np.int64)
    phases = positions[:, None] * positions[None, :] % length
    angles = phases.astype(np.float32) * np.float32(2.0 * math.pi / length)
    return (np.cos(angles).astype(np.float32), np.sin(angles).astype(np.float32))


def table(values):
    return jnp.asarray(values.astype(ml_dtypes.bfloat16))


def wavenumbers(length):
    positions = jnp.arange(length, dtype=jnp.int32)
    signed = positions - length * (positions >= (length + 1) // 2).astype(jnp.int32)
    return signed.astype(jnp.float32) * (2.0 / length)


def dot32(a, b):
    return jnp.dot(a, b, preferred_element_type=jnp.float32)


def flexion_fields(pixels):
    row_count = pixels.shape[0]
    col_count = pixels.shape[1]
    assert row_count == col_count
    cos_np, sin_np = dft_tables(row_count)
    cosine, sine = table(cos_np), table(sin_np)
    n = row_count
    halves = jnp.concatenate([dot32(pixels, cosine), dot32(pixels, sine)], axis=1).astype(
        jnp.bfloat16
    )
    by_cos = dot32(cosine, halves)
    by_sin = dot32(sine, halves)
    real_part = by_cos[:, :n] - by_sin[:, n:]
    imag_part = -(by_sin[:, :n] + by_cos[:, n:])
    across = wavenumbers(col_count)[None, :]
    down = wavenumbers(row_count)[:, None]
    scale = 1.0 / (row_count * col_count)
    power = across * across + down * down
    safe_power = jnp.where(power > 0, power, 1.0)
    cube_real = across * across * across - 3.0 * across * down * down
    cube_imag = 3.0 * across * across * down - down * down * down
    one_real = (-down * real_part - across * imag_part) * scale
    one_imag = (across * real_part - down * imag_part) * scale
    kernel_real = -cube_imag / safe_power
    kernel_imag = cube_real / safe_power
    three_real = (kernel_real * real_part - kernel_imag * imag_part) * scale
    three_imag = (kernel_real * imag_part + kernel_imag * real_part) * scale
    spectra = jnp.concatenate([one_real, three_real, one_imag, three_imag], axis=1).astype(
        jnp.bfloat16
    )
    by_cos = dot32(cosine, spectra)
    by_sin = dot32(sine, spectra)
    columns_done = jnp.concatenate(
        [
            by_cos[:, : 2 * n] - by_sin[:, 2 * n :],
            by_sin[:, : 2 * n] + by_cos[:, 2 * n :],
        ],
        axis=1,
    ).astype(jnp.bfloat16)
    arranged = jnp.concatenate(
        [columns_done[:, k * n : (k + 1) * n] for k in range(4)], axis=0
    )
    by_cos = dot32(arranged, cosine)
    by_sin = dot32(arranged, sine)
    return jnp.stack(
        [
            by_cos[:n] - by_sin[2 * n : 3 * n],
            by_sin[:n] + by_cos[2 * n : 3 * n],
            by_cos[n : 2 * n] - by_sin[3 * n :],
            by_sin[n : 2 * n] + by_cos[3 * n :],
        ]
    ).astype(jnp.bfloat16)


def blend_edges(extended, has_top, has_bottom, has_left, has_right, width):
    values = extended.astype(jnp.float32)
    row_count = values.shape[1] - 2 * width
    col_count = values.shape[2] - 2 * width
    ramp = (jnp.arange(width, dtype=jnp.float32) + 0.5) / width
    top_weight = jnp.where(has_top, ramp, 1.0)[None, :, None]
    bottom_weight = jnp.where(has_bottom, ramp[::-1], 1.0)[None, :, None]
    middle = values[:, width : width + row_count, :]
    top_band = top_weight * middle[:, :width] + (1.0 - top_weight) * values[:, :width]
    bottom_band = (
        bottom_weight * middle[:, row_count - width :]
        + (1.0 - bottom_weight) * values[:, row_count + width :]
    )
    middle = jnp.concatenate([top_band, middle[:, width : row_count - width], bottom_band], axis=1)
    left_weight = jnp.where(has_left, ramp, 1.0)[None, None, :]
    right_weight = jnp.where(has_right, ramp[::-1], 1.0)[None, None, :]
    inner = middle[:, :, width : width + col_count]
    left_band = left_weight * inner[:, :, :width] + (1.0 - left_weight) * middle[:, :, :width]
    right_band = (
        right_weight * inner[:, :, col_count - width :]
        + (1.0 - right_weight) * middle[:, :, col_count + width :]
    )
    return jnp.concatenate([left_band, inner[:, :, width : col_count - width], right_band], axis=2)


def one_hot_rows(codes, count, values):
    picks = codes[None, :] == jnp.arange(1, count + 1, dtype=jnp.int32)[:, None]
    return jnp.dot(picks.astype(values.dtype), values, preferred_element_type=jnp.float32)


def gathered_rows(table_rows, picks):
    chosen = picks.reshape(-1)[:, None] == jnp.arange(table_rows.shape[0], dtype=jnp.int32)
    values = jnp.dot(chosen.astype(table_rows.dtype), table_rows, preferred_element_type=jnp.float32)
    return values.astype(table_rows.dtype).reshape(picks.shape + table_rows.shape[1:])


CODE_SPLIT = 64
CODE_ROWS = 16


def with_codes(values, codes):
    depth, width = values.shape[1], values.shape[2]
    halves = jnp.concatenate([codes // CODE_SPLIT, codes % CODE_SPLIT], axis=1)
    code_rows = halves.reshape(values.shape[0], -1, width).astype(values.dtype)
    pad = jnp.zeros((values.shape[0], CODE_ROWS - code_rows.shape[1], width), values.dtype)
    return jnp.concatenate([values, code_rows, pad], axis=1)


def split_codes(payload, depth):
    width = payload.shape[2]
    used = 2 * depth // width
    halves = payload[:, depth : depth + used].reshape(payload.shape[0], 2 * depth)
    halves = halves.astype(jnp.int32)
    codes = halves[:, :depth] * CODE_SPLIT + halves[:, depth:]
    return payload[:, :depth].reshape(-1, width), codes.reshape(-1)


def sent_block(kappa, lists, slots, counts):
    depth = lists.shape[1]
    live = jnp.arange(depth, dtype=jnp.int32)[None, :] < counts[:, None]
    codes = jnp.where(live, slots + 1, 0)
    return with_codes(gathered_rows(kappa, lists), codes)


def row_blend(own, above, below, top_weight, bottom_weight, width):
    count = own.shape[1]
    top = top_weight * own[:, :width] + (1.0 - top_weight) * above
    bottom = bottom_weight * own[:, count - width :] + (1.0 - bottom_weight) * below
    return jnp.concatenate([top, own[:, width : count - width], bottom], axis=1)


def on_device(kappa, send_list, dest_slot, send_count):
    tile_width = kappa.shape[1]
    rows_axis = lax.axis_size("px")
    cols_axis = lax.axis_size("py")
    band_index = lax.axis_index("px")
    column_index = lax.axis_index("py")
    tile_lists = send_list[0].reshape(rows_axis, cols_axis, -1)
    slot_lists = dest_slot[0].reshape(rows_axis, cols_axis, -1)
    pair_counts = send_count[0].reshape(rows_axis, cols_axis)
    slot_depth = tile_lists.shape[2]
    upper_band = jnp.maximum(band_index - 1, 0)
    upper_counts = jnp.where(band_index > 0, pair_counts[upper_band], 0)
    same_sent = sent_block(
        kappa, tile_lists[band_index], slot_lists[band_index], pair_counts[band_index]
    )
    rise_sent = sent_block(kappa, tile_lists[upper_band], slot_lists[upper_band], upper_counts)
    arrived = lax.all_to_all(jnp.stack([same_sent, rise_sent], axis=1), "py", 0, 0, tiled=True)
    same_values, same_codes = split_codes(arrived[:, 0], slot_depth)
    rise_values, rise_codes = split_codes(arrived[:, 1], slot_depth)
    rise_total = PATCH_ROWS * PATCH_COLS // tile_width // 4
    rise_live = rise_codes > 0
    rise_place = jnp.where(rise_live, jnp.cumsum(rise_live.astype(jnp.int32)), 0)
    packed_values = one_hot_rows(rise_place, rise_total, rise_values).astype(kappa.dtype)
    packed_picks = rise_place[None, :] == jnp.arange(1, rise_total + 1, dtype=jnp.int32)[:, None]
    packed_codes = jnp.sum(jnp.where(packed_picks, rise_codes[None, :], 0), axis=1)
    packed = with_codes(packed_values.reshape(1, rise_total, tile_width), packed_codes[None])
    raised_values, raised_codes = split_codes(shifted(packed, "px", -1), rise_total)
    slot_total = PATCH_ROWS * PATCH_COLS // tile_width
    patch_tiles = (
        one_hot_rows(same_codes, slot_total, same_values)
        + one_hot_rows(raised_codes, slot_total, raised_values)
    ).astype(kappa.dtype)
    fields = flexion_fields(patch_tiles.reshape(PATCH_ROWS, PATCH_COLS))
    width = tile_width
    last = PATCH_ROWS - width
    above = shifted(fields[:, last:], "px", 1)
    below = shifted(fields[:, :width], "px", -1)
    left = shifted(fields[:, :, last:], "py", 1)
    right = shifted(fields[:, :, :width], "py", -1)
    corners_left = shifted(
        jnp.concatenate([above[:, :, last:], below[:, :, last:]], axis=1), "py", 1
    )
    corners_right = shifted(
        jnp.concatenate([above[:, :, :width], below[:, :, :width]], axis=1), "py", -1
    )
    above_left, below_left = corners_left[:, :width], corners_left[:, width:]
    above_right, below_right = corners_right[:, :width], corners_right[:, width:]
    ramp = (jnp.arange(width, dtype=jnp.float32) + 0.5) / width
    top_weight = jnp.where(band_index > 0, ramp, 1.0)[None, :, None]
    bottom_weight = jnp.where(band_index < rows_axis - 1, ramp[::-1], 1.0)[None, :, None]
    left_weight = jnp.where(column_index > 0, ramp, 1.0)[None, None, :]
    right_weight = jnp.where(column_index < cols_axis - 1, ramp[::-1], 1.0)[None, None, :]
    f32 = lambda x: x.astype(jnp.float32)
    inner = row_blend(f32(fields), f32(above), f32(below), top_weight, bottom_weight, width)
    left_strip = row_blend(
        f32(left), f32(above_left), f32(below_left), top_weight, bottom_weight, width
    )
    right_strip = row_blend(
        f32(right), f32(above_right), f32(below_right), top_weight, bottom_weight, width
    )
    col_count = inner.shape[2]
    left_band = left_weight * inner[:, :, :width] + (1.0 - left_weight) * left_strip
    right_band = right_weight * inner[:, :, col_count - width :] + (1.0 - right_weight) * right_strip
    return jnp.concatenate(
        [left_band, inner[:, :, width : col_count - width], right_band], axis=2
    )


def solution(mesh):
    placed = (
        P(("px", "py"), None),
        P(("px", "py"), None, None),
        P(("px", "py"), None, None),
        P(("px", "py"), None),
    )
    return jax.shard_map(
        on_device, mesh=mesh, in_specs=placed, out_specs=P(None, "px", "py"), check_vma=False
    )
```

```python
import math

import jax
import ml_dtypes
import numpy as np
import jax.numpy as jnp
from jax import lax
from jax.sharding import PartitionSpec as P

PATCH_ROWS = 512
PATCH_COLS = 512


def shifted(shard, axis, by):
    size = lax.axis_size(axis)
    pairs = [(i, i + by) for i in range(size) if 0 <= i + by < size]
    return lax.ppermute(shard, axis, pairs)


def padded(block, sides, width):
    for axis, dim in sides:
        count = lax.axis_size(axis)
        forward = [(i, i + 1) for i in range(count - 1)]
        backward = [(target, source) for source, target in forward]
        low = lax.ppermute(
            lax.slice_in_dim(block, block.shape[dim] - width, None, axis=dim), axis, forward
        )
        high = lax.ppermute(lax.slice_in_dim(block, 0, width, axis=dim), axis, backward)
        block = jnp.concatenate([low, block, high], axis=dim)
    return block


def dft_tables(length):
    positions = np.arange(length, dtype=np.int64)
    phases = positions[:, None] * positions[None, :] % length
    angles = phases.astype(np.float32) * np.float32(2.0 * math.pi / length)
    return (np.cos(angles).astype(np.float32), np.sin(angles).astype(np.float32))


def table(values):
    return jnp.asarray(values.astype(ml_dtypes.bfloat16))


def wavenumbers(length):
    positions = jnp.arange(length, dtype=jnp.int32)
    signed = positions - length * (positions >= (length + 1) // 2).astype(jnp.int32)
    return signed.astype(jnp.float32) * (2.0 / length)


def dot32(a, b):
    return jnp.dot(a, b, preferred_element_type=jnp.float32)


def flexion_fields(pixels):
    row_count = pixels.shape[0]
    col_count = pixels.shape[1]
    assert row_count == col_count
    cos_np, sin_np = dft_tables(row_count)
    cosine, sine = table(cos_np), table(sin_np)
    n = row_count
    halves = jnp.concatenate([dot32(pixels, cosine), dot32(pixels, sine)], axis=1).astype(
        jnp.bfloat16
    )
    by_cos = dot32(cosine, halves)
    by_sin = dot32(sine, halves)
    real_part = by_cos[:, :n] - by_sin[:, n:]
    imag_part = -(by_sin[:, :n] + by_cos[:, n:])
    across = wavenumbers(col_count)[None, :]
    down = wavenumbers(row_count)[:, None]
    scale = 1.0 / (row_count * col_count)
    power = across * across + down * down
    safe_power = jnp.where(power > 0, power, 1.0)
    cube_real = across * across * across - 3.0 * across * down * down
    cube_imag = 3.0 * across * across * down - down * down * down
    one_real = (-down * real_part - across * imag_part) * scale
    one_imag = (across * real_part - down * imag_part) * scale
    kernel_real = -cube_imag / safe_power
    kernel_imag = cube_real / safe_power
    three_real = (kernel_real * real_part - kernel_imag * imag_part) * scale
    three_imag = (kernel_real * imag_part + kernel_imag * real_part) * scale
    spectra = jnp.concatenate([one_real, three_real, one_imag, three_imag], axis=1).astype(
        jnp.bfloat16
    )
    by_cos = dot32(cosine, spectra)
    by_sin = dot32(sine, spectra)
    columns_done = jnp.concatenate(
        [
            by_cos[:, : 2 * n] - by_sin[:, 2 * n :],
            by_sin[:, : 2 * n] + by_cos[:, 2 * n :],
        ],
        axis=1,
    ).astype(jnp.bfloat16)
    arranged = jnp.concatenate(
        [columns_done[:, k * n : (k + 1) * n] for k in range(4)], axis=0
    )
    by_cos = dot32(arranged, cosine)
    by_sin = dot32(arranged, sine)
    return jnp.stack(
        [
            by_cos[:n] - by_sin[2 * n : 3 * n],
            by_sin[:n] + by_cos[2 * n : 3 * n],
            by_cos[n : 2 * n] - by_sin[3 * n :],
            by_sin[n : 2 * n] + by_cos[3 * n :],
        ]
    ).astype(jnp.bfloat16)


def blend_edges(extended, has_top, has_bottom, has_left, has_right, width):
    values = extended.astype(jnp.float32)
    row_count = values.shape[1] - 2 * width
    col_count = values.shape[2] - 2 * width
    ramp = (jnp.arange(width, dtype=jnp.float32) + 0.5) / width
    top_weight = jnp.where(has_top, ramp, 1.0)[None, :, None]
    bottom_weight = jnp.where(has_bottom, ramp[::-1], 1.0)[None, :, None]
    middle = values[:, width : width + row_count, :]
    top_band = top_weight * middle[:, :width] + (1.0 - top_weight) * values[:, :width]
    bottom_band = (
        bottom_weight * middle[:, row_count - width :]
        + (1.0 - bottom_weight) * values[:, row_count + width :]
    )
    middle = jnp.concatenate([top_band, middle[:, width : row_count - width], bottom_band], axis=1)
    left_weight = jnp.where(has_left, ramp, 1.0)[None, None, :]
    right_weight = jnp.where(has_right, ramp[::-1], 1.0)[None, None, :]
    inner = middle[:, :, width : width + col_count]
    left_band = left_weight * inner[:, :, :width] + (1.0 - left_weight) * middle[:, :, :width]
    right_band = (
        right_weight * inner[:, :, col_count - width :]
        + (1.0 - right_weight) * middle[:, :, col_count + width :]
    )
    return jnp.concatenate([left_band, inner[:, :, width : col_count - width], right_band], axis=2)


def one_hot_rows(codes, count, values):
    picks = codes[None, :] == jnp.arange(1, count + 1, dtype=jnp.int32)[:, None]
    return jnp.dot(picks.astype(values.dtype), values, preferred_element_type=jnp.float32)


def gathered_rows(table_rows, picks):
    chosen = picks.reshape(-1)[:, None] == jnp.arange(table_rows.shape[0], dtype=jnp.int32)
    values = jnp.dot(chosen.astype(table_rows.dtype), table_rows, preferred_element_type=jnp.float32)
    return values.astype(table_rows.dtype).reshape(picks.shape + table_rows.shape[1:])


CODE_SPLIT = 64
CODE_ROWS = 16


def with_codes(values, codes):
    depth, width = values.shape[1], values.shape[2]
    halves = jnp.concatenate([codes // CODE_SPLIT, codes % CODE_SPLIT], axis=1)
    code_rows = halves.reshape(values.shape[0], -1, width).astype(values.dtype)
    pad = jnp.zeros((values.shape[0], CODE_ROWS - code_rows.shape[1], width), values.dtype)
    return jnp.concatenate([values, code_rows, pad], axis=1)


def split_codes(payload, depth):
    width = payload.shape[2]
    used = 2 * depth // width
    halves = payload[:, depth : depth + used].reshape(payload.shape[0], 2 * depth)
    halves = halves.astype(jnp.int32)
    codes = halves[:, :depth] * CODE_SPLIT + halves[:, depth:]
    return payload[:, :depth].reshape(-1, width), codes.reshape(-1)


def sent_block(kappa, lists, slots, counts):
    depth = lists.shape[1]
    live = jnp.arange(depth, dtype=jnp.int32)[None, :] < counts[:, None]
    codes = jnp.where(live, slots + 1, 0)
    return with_codes(gathered_rows(kappa, lists), codes)


def row_blend(own, above, below, top_weight, bottom_weight, width):
    count = own.shape[1]
    top = top_weight * own[:, :width] + (1.0 - top_weight) * above
    bottom = bottom_weight * own[:, count - width :] + (1.0 - bottom_weight) * below
    return jnp.concatenate([top, own[:, width : count - width], bottom], axis=1)


def on_device(kappa, send_list, dest_slot, send_count):
    tile_width = kappa.shape[1]
    rows_axis = lax.axis_size("px")
    cols_axis = lax.axis_size("py")
    band_index = lax.axis_index("px")
    column_index = lax.axis_index("py")
    tile_lists = send_list[0].reshape(rows_axis, cols_axis, -1)
    slot_lists = dest_slot[0].reshape(rows_axis, cols_axis, -1)
    pair_counts = send_count[0].reshape(rows_axis, cols_axis)
    slot_depth = tile_lists.shape[2]
    upper_band = jnp.maximum(band_index - 1, 0)
    upper_counts = jnp.where(band_index > 0, pair_counts[upper_band], 0)
    same_sent = sent_block(
        kappa, tile_lists[band_index], slot_lists[band_index], pair_counts[band_index]
    )
    rise_sent = sent_block(kappa, tile_lists[upper_band], slot_lists[upper_band], upper_counts)
    arrived = lax.all_to_all(jnp.stack([same_sent, rise_sent], axis=1), "py", 0, 0, tiled=True)
    same_values, same_codes = split_codes(arrived[:, 0], slot_depth)
    rise_values, rise_codes = split_codes(arrived[:, 1], slot_depth)
    rise_total = PATCH_ROWS * PATCH_COLS // tile_width // 4
    rise_live = rise_codes > 0
    rise_place = jnp.where(rise_live, jnp.cumsum(rise_live.astype(jnp.int32)), 0)
    packed_values = one_hot_rows(rise_place, rise_total, rise_values).astype(kappa.dtype)
    packed_picks = rise_place[None, :] == jnp.arange(1, rise_total + 1, dtype=jnp.int32)[:, None]
    packed_codes = jnp.sum(jnp.where(packed_picks, rise_codes[None, :], 0), axis=1)
    packed = with_codes(packed_values.reshape(1, rise_total, tile_width), packed_codes[None])
    raised_values, raised_codes = split_codes(shifted(packed, "px", -1), rise_total)
    slot_total = PATCH_ROWS * PATCH_COLS // tile_width
    patch_tiles = (
        one_hot_rows(same_codes, slot_total, same_values)
        + one_hot_rows(raised_codes, slot_total, raised_values)
    ).astype(kappa.dtype)
    fields = flexion_fields(patch_tiles.reshape(PATCH_ROWS, PATCH_COLS))
    width = tile_width
    last = PATCH_ROWS - width
    left = shifted(fields[:, :, last:], "py", 1)
    right = shifted(fields[:, :, :width], "py", -1)
    above = shifted(fields[:, last:], "px", 1)
    below = shifted(fields[:, :width], "px", -1)
    corners_above = shifted(
        jnp.concatenate([left[:, last:], right[:, last:]], axis=2), "px", 1
    )
    corners_below = shifted(
        jnp.concatenate([left[:, :width], right[:, :width]], axis=2), "px", -1
    )
    above_left, above_right = corners_above[:, :, :width], corners_above[:, :, width:]
    below_left, below_right = corners_below[:, :, :width], corners_below[:, :, width:]
    ramp = (jnp.arange(width, dtype=jnp.float32) + 0.5) / width
    top_weight = jnp.where(band_index > 0, ramp, 1.0)[None, :, None]
    bottom_weight = jnp.where(band_index < rows_axis - 1, ramp[::-1], 1.0)[None, :, None]
    left_weight = jnp.where(column_index > 0, ramp, 1.0)[None, None, :]
    right_weight = jnp.where(column_index < cols_axis - 1, ramp[::-1], 1.0)[None, None, :]
    f32 = lambda x: x.astype(jnp.float32)
    inner = row_blend(f32(fields), f32(above), f32(below), top_weight, bottom_weight, width)
    left_strip = row_blend(
        f32(left), f32(above_left), f32(below_left), top_weight, bottom_weight, width
    )
    right_strip = row_blend(
        f32(right), f32(above_right), f32(below_right), top_weight, bottom_weight, width
    )
    col_count = inner.shape[2]
    left_band = left_weight * inner[:, :, :width] + (1.0 - left_weight) * left_strip
    right_band = right_weight * inner[:, :, col_count - width :] + (1.0 - right_weight) * right_strip
    return jnp.concatenate(
        [left_band, inner[:, :, width : col_count - width], right_band], axis=2
    )


def solution(mesh):
    placed = (
        P(("px", "py"), None),
        P(("px", "py"), None, None),
        P(("px", "py"), None, None),
        P(("px", "py"), None),
    )
    return jax.shard_map(
        on_device, mesh=mesh, in_specs=placed, out_specs=P(None, "px", "py"), check_vma=False
    )
```

```python
import math

import jax
import ml_dtypes
import numpy as np
import jax.numpy as jnp
from jax import lax
from jax.experimental import pallas as pl
from jax.sharding import PartitionSpec as P

PATCH_ROWS = 512
PATCH_COLS = 512


def shifted(shard, axis, by):
    size = lax.axis_size(axis)
    pairs = [(i, i + by) for i in range(size) if 0 <= i + by < size]
    return lax.ppermute(shard, axis, pairs)


def padded(block, sides, width):
    for axis, dim in sides:
        count = lax.axis_size(axis)
        forward = [(i, i + 1) for i in range(count - 1)]
        backward = [(target, source) for source, target in forward]
        low = lax.ppermute(
            lax.slice_in_dim(block, block.shape[dim] - width, None, axis=dim), axis, forward
        )
        high = lax.ppermute(lax.slice_in_dim(block, 0, width, axis=dim), axis, backward)
        block = jnp.concatenate([low, block, high], axis=dim)
    return block


def dft_tables(length):
    positions = np.arange(length, dtype=np.int64)
    phases = positions[:, None] * positions[None, :] % length
    angles = phases.astype(np.float32) * np.float32(2.0 * math.pi / length)
    return (np.cos(angles).astype(np.float32), np.sin(angles).astype(np.float32))


def table(values):
    return jnp.asarray(values.astype(ml_dtypes.bfloat16))


def wavenumbers(length):
    positions = jnp.arange(length, dtype=jnp.int32)
    signed = positions - length * (positions >= (length + 1) // 2).astype(jnp.int32)
    return signed.astype(jnp.float32) * (2.0 / length)


def dot32(a, b):
    return jnp.dot(a, b, preferred_element_type=jnp.float32)


def flexion_fields(pixels):
    row_count = pixels.shape[0]
    col_count = pixels.shape[1]
    assert row_count == col_count
    cos_np, sin_np = dft_tables(row_count)
    cosine, sine = table(cos_np), table(sin_np)
    n = row_count
    halves = jnp.concatenate([dot32(pixels, cosine), dot32(pixels, sine)], axis=1).astype(
        jnp.bfloat16
    )
    by_cos = dot32(cosine, halves)
    by_sin = dot32(sine, halves)
    real_part = by_cos[:, :n] - by_sin[:, n:]
    imag_part = -(by_sin[:, :n] + by_cos[:, n:])
    across = wavenumbers(col_count)[None, :]
    down = wavenumbers(row_count)[:, None]
    scale = 1.0 / (row_count * col_count)
    power = across * across + down * down
    safe_power = jnp.where(power > 0, power, 1.0)
    cube_real = across * across * across - 3.0 * across * down * down
    cube_imag = 3.0 * across * across * down - down * down * down
    one_real = (-down * real_part - across * imag_part) * scale
    one_imag = (across * real_part - down * imag_part) * scale
    kernel_real = -cube_imag / safe_power
    kernel_imag = cube_real / safe_power
    three_real = (kernel_real * real_part - kernel_imag * imag_part) * scale
    three_imag = (kernel_real * imag_part + kernel_imag * real_part) * scale
    spectra = jnp.concatenate([one_real, three_real, one_imag, three_imag], axis=1).astype(
        jnp.bfloat16
    )
    by_cos = dot32(cosine, spectra)
    by_sin = dot32(sine, spectra)
    columns_done = jnp.concatenate(
        [
            by_cos[:, : 2 * n] - by_sin[:, 2 * n :],
            by_sin[:, : 2 * n] + by_cos[:, 2 * n :],
        ],
        axis=1,
    ).astype(jnp.bfloat16)
    arranged = jnp.concatenate(
        [columns_done[:, k * n : (k + 1) * n] for k in range(4)], axis=0
    )
    by_cos = dot32(arranged, cosine)
    by_sin = dot32(arranged, sine)
    return jnp.stack(
        [
            by_cos[:n] - by_sin[2 * n : 3 * n],
            by_sin[:n] + by_cos[2 * n : 3 * n],
            by_cos[n : 2 * n] - by_sin[3 * n :],
            by_sin[n : 2 * n] + by_cos[3 * n :],
        ]
    ).astype(jnp.bfloat16)


def blend_edges(extended, has_top, has_bottom, has_left, has_right, width):
    values = extended.astype(jnp.float32)
    row_count = values.shape[1] - 2 * width
    col_count = values.shape[2] - 2 * width
    ramp = (jnp.arange(width, dtype=jnp.float32) + 0.5) / width
    top_weight = jnp.where(has_top, ramp, 1.0)[None, :, None]
    bottom_weight = jnp.where(has_bottom, ramp[::-1], 1.0)[None, :, None]
    middle = values[:, width : width + row_count, :]
    top_band = top_weight * middle[:, :width] + (1.0 - top_weight) * values[:, :width]
    bottom_band = (
        bottom_weight * middle[:, row_count - width :]
        + (1.0 - bottom_weight) * values[:, row_count + width :]
    )
    middle = jnp.concatenate([top_band, middle[:, width : row_count - width], bottom_band], axis=1)
    left_weight = jnp.where(has_left, ramp, 1.0)[None, None, :]
    right_weight = jnp.where(has_right, ramp[::-1], 1.0)[None, None, :]
    inner = middle[:, :, width : width + col_count]
    left_band = left_weight * inner[:, :, :width] + (1.0 - left_weight) * middle[:, :, :width]
    right_band = (
        right_weight * inner[:, :, col_count - width :]
        + (1.0 - right_weight) * middle[:, :, col_count + width :]
    )
    return jnp.concatenate([left_band, inner[:, :, width : col_count - width], right_band], axis=2)


def one_hot_rows(codes, count, values):
    picks = codes[None, :] == jnp.arange(1, count + 1, dtype=jnp.int32)[:, None]
    return jnp.dot(picks.astype(values.dtype), values, preferred_element_type=jnp.float32)


def gathered_rows(table_rows, picks):
    chosen = picks.reshape(-1)[:, None] == jnp.arange(table_rows.shape[0], dtype=jnp.int32)
    values = jnp.dot(chosen.astype(table_rows.dtype), table_rows, preferred_element_type=jnp.float32)
    return values.astype(table_rows.dtype).reshape(picks.shape + table_rows.shape[1:])


CODE_SPLIT = 64
CODE_ROWS = 16


def with_codes(values, codes):
    depth, width = values.shape[1], values.shape[2]
    halves = jnp.concatenate([codes // CODE_SPLIT, codes % CODE_SPLIT], axis=1)
    code_rows = halves.reshape(values.shape[0], -1, width).astype(values.dtype)
    pad = jnp.zeros((values.shape[0], CODE_ROWS - code_rows.shape[1], width), values.dtype)
    return jnp.concatenate([values, code_rows, pad], axis=1)


def split_codes(payload, depth):
    width = payload.shape[2]
    used = 2 * depth // width
    halves = payload[:, depth : depth + used].reshape(payload.shape[0], 2 * depth)
    halves = halves.astype(jnp.int32)
    codes = halves[:, :depth] * CODE_SPLIT + halves[:, depth:]
    return payload[:, :depth].reshape(-1, width), codes.reshape(-1)


def sent_block(kappa, lists, slots, counts):
    depth = lists.shape[1]
    live = jnp.arange(depth, dtype=jnp.int32)[None, :] < counts[:, None]
    codes = jnp.where(live, slots + 1, 0)
    return with_codes(gathered_rows(kappa, lists), codes)


def row_blend(own, above, below, top_weight, bottom_weight, width):
    count = own.shape[1]
    top = top_weight * own[:, :width] + (1.0 - top_weight) * above
    bottom = bottom_weight * own[:, count - width :] + (1.0 - bottom_weight) * below
    return jnp.concatenate([top, own[:, width : count - width], bottom], axis=1)


def on_device(kappa, send_list, dest_slot, send_count):
    tile_width = kappa.shape[1]
    rows_axis = lax.axis_size("px")
    cols_axis = lax.axis_size("py")
    band_index = lax.axis_index("px")
    column_index = lax.axis_index("py")
    tile_lists = send_list[0].reshape(rows_axis, cols_axis, -1)
    slot_lists = dest_slot[0].reshape(rows_axis, cols_axis, -1)
    pair_counts = send_count[0].reshape(rows_axis, cols_axis)
    slot_depth = tile_lists.shape[2]
    upper_band = jnp.maximum(band_index - 1, 0)
    upper_counts = jnp.where(band_index > 0, pair_counts[upper_band], 0)
    same_sent = sent_block(
        kappa, tile_lists[band_index], slot_lists[band_index], pair_counts[band_index]
    )
    rise_sent = sent_block(kappa, tile_lists[upper_band], slot_lists[upper_band], upper_counts)
    arrived = lax.all_to_all(jnp.stack([same_sent, rise_sent], axis=1), "py", 0, 0, tiled=True)
    same_values, same_codes = split_codes(arrived[:, 0], slot_depth)
    rise_values, rise_codes = split_codes(arrived[:, 1], slot_depth)
    rise_total = PATCH_ROWS * PATCH_COLS // tile_width // 4
    rise_live = rise_codes > 0
    rise_place = jnp.where(rise_live, jnp.cumsum(rise_live.astype(jnp.int32)), 0)
    packed_values = one_hot_rows(rise_place, rise_total, rise_values).astype(kappa.dtype)
    packed_picks = rise_place[None, :] == jnp.arange(1, rise_total + 1, dtype=jnp.int32)[:, None]
    packed_codes = jnp.sum(jnp.where(packed_picks, rise_codes[None, :], 0), axis=1)
    packed = with_codes(packed_values.reshape(1, rise_total, tile_width), packed_codes[None])
    raised_values, raised_codes = split_codes(shifted(packed, "px", -1), rise_total)
    slot_total = PATCH_ROWS * PATCH_COLS // tile_width
    patch_tiles = (
        one_hot_rows(same_codes, slot_total, same_values)
        + one_hot_rows(raised_codes, slot_total, raised_values)
    ).astype(kappa.dtype)
    fields = flexion_fields(patch_tiles.reshape(PATCH_ROWS, PATCH_COLS))
    width = tile_width
    last = PATCH_ROWS - width
    left = shifted(fields[:, :, last:], "py", 1)
    right = shifted(fields[:, :, :width], "py", -1)
    above = shifted(fields[:, last:], "px", 1)
    below = shifted(fields[:, :width], "px", -1)
    corners_above = shifted(
        jnp.concatenate([left[:, last:], right[:, last:]], axis=2), "px", 1
    )
    corners_below = shifted(
        jnp.concatenate([left[:, :width], right[:, :width]], axis=2), "px", -1
    )
    above_left, above_right = corners_above[:, :, :width], corners_above[:, :, width:]
    below_left, below_right = corners_below[:, :, :width], corners_below[:, :, width:]
    ramp = (jnp.arange(width, dtype=jnp.float32) + 0.5) / width
    top_weight = jnp.where(band_index > 0, ramp, 1.0)[None, :, None]
    bottom_weight = jnp.where(band_index < rows_axis - 1, ramp[::-1], 1.0)[None, :, None]
    left_weight = jnp.where(column_index > 0, ramp, 1.0)[None, None, :]
    right_weight = jnp.where(column_index < cols_axis - 1, ramp[::-1], 1.0)[None, None, :]
    weights = (
        top_weight[0, :, :],
        bottom_weight[0, :, :],
        left_weight[0, :, :],
        right_weight[0, :, :],
    )
    return blended(fields, above, below, left, right, corners_above, corners_below, weights)


def blend_kernel(own_ref, above_ref, below_ref, left_ref, right_ref, ca_ref, cb_ref,
                 tw_ref, bw_ref, lw_ref, rw_ref, out_ref):
    width = above_ref.shape[1]
    count = own_ref.shape[1]
    last = count - width
    tw, bw, lw, rw = tw_ref[...], bw_ref[...], lw_ref[...], rw_ref[...]
    own = own_ref[0].astype(jnp.float32)
    above = above_ref[0].astype(jnp.float32)
    below = below_ref[0].astype(jnp.float32)
    out_ref[0, :width] = tw * own[:width] + (1.0 - tw) * above
    out_ref[0, width:last] = own[width:last]
    out_ref[0, last:] = bw * own[last:] + (1.0 - bw) * below
    for strip_ref, corner, col, weight in (
        (left_ref, slice(0, width), slice(0, width), lw),
        (right_ref, slice(width, 2 * width), slice(last, count), rw),
    ):
        strip = strip_ref[0].astype(jnp.float32)
        upper = ca_ref[0, :, corner].astype(jnp.float32)
        lower = cb_ref[0, :, corner].astype(jnp.float32)
        strip_rows = jnp.concatenate(
            [
                tw * strip[:width] + (1.0 - tw) * upper,
                strip[width:last],
                bw * strip[last:] + (1.0 - bw) * lower,
            ],
            axis=0,
        )
        out_ref[0, :, col] = weight * out_ref[0, :, col] + (1.0 - weight) * strip_rows


def blended(fields, above, below, left, right, corners_above, corners_below, weights):
    planes, count = fields.shape[0], fields.shape[1]
    width = above.shape[1]
    per_plane = lambda shape: pl.BlockSpec((1,) + shape, lambda f: (f, 0, 0))
    whole = lambda shape: pl.BlockSpec(shape, lambda f: (0, 0))
    return pl.pallas_call(
        blend_kernel,
        grid=(planes,),
        in_specs=[
            per_plane((count, count)),
            per_plane((width, count)),
            per_plane((width, count)),
            per_plane((count, width)),
            per_plane((count, width)),
            per_plane((width, 2 * width)),
            per_plane((width, 2 * width)),
            whole((width, 1)),
            whole((width, 1)),
            whole((1, width)),
            whole((1, width)),
        ],
        out_specs=per_plane((count, count)),
        out_shape=jax.ShapeDtypeStruct(fields.shape, jnp.float32),
        cost_estimate=pl.CostEstimate(
            flops=12 * planes * count * width, bytes_accessed=planes * count * count * 6,
            transcendentals=0,
        ),
    )(fields, above, below, left, right, corners_above, corners_below, *weights)


def solution(mesh):
    placed = (
        P(("px", "py"), None),
        P(("px", "py"), None, None),
        P(("px", "py"), None, None),
        P(("px", "py"), None),
    )
    return jax.shard_map(
        on_device, mesh=mesh, in_specs=placed, out_specs=P(None, "px", "py"), check_vma=False
    )
```

```python
import math

import jax
import ml_dtypes
import numpy as np
import jax.numpy as jnp
from jax import lax
from jax.experimental import pallas as pl
from jax.sharding import PartitionSpec as P

PATCH_ROWS = 512
PATCH_COLS = 512


def shifted(shard, axis, by):
    size = lax.axis_size(axis)
    pairs = [(i, i + by) for i in range(size) if 0 <= i + by < size]
    return lax.ppermute(shard, axis, pairs)


def padded(block, sides, width):
    for axis, dim in sides:
        count = lax.axis_size(axis)
        forward = [(i, i + 1) for i in range(count - 1)]
        backward = [(target, source) for source, target in forward]
        low = lax.ppermute(
            lax.slice_in_dim(block, block.shape[dim] - width, None, axis=dim), axis, forward
        )
        high = lax.ppermute(lax.slice_in_dim(block, 0, width, axis=dim), axis, backward)
        block = jnp.concatenate([low, block, high], axis=dim)
    return block


def dft_tables(length):
    positions = np.arange(length, dtype=np.int64)
    phases = positions[:, None] * positions[None, :] % length
    angles = phases.astype(np.float32) * np.float32(2.0 * math.pi / length)
    return (np.cos(angles).astype(np.float32), np.sin(angles).astype(np.float32))


def table(values):
    return jnp.asarray(values.astype(ml_dtypes.bfloat16))


def wavenumbers(length):
    positions = jnp.arange(length, dtype=jnp.int32)
    signed = positions - length * (positions >= (length + 1) // 2).astype(jnp.int32)
    return signed.astype(jnp.float32) * (2.0 / length)


def dot32(a, b):
    return jnp.dot(a, b, preferred_element_type=jnp.float32)


def flexion_fields(pixels):
    row_count = pixels.shape[0]
    col_count = pixels.shape[1]
    assert row_count == col_count
    cos_np, sin_np = dft_tables(row_count)
    cosine, sine = table(cos_np), table(sin_np)
    n = row_count
    halves = jnp.concatenate([dot32(pixels, cosine), dot32(pixels, sine)], axis=1).astype(
        jnp.bfloat16
    )
    by_cos = dot32(cosine, halves)
    by_sin = dot32(sine, halves)
    real_part = by_cos[:, :n] - by_sin[:, n:]
    imag_part = -(by_sin[:, :n] + by_cos[:, n:])
    across = wavenumbers(col_count)[None, :]
    down = wavenumbers(row_count)[:, None]
    scale = 1.0 / (row_count * col_count)
    power = across * across + down * down
    safe_power = jnp.where(power > 0, power, 1.0)
    cube_real = across * across * across - 3.0 * across * down * down
    cube_imag = 3.0 * across * across * down - down * down * down
    one_real = (-down * real_part - across * imag_part) * scale
    one_imag = (across * real_part - down * imag_part) * scale
    kernel_real = -cube_imag / safe_power
    kernel_imag = cube_real / safe_power
    three_real = (kernel_real * real_part - kernel_imag * imag_part) * scale
    three_imag = (kernel_real * imag_part + kernel_imag * real_part) * scale
    spectra = jnp.concatenate([one_real, three_real, one_imag, three_imag], axis=1).astype(
        jnp.bfloat16
    )
    by_cos = dot32(cosine, spectra)
    by_sin = dot32(sine, spectra)
    columns_done = jnp.concatenate(
        [
            by_cos[:, : 2 * n] - by_sin[:, 2 * n :],
            by_sin[:, : 2 * n] + by_cos[:, 2 * n :],
        ],
        axis=1,
    ).astype(jnp.bfloat16)
    arranged = jnp.concatenate(
        [columns_done[:, k * n : (k + 1) * n] for k in range(4)], axis=0
    )
    by_cos = dot32(arranged, cosine)
    by_sin = dot32(arranged, sine)
    return jnp.stack(
        [
            by_cos[:n] - by_sin[2 * n : 3 * n],
            by_sin[:n] + by_cos[2 * n : 3 * n],
            by_cos[n : 2 * n] - by_sin[3 * n :],
            by_sin[n : 2 * n] + by_cos[3 * n :],
        ]
    ).astype(jnp.bfloat16)


def blend_edges(extended, has_top, has_bottom, has_left, has_right, width):
    values = extended.astype(jnp.float32)
    row_count = values.shape[1] - 2 * width
    col_count = values.shape[2] - 2 * width
    ramp = (jnp.arange(width, dtype=jnp.float32) + 0.5) / width
    top_weight = jnp.where(has_top, ramp, 1.0)[None, :, None]
    bottom_weight = jnp.where(has_bottom, ramp[::-1], 1.0)[None, :, None]
    middle = values[:, width : width + row_count, :]
    top_band = top_weight * middle[:, :width] + (1.0 - top_weight) * values[:, :width]
    bottom_band = (
        bottom_weight * middle[:, row_count - width :]
        + (1.0 - bottom_weight) * values[:, row_count + width :]
    )
    middle = jnp.concatenate([top_band, middle[:, width : row_count - width], bottom_band], axis=1)
    left_weight = jnp.where(has_left, ramp, 1.0)[None, None, :]
    right_weight = jnp.where(has_right, ramp[::-1], 1.0)[None, None, :]
    inner = middle[:, :, width : width + col_count]
    left_band = left_weight * inner[:, :, :width] + (1.0 - left_weight) * middle[:, :, :width]
    right_band = (
        right_weight * inner[:, :, col_count - width :]
        + (1.0 - right_weight) * middle[:, :, col_count + width :]
    )
    return jnp.concatenate([left_band, inner[:, :, width : col_count - width], right_band], axis=2)


def one_hot_rows(codes, count, values):
    picks = codes[None, :] == jnp.arange(1, count + 1, dtype=jnp.int32)[:, None]
    return jnp.dot(picks.astype(values.dtype), values, preferred_element_type=jnp.float32)


def gathered_rows(table_rows, picks):
    chosen = picks.reshape(-1)[:, None] == jnp.arange(table_rows.shape[0], dtype=jnp.int32)
    values = jnp.dot(chosen.astype(table_rows.dtype), table_rows, preferred_element_type=jnp.float32)
    return values.astype(table_rows.dtype).reshape(picks.shape + table_rows.shape[1:])


CODE_SPLIT = 64
CODE_ROWS = 16


def with_codes(values, codes):
    depth, width = values.shape[1], values.shape[2]
    halves = jnp.concatenate([codes // CODE_SPLIT, codes % CODE_SPLIT], axis=1)
    code_rows = halves.reshape(values.shape[0], -1, width).astype(values.dtype)
    pad = jnp.zeros((values.shape[0], CODE_ROWS - code_rows.shape[1], width), values.dtype)
    return jnp.concatenate([values, code_rows, pad], axis=1)


def split_codes(payload, depth):
    width = payload.shape[2]
    used = 2 * depth // width
    halves = payload[:, depth : depth + used].reshape(payload.shape[0], 2 * depth)
    halves = halves.astype(jnp.int32)
    codes = halves[:, :depth] * CODE_SPLIT + halves[:, depth:]
    return payload[:, :depth].reshape(-1, width), codes.reshape(-1)


def sent_block(kappa, lists, slots, counts):
    depth = lists.shape[1]
    live = jnp.arange(depth, dtype=jnp.int32)[None, :] < counts[:, None]
    codes = jnp.where(live, slots + 1, 0)
    return with_codes(gathered_rows(kappa, lists), codes)


def row_blend(own, above, below, top_weight, bottom_weight, width):
    count = own.shape[1]
    top = top_weight * own[:, :width] + (1.0 - top_weight) * above
    bottom = bottom_weight * own[:, count - width :] + (1.0 - bottom_weight) * below
    return jnp.concatenate([top, own[:, width : count - width], bottom], axis=1)


def on_device(kappa, send_list, dest_slot, send_count):
    tile_width = kappa.shape[1]
    rows_axis = lax.axis_size("px")
    cols_axis = lax.axis_size("py")
    band_index = lax.axis_index("px")
    column_index = lax.axis_index("py")
    tile_lists = send_list[0].reshape(rows_axis, cols_axis, -1)
    slot_lists = dest_slot[0].reshape(rows_axis, cols_axis, -1)
    pair_counts = send_count[0].reshape(rows_axis, cols_axis)
    slot_depth = tile_lists.shape[2]
    upper_band = jnp.maximum(band_index - 1, 0)
    upper_counts = jnp.where(band_index > 0, pair_counts[upper_band], 0)
    same_sent = sent_block(
        kappa, tile_lists[band_index], slot_lists[band_index], pair_counts[band_index]
    )
    rise_sent = sent_block(kappa, tile_lists[upper_band], slot_lists[upper_band], upper_counts)
    arrived = lax.all_to_all(jnp.stack([same_sent, rise_sent], axis=1), "py", 0, 0, tiled=True)
    same_values, same_codes = split_codes(arrived[:, 0], slot_depth)
    rise_values, rise_codes = split_codes(arrived[:, 1], slot_depth)
    rise_total = PATCH_ROWS * PATCH_COLS // tile_width // 4
    rise_live = rise_codes > 0
    rise_place = jnp.where(rise_live, jnp.cumsum(rise_live.astype(jnp.int32)), 0)
    packed_values = one_hot_rows(rise_place, rise_total, rise_values).astype(kappa.dtype)
    packed_picks = rise_place[None, :] == jnp.arange(1, rise_total + 1, dtype=jnp.int32)[:, None]
    packed_codes = jnp.sum(jnp.where(packed_picks, rise_codes[None, :], 0), axis=1)
    packed = with_codes(packed_values.reshape(1, rise_total, tile_width), packed_codes[None])
    raised_values, raised_codes = split_codes(shifted(packed, "px", -1), rise_total)
    slot_total = PATCH_ROWS * PATCH_COLS // tile_width
    patch_tiles = (
        one_hot_rows(same_codes, slot_total, same_values)
        + one_hot_rows(raised_codes, slot_total, raised_values)
    ).astype(kappa.dtype)
    fields = flexion_fields(patch_tiles.reshape(PATCH_ROWS, PATCH_COLS))
    width = tile_width
    last = PATCH_ROWS - width
    left = shifted(fields[:, :, last:], "py", 1)
    right = shifted(fields[:, :, :width], "py", -1)
    above = shifted(fields[:, last:], "px", 1)
    below = shifted(fields[:, :width], "px", -1)
    corners_above = shifted(
        jnp.concatenate([left[:, last:], right[:, last:]], axis=2), "px", 1
    )
    corners_below = shifted(
        jnp.concatenate([left[:, :width], right[:, :width]], axis=2), "px", -1
    )
    above_left, above_right = corners_above[:, :, :width], corners_above[:, :, width:]
    below_left, below_right = corners_below[:, :, :width], corners_below[:, :, width:]
    ramp = (jnp.arange(width, dtype=jnp.float32) + 0.5) / width
    top_weight = jnp.where(band_index > 0, ramp, 1.0)[None, :, None]
    bottom_weight = jnp.where(band_index < rows_axis - 1, ramp[::-1], 1.0)[None, :, None]
    left_weight = jnp.where(column_index > 0, ramp, 1.0)[None, None, :]
    right_weight = jnp.where(column_index < cols_axis - 1, ramp[::-1], 1.0)[None, None, :]
    edges = edge_blend(
        fields, above, below, left, right, top_weight[0], bottom_weight[0], left_weight[0],
        right_weight[0],
    )
    return corner_blend(
        edges,
        fields,
        jnp.stack([above, below], axis=1),
        jnp.stack([left, right], axis=1),
        jnp.stack([corners_above, corners_below], axis=1),
        jnp.stack([top_weight[0], bottom_weight[0]]),
        jnp.stack([left_weight[0], right_weight[0]]),
    )


def edge_kernel(own_ref, above_ref, below_ref, left_ref, right_ref, tw_ref, bw_ref, lw_ref,
                rw_ref, out_ref):
    row_block = pl.program_id(1)
    width = left_ref.shape[2]
    count = own_ref.shape[2]
    own = own_ref[0].astype(jnp.float32)
    tw, bw = tw_ref[...], bw_ref[...]

    @pl.when(row_block == 0)
    def _():
        out_ref[0] = tw * own + (1.0 - tw) * above_ref[0].astype(jnp.float32)

    @pl.when(row_block == pl.num_programs(1) - 1)
    def _():
        out_ref[0] = bw * own + (1.0 - bw) * below_ref[0].astype(jnp.float32)

    @pl.when((row_block > 0) & (row_block < pl.num_programs(1) - 1))
    def _():
        out_ref[0] = own

    lw, rw = lw_ref[...], rw_ref[...]
    out_ref[0, :, :width] = (
        lw * out_ref[0, :, :width] + (1.0 - lw) * left_ref[0].astype(jnp.float32)
    )
    out_ref[0, :, count - width :] = (
        rw * out_ref[0, :, count - width :] + (1.0 - rw) * right_ref[0].astype(jnp.float32)
    )


def edge_blend(fields, above, below, left, right, tw, bw, lw, rw):
    planes, count = fields.shape[0], fields.shape[1]
    width = above.shape[1]
    blocks = count // width
    return pl.pallas_call(
        edge_kernel,
        grid=(planes, blocks),
        in_specs=[
            pl.BlockSpec((1, width, count), lambda f, r: (f, r, 0)),
            pl.BlockSpec((1, width, count), lambda f, r: (f, 0, 0)),
            pl.BlockSpec((1, width, count), lambda f, r: (f, 0, 0)),
            pl.BlockSpec((1, width, width), lambda f, r: (f, r, 0)),
            pl.BlockSpec((1, width, width), lambda f, r: (f, r, 0)),
            pl.BlockSpec((width, 1), lambda f, r: (0, 0)),
            pl.BlockSpec((width, 1), lambda f, r: (0, 0)),
            pl.BlockSpec((1, width), lambda f, r: (0, 0)),
            pl.BlockSpec((1, width), lambda f, r: (0, 0)),
        ],
        out_specs=pl.BlockSpec((1, width, count), lambda f, r: (f, r, 0)),
        out_shape=jax.ShapeDtypeStruct(fields.shape, jnp.float32),
        cost_estimate=pl.CostEstimate(
            flops=6 * planes * count * count, bytes_accessed=planes * count * count * 7,
            transcendentals=0,
        ),
    )(fields, above, below, left, right, tw, bw, lw, rw)


def corner_kernel(edges_ref, own_ref, row_ref, col_ref, corner_ref, rw_ref, cw_ref, out_ref):
    del edges_ref
    own = own_ref[0].astype(jnp.float32)
    row_weight, col_weight = rw_ref[0], cw_ref[0]
    rows_done = row_weight * own + (1.0 - row_weight) * row_ref[0, 0].astype(jnp.float32)
    strip_rows = (
        row_weight * col_ref[0, 0].astype(jnp.float32)
        + (1.0 - row_weight) * corner_ref[0, 0].astype(jnp.float32)
    )
    out_ref[0] = col_weight * rows_done + (1.0 - col_weight) * strip_rows


def corner_blend(edges, fields, row_strips, col_strips, corners, row_weights, col_weights):
    planes, count = fields.shape[0], fields.shape[1]
    width = row_strips.shape[2]
    far = count // width - 1
    return pl.pallas_call(
        corner_kernel,
        grid=(planes, 2, 2),
        in_specs=[
            pl.BlockSpec(memory_space=pl.ANY),
            pl.BlockSpec((1, width, width), lambda f, a, c: (f, a * far, c * far)),
            pl.BlockSpec((1, 1, width, width), lambda f, a, c: (f, a, 0, c * far)),
            pl.BlockSpec((1, 1, width, width), lambda f, a, c: (f, c, a * far, 0)),
            pl.BlockSpec((1, 1, width, width), lambda f, a, c: (f, a, 0, c)),
            pl.BlockSpec((1, width, 1), lambda f, a, c: (a, 0, 0)),
            pl.BlockSpec((1, 1, width), lambda f, a, c: (c, 0, 0)),
        ],
        out_specs=pl.BlockSpec((1, width, width), lambda f, a, c: (f, a * far, c * far)),
        out_shape=jax.ShapeDtypeStruct(edges.shape, edges.dtype),
        input_output_aliases={0: 0},
        cost_estimate=pl.CostEstimate(
            flops=9 * planes * 4 * width * width, bytes_accessed=planes * 4 * width * width * 12,
            transcendentals=0,
        ),
    )(edges, fields, row_strips, col_strips, corners, row_weights, col_weights)


def solution(mesh):
    placed = (
        P(("px", "py"), None),
        P(("px", "py"), None, None),
        P(("px", "py"), None, None),
        P(("px", "py"), None),
    )
    return jax.shard_map(
        on_device, mesh=mesh, in_specs=placed, out_specs=P(None, "px", "py"), check_vma=False
    )
```

```python
import math

import jax
import ml_dtypes
import numpy as np
import jax.numpy as jnp
from jax import lax
from jax.sharding import PartitionSpec as P

PATCH_ROWS = 512
PATCH_COLS = 512


def shifted(shard, axis, by):
    size = lax.axis_size(axis)
    pairs = [(i, i + by) for i in range(size) if 0 <= i + by < size]
    return lax.ppermute(shard, axis, pairs)


def padded(block, sides, width):
    for axis, dim in sides:
        count = lax.axis_size(axis)
        forward = [(i, i + 1) for i in range(count - 1)]
        backward = [(target, source) for source, target in forward]
        low = lax.ppermute(
            lax.slice_in_dim(block, block.shape[dim] - width, None, axis=dim), axis, forward
        )
        high = lax.ppermute(lax.slice_in_dim(block, 0, width, axis=dim), axis, backward)
        block = jnp.concatenate([low, block, high], axis=dim)
    return block


def dft_tables(length):
    positions = np.arange(length, dtype=np.int64)
    phases = positions[:, None] * positions[None, :] % length
    angles = phases.astype(np.float32) * np.float32(2.0 * math.pi / length)
    return (np.cos(angles).astype(np.float32), np.sin(angles).astype(np.float32))


def table(values):
    return jnp.asarray(values.astype(ml_dtypes.bfloat16))


def wavenumbers(length):
    positions = jnp.arange(length, dtype=jnp.int32)
    signed = positions - length * (positions >= (length + 1) // 2).astype(jnp.int32)
    return signed.astype(jnp.float32) * (2.0 / length)


def dot32(a, b):
    return jnp.dot(a, b, preferred_element_type=jnp.float32)


def flexion_fields(pixels):
    row_count = pixels.shape[0]
    col_count = pixels.shape[1]
    assert row_count == col_count
    cos_np, sin_np = dft_tables(row_count)
    cosine, sine = table(cos_np), table(sin_np)
    n = row_count
    halves = jnp.concatenate([dot32(pixels, cosine), dot32(pixels, sine)], axis=1).astype(
        jnp.bfloat16
    )
    by_cos = dot32(cosine, halves)
    by_sin = dot32(sine, halves)
    real_part = by_cos[:, :n] - by_sin[:, n:]
    imag_part = -(by_sin[:, :n] + by_cos[:, n:])
    across = wavenumbers(col_count)[None, :]
    down = wavenumbers(row_count)[:, None]
    scale = 1.0 / (row_count * col_count)
    power = across * across + down * down
    safe_power = jnp.where(power > 0, power, 1.0)
    cube_real = across * across * across - 3.0 * across * down * down
    cube_imag = 3.0 * across * across * down - down * down * down
    one_real = (-down * real_part - across * imag_part) * scale
    one_imag = (across * real_part - down * imag_part) * scale
    kernel_real = -cube_imag / safe_power
    kernel_imag = cube_real / safe_power
    three_real = (kernel_real * real_part - kernel_imag * imag_part) * scale
    three_imag = (kernel_real * imag_part + kernel_imag * real_part) * scale
    spectra = jnp.concatenate([one_real, three_real, one_imag, three_imag], axis=1).astype(
        jnp.bfloat16
    )
    by_cos = dot32(cosine, spectra)
    by_sin = dot32(sine, spectra)
    columns_done = jnp.concatenate(
        [
            by_cos[:, : 2 * n] - by_sin[:, 2 * n :],
            by_sin[:, : 2 * n] + by_cos[:, 2 * n :],
        ],
        axis=1,
    ).astype(jnp.bfloat16)
    arranged = jnp.concatenate(
        [columns_done[:, k * n : (k + 1) * n] for k in range(4)], axis=0
    )
    width = n // 4
    edge_cols = jnp.concatenate(
        [cosine[:, :width], cosine[:, n - width :], sine[:, :width], sine[:, n - width :]], axis=1
    )
    edge = dot32(arranged, edge_cols)
    edge_cos, edge_sin = edge[:, : 2 * width], edge[:, 2 * width :]
    edge_fields = jnp.stack(
        [
            edge_cos[:n] - edge_sin[2 * n : 3 * n],
            edge_sin[:n] + edge_cos[2 * n : 3 * n],
            edge_cos[n : 2 * n] - edge_sin[3 * n :],
            edge_sin[n : 2 * n] + edge_cos[3 * n :],
        ]
    ).astype(jnp.bfloat16)
    by_cos = dot32(arranged, cosine)
    by_sin = dot32(arranged, sine)
    return edge_fields, jnp.stack(
        [
            by_cos[:n] - by_sin[2 * n : 3 * n],
            by_sin[:n] + by_cos[2 * n : 3 * n],
            by_cos[n : 2 * n] - by_sin[3 * n :],
            by_sin[n : 2 * n] + by_cos[3 * n :],
        ]
    ).astype(jnp.bfloat16)


def blend_edges(extended, has_top, has_bottom, has_left, has_right, width):
    values = extended.astype(jnp.float32)
    row_count = values.shape[1] - 2 * width
    col_count = values.shape[2] - 2 * width
    ramp = (jnp.arange(width, dtype=jnp.float32) + 0.5) / width
    top_weight = jnp.where(has_top, ramp, 1.0)[None, :, None]
    bottom_weight = jnp.where(has_bottom, ramp[::-1], 1.0)[None, :, None]
    middle = values[:, width : width + row_count, :]
    top_band = top_weight * middle[:, :width] + (1.0 - top_weight) * values[:, :width]
    bottom_band = (
        bottom_weight * middle[:, row_count - width :]
        + (1.0 - bottom_weight) * values[:, row_count + width :]
    )
    middle = jnp.concatenate([top_band, middle[:, width : row_count - width], bottom_band], axis=1)
    left_weight = jnp.where(has_left, ramp, 1.0)[None, None, :]
    right_weight = jnp.where(has_right, ramp[::-1], 1.0)[None, None, :]
    inner = middle[:, :, width : width + col_count]
    left_band = left_weight * inner[:, :, :width] + (1.0 - left_weight) * middle[:, :, :width]
    right_band = (
        right_weight * inner[:, :, col_count - width :]
        + (1.0 - right_weight) * middle[:, :, col_count + width :]
    )
    return jnp.concatenate([left_band, inner[:, :, width : col_count - width], right_band], axis=2)


def one_hot_rows(codes, count, values):
    picks = codes[None, :] == jnp.arange(1, count + 1, dtype=jnp.int32)[:, None]
    return jnp.dot(picks.astype(values.dtype), values, preferred_element_type=jnp.float32)


def gathered_rows(table_rows, picks):
    chosen = picks.reshape(-1)[:, None] == jnp.arange(table_rows.shape[0], dtype=jnp.int32)
    values = jnp.dot(chosen.astype(table_rows.dtype), table_rows, preferred_element_type=jnp.float32)
    return values.astype(table_rows.dtype).reshape(picks.shape + table_rows.shape[1:])


CODE_SPLIT = 64
CODE_ROWS = 16


def with_codes(values, codes):
    depth, width = values.shape[1], values.shape[2]
    halves = jnp.concatenate([codes // CODE_SPLIT, codes % CODE_SPLIT], axis=1)
    code_rows = halves.reshape(values.shape[0], -1, width).astype(values.dtype)
    pad = jnp.zeros((values.shape[0], CODE_ROWS - code_rows.shape[1], width), values.dtype)
    return jnp.concatenate([values, code_rows, pad], axis=1)


def split_codes(payload, depth):
    width = payload.shape[2]
    used = 2 * depth // width
    halves = payload[:, depth : depth + used].reshape(payload.shape[0], 2 * depth)
    halves = halves.astype(jnp.int32)
    codes = halves[:, :depth] * CODE_SPLIT + halves[:, depth:]
    return payload[:, :depth].reshape(-1, width), codes.reshape(-1)


def sent_block(kappa, lists, slots, counts):
    depth = lists.shape[1]
    live = jnp.arange(depth, dtype=jnp.int32)[None, :] < counts[:, None]
    codes = jnp.where(live, slots + 1, 0)
    return with_codes(gathered_rows(kappa, lists), codes)


def row_blend(own, above, below, top_weight, bottom_weight, width):
    count = own.shape[1]
    top = top_weight * own[:, :width] + (1.0 - top_weight) * above
    bottom = bottom_weight * own[:, count - width :] + (1.0 - bottom_weight) * below
    return jnp.concatenate([top, own[:, width : count - width], bottom], axis=1)


def on_device(kappa, send_list, dest_slot, send_count):
    tile_width = kappa.shape[1]
    rows_axis = lax.axis_size("px")
    cols_axis = lax.axis_size("py")
    band_index = lax.axis_index("px")
    column_index = lax.axis_index("py")
    tile_lists = send_list[0].reshape(rows_axis, cols_axis, -1)
    slot_lists = dest_slot[0].reshape(rows_axis, cols_axis, -1)
    pair_counts = send_count[0].reshape(rows_axis, cols_axis)
    slot_depth = tile_lists.shape[2]
    upper_band = jnp.maximum(band_index - 1, 0)
    upper_counts = jnp.where(band_index > 0, pair_counts[upper_band], 0)
    same_sent = sent_block(
        kappa, tile_lists[band_index], slot_lists[band_index], pair_counts[band_index]
    )
    rise_sent = sent_block(kappa, tile_lists[upper_band], slot_lists[upper_band], upper_counts)
    arrived = lax.all_to_all(jnp.stack([same_sent, rise_sent], axis=1), "py", 0, 0, tiled=True)
    same_values, same_codes = split_codes(arrived[:, 0], slot_depth)
    rise_values, rise_codes = split_codes(arrived[:, 1], slot_depth)
    rise_total = PATCH_ROWS * PATCH_COLS // tile_width // 4
    rise_live = rise_codes > 0
    rise_place = jnp.where(rise_live, jnp.cumsum(rise_live.astype(jnp.int32)), 0)
    packed_values = one_hot_rows(rise_place, rise_total, rise_values).astype(kappa.dtype)
    packed_picks = rise_place[None, :] == jnp.arange(1, rise_total + 1, dtype=jnp.int32)[:, None]
    packed_codes = jnp.sum(jnp.where(packed_picks, rise_codes[None, :], 0), axis=1)
    packed = with_codes(packed_values.reshape(1, rise_total, tile_width), packed_codes[None])
    raised_values, raised_codes = split_codes(shifted(packed, "px", -1), rise_total)
    slot_total = PATCH_ROWS * PATCH_COLS // tile_width
    patch_tiles = (
        one_hot_rows(same_codes, slot_total, same_values)
        + one_hot_rows(raised_codes, slot_total, raised_values)
    ).astype(kappa.dtype)
    edge_fields, fields = flexion_fields(patch_tiles.reshape(PATCH_ROWS, PATCH_COLS))
    width = tile_width
    last = PATCH_ROWS - width
    left = shifted(edge_fields[:, :, width:], "py", 1)
    right = shifted(edge_fields[:, :, :width], "py", -1)
    above = shifted(fields[:, last:], "px", 1)
    below = shifted(fields[:, :width], "px", -1)
    corners_above = shifted(
        jnp.concatenate([left[:, last:], right[:, last:]], axis=2), "px", 1
    )
    corners_below = shifted(
        jnp.concatenate([left[:, :width], right[:, :width]], axis=2), "px", -1
    )
    above_left, above_right = corners_above[:, :, :width], corners_above[:, :, width:]
    below_left, below_right = corners_below[:, :, :width], corners_below[:, :, width:]
    ramp = (jnp.arange(width, dtype=jnp.float32) + 0.5) / width
    top_weight = jnp.where(band_index > 0, ramp, 1.0)[None, :, None]
    bottom_weight = jnp.where(band_index < rows_axis - 1, ramp[::-1], 1.0)[None, :, None]
    left_weight = jnp.where(column_index > 0, ramp, 1.0)[None, None, :]
    right_weight = jnp.where(column_index < cols_axis - 1, ramp[::-1], 1.0)[None, None, :]
    f32 = lambda x: x.astype(jnp.float32)
    inner = row_blend(f32(fields), f32(above), f32(below), top_weight, bottom_weight, width)
    left_strip = row_blend(
        f32(left), f32(above_left), f32(below_left), top_weight, bottom_weight, width
    )
    right_strip = row_blend(
        f32(right), f32(above_right), f32(below_right), top_weight, bottom_weight, width
    )
    col_count = inner.shape[2]
    left_band = left_weight * inner[:, :, :width] + (1.0 - left_weight) * left_strip
    right_band = right_weight * inner[:, :, col_count - width :] + (1.0 - right_weight) * right_strip
    return jnp.concatenate(
        [left_band, inner[:, :, width : col_count - width], right_band], axis=2
    )


def solution(mesh):
    placed = (
        P(("px", "py"), None),
        P(("px", "py"), None, None),
        P(("px", "py"), None, None),
        P(("px", "py"), None),
    )
    return jax.shard_map(
        on_device, mesh=mesh, in_specs=placed, out_specs=P(None, "px", "py"), check_vma=False
    )
```

```python
import math

import jax
import ml_dtypes
import numpy as np
import jax.numpy as jnp
from jax import lax
from jax.sharding import PartitionSpec as P

PATCH_ROWS = 512
PATCH_COLS = 512


def shifted(shard, axis, by):
    size = lax.axis_size(axis)
    pairs = [(i, i + by) for i in range(size) if 0 <= i + by < size]
    return lax.ppermute(shard, axis, pairs)


def padded(block, sides, width):
    for axis, dim in sides:
        count = lax.axis_size(axis)
        forward = [(i, i + 1) for i in range(count - 1)]
        backward = [(target, source) for source, target in forward]
        low = lax.ppermute(
            lax.slice_in_dim(block, block.shape[dim] - width, None, axis=dim), axis, forward
        )
        high = lax.ppermute(lax.slice_in_dim(block, 0, width, axis=dim), axis, backward)
        block = jnp.concatenate([low, block, high], axis=dim)
    return block


def dft_tables(length):
    positions = np.arange(length, dtype=np.int64)
    phases = positions[:, None] * positions[None, :] % length
    angles = phases.astype(np.float32) * np.float32(2.0 * math.pi / length)
    return (np.cos(angles).astype(np.float32), np.sin(angles).astype(np.float32))


def table(values):
    return jnp.asarray(values.astype(ml_dtypes.bfloat16))


def wavenumbers(length):
    positions = jnp.arange(length, dtype=jnp.int32)
    signed = positions - length * (positions >= (length + 1) // 2).astype(jnp.int32)
    return signed.astype(jnp.float32) * (2.0 / length)


def dot32(a, b):
    return jnp.dot(a, b, preferred_element_type=jnp.float32)


def flexion_fields(pixels):
    row_count = pixels.shape[0]
    col_count = pixels.shape[1]
    assert row_count == col_count
    cos_np, sin_np = dft_tables(row_count)
    cosine, sine = table(cos_np), table(sin_np)
    n = row_count
    halves = jnp.concatenate([dot32(pixels, cosine), dot32(pixels, sine)], axis=1).astype(
        jnp.bfloat16
    )
    by_cos = dot32(cosine, halves)
    by_sin = dot32(sine, halves)
    real_part = by_cos[:, :n] - by_sin[:, n:]
    imag_part = -(by_sin[:, :n] + by_cos[:, n:])
    across = wavenumbers(col_count)[None, :]
    down = wavenumbers(row_count)[:, None]
    scale = 1.0 / (row_count * col_count)
    power = across * across + down * down
    safe_power = jnp.where(power > 0, power, 1.0)
    cube_real = across * across * across - 3.0 * across * down * down
    cube_imag = 3.0 * across * across * down - down * down * down
    one_real = (-down * real_part - across * imag_part) * scale
    one_imag = (across * real_part - down * imag_part) * scale
    kernel_real = -cube_imag / safe_power
    kernel_imag = cube_real / safe_power
    three_real = (kernel_real * real_part - kernel_imag * imag_part) * scale
    three_imag = (kernel_real * imag_part + kernel_imag * real_part) * scale
    spectra = jnp.concatenate([one_real, three_real, one_imag, three_imag], axis=1).astype(
        jnp.bfloat16
    )
    by_cos = dot32(cosine, spectra)
    by_sin = dot32(sine, spectra)
    columns_done = jnp.concatenate(
        [
            by_cos[:, : 2 * n] - by_sin[:, 2 * n :],
            by_sin[:, : 2 * n] + by_cos[:, 2 * n :],
        ],
        axis=1,
    ).astype(jnp.bfloat16)
    arranged = jnp.concatenate(
        [columns_done[:, k * n : (k + 1) * n] for k in range(4)], axis=0
    )
    width = n // 4
    edge_cols = jnp.concatenate(
        [cosine[:, :width], cosine[:, n - width :], sine[:, :width], sine[:, n - width :]], axis=1
    )
    edge = dot32(arranged, edge_cols)
    edge_cos, edge_sin = edge[:, : 2 * width], edge[:, 2 * width :]
    edge_fields = jnp.stack(
        [
            edge_cos[:n] - edge_sin[2 * n : 3 * n],
            edge_sin[:n] + edge_cos[2 * n : 3 * n],
            edge_cos[n : 2 * n] - edge_sin[3 * n :],
            edge_sin[n : 2 * n] + edge_cos[3 * n :],
        ]
    ).astype(jnp.bfloat16)
    by_cos = dot32(arranged, cosine)
    by_sin = dot32(arranged, sine)
    return edge_fields, jnp.stack(
        [
            by_cos[:n] - by_sin[2 * n : 3 * n],
            by_sin[:n] + by_cos[2 * n : 3 * n],
            by_cos[n : 2 * n] - by_sin[3 * n :],
            by_sin[n : 2 * n] + by_cos[3 * n :],
        ]
    ).astype(jnp.bfloat16)


def blend_edges(extended, has_top, has_bottom, has_left, has_right, width):
    values = extended.astype(jnp.float32)
    row_count = values.shape[1] - 2 * width
    col_count = values.shape[2] - 2 * width
    ramp = (jnp.arange(width, dtype=jnp.float32) + 0.5) / width
    top_weight = jnp.where(has_top, ramp, 1.0)[None, :, None]
    bottom_weight = jnp.where(has_bottom, ramp[::-1], 1.0)[None, :, None]
    middle = values[:, width : width + row_count, :]
    top_band = top_weight * middle[:, :width] + (1.0 - top_weight) * values[:, :width]
    bottom_band = (
        bottom_weight * middle[:, row_count - width :]
        + (1.0 - bottom_weight) * values[:, row_count + width :]
    )
    middle = jnp.concatenate([top_band, middle[:, width : row_count - width], bottom_band], axis=1)
    left_weight = jnp.where(has_left, ramp, 1.0)[None, None, :]
    right_weight = jnp.where(has_right, ramp[::-1], 1.0)[None, None, :]
    inner = middle[:, :, width : width + col_count]
    left_band = left_weight * inner[:, :, :width] + (1.0 - left_weight) * middle[:, :, :width]
    right_band = (
        right_weight * inner[:, :, col_count - width :]
        + (1.0 - right_weight) * middle[:, :, col_count + width :]
    )
    return jnp.concatenate([left_band, inner[:, :, width : col_count - width], right_band], axis=2)


def one_hot_rows(codes, count, values):
    picks = codes[None, :] == jnp.arange(1, count + 1, dtype=jnp.int32)[:, None]
    return jnp.dot(picks.astype(values.dtype), values, preferred_element_type=jnp.float32)


def gathered_rows(table_rows, picks):
    chosen = picks.reshape(-1)[:, None] == jnp.arange(table_rows.shape[0], dtype=jnp.int32)
    values = jnp.dot(chosen.astype(table_rows.dtype), table_rows, preferred_element_type=jnp.float32)
    return values.astype(table_rows.dtype).reshape(picks.shape + table_rows.shape[1:])


CODE_SPLIT = 64
CODE_ROWS = 16


def with_codes(values, codes):
    depth, width = values.shape[1], values.shape[2]
    halves = jnp.concatenate([codes // CODE_SPLIT, codes % CODE_SPLIT], axis=1)
    code_rows = halves.reshape(values.shape[0], -1, width).astype(values.dtype)
    pad = jnp.zeros((values.shape[0], CODE_ROWS - code_rows.shape[1], width), values.dtype)
    return jnp.concatenate([values, code_rows, pad], axis=1)


def split_codes(payload, depth):
    width = payload.shape[2]
    used = 2 * depth // width
    halves = payload[:, depth : depth + used].reshape(payload.shape[0], 2 * depth)
    halves = halves.astype(jnp.int32)
    codes = halves[:, :depth] * CODE_SPLIT + halves[:, depth:]
    return payload[:, :depth].reshape(-1, width), codes.reshape(-1)


def sent_block(kappa, lists, slots, counts):
    depth = lists.shape[1]
    live = jnp.arange(depth, dtype=jnp.int32)[None, :] < counts[:, None]
    codes = jnp.where(live, slots + 1, 0)
    return with_codes(gathered_rows(kappa, lists), codes)


def row_blend(own, above, below, top_weight, bottom_weight, width):
    count = own.shape[1]
    top = top_weight * own[:, :width] + (1.0 - top_weight) * above
    bottom = bottom_weight * own[:, count - width :] + (1.0 - bottom_weight) * below
    return jnp.concatenate([top, own[:, width : count - width], bottom], axis=1)


def on_device(kappa, send_list, dest_slot, send_count):
    tile_width = kappa.shape[1]
    rows_axis = lax.axis_size("px")
    cols_axis = lax.axis_size("py")
    band_index = lax.axis_index("px")
    column_index = lax.axis_index("py")
    slot_depth = send_list.shape[2]
    upper_band = jnp.maximum(band_index - 1, 0)
    band_rows = lambda table, band: lax.dynamic_slice_in_dim(table[0], band * cols_axis, cols_axis)
    upper_counts = jnp.where(band_index > 0, band_rows(send_count, upper_band), 0)
    same_sent = sent_block(
        kappa,
        band_rows(send_list, band_index),
        band_rows(dest_slot, band_index),
        band_rows(send_count, band_index),
    )
    rise_sent = sent_block(
        kappa, band_rows(send_list, upper_band), band_rows(dest_slot, upper_band), upper_counts
    )
    arrived = lax.all_to_all(jnp.stack([same_sent, rise_sent], axis=1), "py", 0, 0, tiled=True)
    same_values, same_codes = split_codes(arrived[:, 0], slot_depth)
    rise_values, rise_codes = split_codes(arrived[:, 1], slot_depth)
    rise_total = PATCH_ROWS * PATCH_COLS // tile_width // 4
    rise_live = rise_codes > 0
    rise_place = jnp.where(rise_live, jnp.cumsum(rise_live.astype(jnp.int32)), 0)
    packed_values = one_hot_rows(rise_place, rise_total, rise_values).astype(kappa.dtype)
    packed_picks = rise_place[None, :] == jnp.arange(1, rise_total + 1, dtype=jnp.int32)[:, None]
    packed_codes = jnp.sum(jnp.where(packed_picks, rise_codes[None, :], 0), axis=1)
    packed = with_codes(packed_values.reshape(1, rise_total, tile_width), packed_codes[None])
    raised_values, raised_codes = split_codes(shifted(packed, "px", -1), rise_total)
    slot_total = PATCH_ROWS * PATCH_COLS // tile_width
    patch_tiles = (
        one_hot_rows(same_codes, slot_total, same_values)
        + one_hot_rows(raised_codes, slot_total, raised_values)
    ).astype(kappa.dtype)
    edge_fields, fields = flexion_fields(patch_tiles.reshape(PATCH_ROWS, PATCH_COLS))
    width = tile_width
    last = PATCH_ROWS - width
    left = shifted(edge_fields[:, :, width:], "py", 1)
    right = shifted(edge_fields[:, :, :width], "py", -1)
    above = shifted(fields[:, last:], "px", 1)
    below = shifted(fields[:, :width], "px", -1)
    corners_above = shifted(
        jnp.concatenate([left[:, last:], right[:, last:]], axis=2), "px", 1
    )
    corners_below = shifted(
        jnp.concatenate([left[:, :width], right[:, :width]], axis=2), "px", -1
    )
    above_left, above_right = corners_above[:, :, :width], corners_above[:, :, width:]
    below_left, below_right = corners_below[:, :, :width], corners_below[:, :, width:]
    ramp = (jnp.arange(width, dtype=jnp.float32) + 0.5) / width
    top_weight = jnp.where(band_index > 0, ramp, 1.0)[None, :, None]
    bottom_weight = jnp.where(band_index < rows_axis - 1, ramp[::-1], 1.0)[None, :, None]
    left_weight = jnp.where(column_index > 0, ramp, 1.0)[None, None, :]
    right_weight = jnp.where(column_index < cols_axis - 1, ramp[::-1], 1.0)[None, None, :]
    f32 = lambda x: x.astype(jnp.float32)
    inner = row_blend(f32(fields), f32(above), f32(below), top_weight, bottom_weight, width)
    left_strip = row_blend(
        f32(left), f32(above_left), f32(below_left), top_weight, bottom_weight, width
    )
    right_strip = row_blend(
        f32(right), f32(above_right), f32(below_right), top_weight, bottom_weight, width
    )
    col_count = inner.shape[2]
    left_band = left_weight * inner[:, :, :width] + (1.0 - left_weight) * left_strip
    right_band = right_weight * inner[:, :, col_count - width :] + (1.0 - right_weight) * right_strip
    return jnp.concatenate(
        [left_band, inner[:, :, width : col_count - width], right_band], axis=2
    )


def solution(mesh):
    placed = (
        P(("px", "py"), None),
        P(("px", "py"), None, None),
        P(("px", "py"), None, None),
        P(("px", "py"), None),
    )
    return jax.shard_map(
        on_device, mesh=mesh, in_specs=placed, out_specs=P(None, "px", "py"), check_vma=False
    )
```

```python
import math

import jax
import ml_dtypes
import numpy as np
import jax.numpy as jnp
from jax import lax
from jax.sharding import PartitionSpec as P

PATCH_ROWS = 512
PATCH_COLS = 512


def shifted(shard, axis, by):
    size = lax.axis_size(axis)
    pairs = [(i, i + by) for i in range(size) if 0 <= i + by < size]
    return lax.ppermute(shard, axis, pairs)


def padded(block, sides, width):
    for axis, dim in sides:
        count = lax.axis_size(axis)
        forward = [(i, i + 1) for i in range(count - 1)]
        backward = [(target, source) for source, target in forward]
        low = lax.ppermute(
            lax.slice_in_dim(block, block.shape[dim] - width, None, axis=dim), axis, forward
        )
        high = lax.ppermute(lax.slice_in_dim(block, 0, width, axis=dim), axis, backward)
        block = jnp.concatenate([low, block, high], axis=dim)
    return block


def dft_tables(length):
    positions = np.arange(length, dtype=np.int64)
    phases = positions[:, None] * positions[None, :] % length
    angles = phases.astype(np.float32) * np.float32(2.0 * math.pi / length)
    return (np.cos(angles).astype(np.float32), np.sin(angles).astype(np.float32))


def table(values):
    return jnp.asarray(values.astype(ml_dtypes.bfloat16))


def wavenumbers(length):
    positions = jnp.arange(length, dtype=jnp.int32)
    signed = positions - length * (positions >= (length + 1) // 2).astype(jnp.int32)
    return signed.astype(jnp.float32) * (2.0 / length)


def dot32(a, b):
    return jnp.dot(a, b, preferred_element_type=jnp.float32)


def flexion_fields(pixels):
    row_count = pixels.shape[0]
    col_count = pixels.shape[1]
    assert row_count == col_count
    cos_np, sin_np = dft_tables(row_count)
    cosine, sine = table(cos_np), table(sin_np)
    n = row_count
    halves = jnp.concatenate([dot32(pixels, cosine), dot32(pixels, sine)], axis=1).astype(
        jnp.bfloat16
    )
    by_cos = dot32(cosine, halves)
    by_sin = dot32(sine, halves)
    real_part = by_cos[:, :n] - by_sin[:, n:]
    imag_part = -(by_sin[:, :n] + by_cos[:, n:])
    across = wavenumbers(col_count)[None, :]
    down = wavenumbers(row_count)[:, None]
    scale = 1.0 / (row_count * col_count)
    power = across * across + down * down
    safe_power = jnp.where(power > 0, power, 1.0)
    cube_real = across * across * across - 3.0 * across * down * down
    cube_imag = 3.0 * across * across * down - down * down * down
    one_real = (-down * real_part - across * imag_part) * scale
    one_imag = (across * real_part - down * imag_part) * scale
    kernel_real = -cube_imag / safe_power
    kernel_imag = cube_real / safe_power
    three_real = (kernel_real * real_part - kernel_imag * imag_part) * scale
    three_imag = (kernel_real * imag_part + kernel_imag * real_part) * scale
    spectra = jnp.concatenate([one_real, three_real, one_imag, three_imag], axis=1).astype(
        jnp.bfloat16
    )
    by_cos = dot32(cosine, spectra)
    by_sin = dot32(sine, spectra)
    columns_done = jnp.concatenate(
        [
            by_cos[:, : 2 * n] - by_sin[:, 2 * n :],
            by_sin[:, : 2 * n] + by_cos[:, 2 * n :],
        ],
        axis=1,
    ).astype(jnp.bfloat16)
    arranged = jnp.concatenate(
        [columns_done[:, k * n : (k + 1) * n] for k in range(4)], axis=0
    )
    width = n // 4
    edge_cols = jnp.concatenate(
        [cosine[:, :width], cosine[:, n - width :], sine[:, :width], sine[:, n - width :]], axis=1
    )
    edge = dot32(arranged, edge_cols)
    edge_cos, edge_sin = edge[:, : 2 * width], edge[:, 2 * width :]
    edge_fields = jnp.stack(
        [
            edge_cos[:n] - edge_sin[2 * n : 3 * n],
            edge_sin[:n] + edge_cos[2 * n : 3 * n],
            edge_cos[n : 2 * n] - edge_sin[3 * n :],
            edge_sin[n : 2 * n] + edge_cos[3 * n :],
        ]
    ).astype(jnp.bfloat16)
    by_cos = dot32(arranged, cosine)
    by_sin = dot32(arranged, sine)
    return edge_fields, jnp.stack(
        [
            by_cos[:n] - by_sin[2 * n : 3 * n],
            by_sin[:n] + by_cos[2 * n : 3 * n],
            by_cos[n : 2 * n] - by_sin[3 * n :],
            by_sin[n : 2 * n] + by_cos[3 * n :],
        ]
    ).astype(jnp.bfloat16)


def blend_edges(extended, has_top, has_bottom, has_left, has_right, width):
    values = extended.astype(jnp.float32)
    row_count = values.shape[1] - 2 * width
    col_count = values.shape[2] - 2 * width
    ramp = (jnp.arange(width, dtype=jnp.float32) + 0.5) / width
    top_weight = jnp.where(has_top, ramp, 1.0)[None, :, None]
    bottom_weight = jnp.where(has_bottom, ramp[::-1], 1.0)[None, :, None]
    middle = values[:, width : width + row_count, :]
    top_band = top_weight * middle[:, :width] + (1.0 - top_weight) * values[:, :width]
    bottom_band = (
        bottom_weight * middle[:, row_count - width :]
        + (1.0 - bottom_weight) * values[:, row_count + width :]
    )
    middle = jnp.concatenate([top_band, middle[:, width : row_count - width], bottom_band], axis=1)
    left_weight = jnp.where(has_left, ramp, 1.0)[None, None, :]
    right_weight = jnp.where(has_right, ramp[::-1], 1.0)[None, None, :]
    inner = middle[:, :, width : width + col_count]
    left_band = left_weight * inner[:, :, :width] + (1.0 - left_weight) * middle[:, :, :width]
    right_band = (
        right_weight * inner[:, :, col_count - width :]
        + (1.0 - right_weight) * middle[:, :, col_count + width :]
    )
    return jnp.concatenate([left_band, inner[:, :, width : col_count - width], right_band], axis=2)


def one_hot_rows(codes, count, values):
    picks = codes[None, :] == jnp.arange(1, count + 1, dtype=jnp.int32)[:, None]
    return jnp.dot(picks.astype(values.dtype), values, preferred_element_type=jnp.float32)


def gathered_rows(table_rows, picks):
    chosen = picks.reshape(-1)[:, None] == jnp.arange(table_rows.shape[0], dtype=jnp.int32)
    values = jnp.dot(chosen.astype(table_rows.dtype), table_rows, preferred_element_type=jnp.float32)
    return values.astype(table_rows.dtype).reshape(picks.shape + table_rows.shape[1:])


CODE_SPLIT = 64
CODE_ROWS = 16


def with_codes(values, codes):
    depth, width = values.shape[1], values.shape[2]
    halves = jnp.concatenate([codes // CODE_SPLIT, codes % CODE_SPLIT], axis=1)
    code_rows = halves.reshape(values.shape[0], -1, width).astype(values.dtype)
    pad = jnp.zeros((values.shape[0], CODE_ROWS - code_rows.shape[1], width), values.dtype)
    return jnp.concatenate([values, code_rows, pad], axis=1)


def split_codes(payload, depth):
    width = payload.shape[2]
    used = 2 * depth // width
    halves = payload[:, depth : depth + used].reshape(payload.shape[0], 2 * depth)
    halves = halves.astype(jnp.int32)
    codes = halves[:, :depth] * CODE_SPLIT + halves[:, depth:]
    return payload[:, :depth].reshape(-1, width), codes.reshape(-1)


def sent_block(kappa, lists, slots, counts):
    depth = lists.shape[1]
    live = jnp.arange(depth, dtype=jnp.int32)[None, :] < counts[:, None]
    codes = jnp.where(live, slots + 1, 0)
    return with_codes(gathered_rows(kappa, lists), codes)


def row_blend(own, above, below, top_weight, bottom_weight, width):
    count = own.shape[1]
    top = top_weight * own[:, :width] + (1.0 - top_weight) * above
    bottom = bottom_weight * own[:, count - width :] + (1.0 - bottom_weight) * below
    return jnp.concatenate([top, own[:, width : count - width], bottom], axis=1)


def on_device(kappa, send_list, dest_slot, send_count):
    tile_width = kappa.shape[1]
    rows_axis = lax.axis_size("px")
    cols_axis = lax.axis_size("py")
    band_index = lax.axis_index("px")
    column_index = lax.axis_index("py")
    slot_depth = send_list.shape[2]
    upper_band = jnp.maximum(band_index - 1, 0)
    band_rows = lambda table, band: lax.dynamic_slice_in_dim(table[0], band * cols_axis, cols_axis)
    upper_counts = jnp.where(band_index > 0, band_rows(send_count, upper_band), 0)
    same_sent = sent_block(
        kappa,
        band_rows(send_list, band_index),
        band_rows(dest_slot, band_index),
        band_rows(send_count, band_index),
    )
    rise_sent = sent_block(
        kappa, band_rows(send_list, upper_band), band_rows(dest_slot, upper_band), upper_counts
    )
    arrived = lax.all_to_all(jnp.stack([same_sent, rise_sent], axis=1), "py", 0, 0, tiled=True)
    same_values, same_codes = split_codes(arrived[:, 0], slot_depth)
    rise_values, rise_codes = split_codes(arrived[:, 1], slot_depth)
    rise_total = PATCH_ROWS * PATCH_COLS // tile_width // 4
    rise_live = rise_codes > 0
    rise_place = jnp.where(rise_live, jnp.cumsum(rise_live.astype(jnp.int32)), 0)
    packed_values = one_hot_rows(rise_place, rise_total, rise_values).astype(kappa.dtype)
    packed_picks = rise_place[None, :] == jnp.arange(1, rise_total + 1, dtype=jnp.int32)[:, None]
    packed_codes = jnp.sum(jnp.where(packed_picks, rise_codes[None, :], 0), axis=1)
    packed = with_codes(packed_values.reshape(1, rise_total, tile_width), packed_codes[None])
    raised_values, raised_codes = split_codes(shifted(packed, "px", -1), rise_total)
    slot_total = PATCH_ROWS * PATCH_COLS // tile_width
    patch_tiles = (
        one_hot_rows(same_codes, slot_total, same_values)
        + one_hot_rows(raised_codes, slot_total, raised_values)
    ).astype(kappa.dtype)
    edge_fields, fields = flexion_fields(patch_tiles.reshape(PATCH_ROWS, PATCH_COLS))
    width = tile_width
    last = PATCH_ROWS - width
    left = shifted(edge_fields[:, :, width:], "py", 1)
    right = shifted(edge_fields[:, :, :width], "py", -1)
    above = shifted(fields[:, last:], "px", 1)
    below = shifted(fields[:, :width], "px", -1)
    corners_above = shifted(
        jnp.concatenate([left[:, last:], right[:, last:]], axis=2), "px", 1
    )
    corners_below = shifted(
        jnp.concatenate([left[:, :width], right[:, :width]], axis=2), "px", -1
    )
    above_left, above_right = corners_above[:, :, :width], corners_above[:, :, width:]
    below_left, below_right = corners_below[:, :, :width], corners_below[:, :, width:]
    ramp = (jnp.arange(width, dtype=jnp.float32) + 0.5) / width
    top_weight = jnp.where(band_index > 0, ramp, 1.0)[None, :, None]
    bottom_weight = jnp.where(band_index < rows_axis - 1, ramp[::-1], 1.0)[None, :, None]
    left_weight = jnp.where(column_index > 0, ramp, 1.0)[None, None, :]
    right_weight = jnp.where(column_index < cols_axis - 1, ramp[::-1], 1.0)[None, None, :]
    f32 = lambda x: x.astype(jnp.float32)
    count = fields.shape[1]
    ones = jnp.ones((count - 2 * width,), jnp.float32)
    row_weight = jnp.concatenate([top_weight[0, :, 0], ones, bottom_weight[0, :, 0]])[:, None]
    col_weight = jnp.concatenate([left_weight[0, 0], ones, right_weight[0, 0]])[None, :]
    zero_rows = jnp.zeros((fields.shape[0], count - 2 * width, 1), jnp.float32)
    vertical = jnp.concatenate(
        [f32(above), jnp.broadcast_to(zero_rows, (fields.shape[0], count - 2 * width, count)),
         f32(below)], axis=1
    )
    rows_done = row_weight * f32(fields) + (1.0 - row_weight) * vertical
    side = lambda strip, upper, lower: row_weight * f32(strip) + (1.0 - row_weight) * jnp.concatenate(
        [f32(upper), jnp.broadcast_to(zero_rows, (fields.shape[0], count - 2 * width, width)),
         f32(lower)], axis=1
    )
    left_rows = side(left, above_left, below_left)
    right_rows = side(right, above_right, below_right)
    horizontal = jnp.concatenate(
        [left_rows, jnp.broadcast_to(zero_rows[:, :1], (fields.shape[0], count, count - 2 * width)),
         right_rows], axis=2
    )
    return col_weight * rows_done + (1.0 - col_weight) * horizontal


def solution(mesh):
    placed = (
        P(("px", "py"), None),
        P(("px", "py"), None, None),
        P(("px", "py"), None, None),
        P(("px", "py"), None),
    )
    return jax.shard_map(
        on_device, mesh=mesh, in_specs=placed, out_specs=P(None, "px", "py"), check_vma=False
    )
```

```python
import math

import jax
import ml_dtypes
import numpy as np
import jax.numpy as jnp
from jax import lax
from jax.sharding import PartitionSpec as P

PATCH_ROWS = 512
PATCH_COLS = 512


def shifted(shard, axis, by):
    size = lax.axis_size(axis)
    pairs = [(i, i + by) for i in range(size) if 0 <= i + by < size]
    return lax.ppermute(shard, axis, pairs)


def padded(block, sides, width):
    for axis, dim in sides:
        count = lax.axis_size(axis)
        forward = [(i, i + 1) for i in range(count - 1)]
        backward = [(target, source) for source, target in forward]
        low = lax.ppermute(
            lax.slice_in_dim(block, block.shape[dim] - width, None, axis=dim), axis, forward
        )
        high = lax.ppermute(lax.slice_in_dim(block, 0, width, axis=dim), axis, backward)
        block = jnp.concatenate([low, block, high], axis=dim)
    return block


def dft_tables(length):
    positions = np.arange(length, dtype=np.int64)
    phases = positions[:, None] * positions[None, :] % length
    angles = phases.astype(np.float32) * np.float32(2.0 * math.pi / length)
    return (np.cos(angles).astype(np.float32), np.sin(angles).astype(np.float32))


def table(values):
    return jnp.asarray(values.astype(ml_dtypes.bfloat16))


def wavenumbers(length):
    positions = jnp.arange(length, dtype=jnp.int32)
    signed = positions - length * (positions >= (length + 1) // 2).astype(jnp.int32)
    return signed.astype(jnp.float32) * (2.0 / length)


def dot32(a, b):
    return jnp.dot(a, b, preferred_element_type=jnp.float32)


def flexion_fields(pixels):
    row_count = pixels.shape[0]
    col_count = pixels.shape[1]
    assert row_count == col_count
    cos_np, sin_np = dft_tables(row_count)
    cosine, sine = table(cos_np), table(sin_np)
    n = row_count
    halves = jnp.concatenate([dot32(pixels, cosine), dot32(pixels, sine)], axis=1).astype(
        jnp.bfloat16
    )
    by_cos = dot32(cosine, halves)
    by_sin = dot32(sine, halves)
    real_part = by_cos[:, :n] - by_sin[:, n:]
    imag_part = -(by_sin[:, :n] + by_cos[:, n:])
    across = wavenumbers(col_count)[None, :]
    down = wavenumbers(row_count)[:, None]
    scale = 1.0 / (row_count * col_count)
    power = across * across + down * down
    safe_power = jnp.where(power > 0, power, 1.0)
    cube_real = across * across * across - 3.0 * across * down * down
    cube_imag = 3.0 * across * across * down - down * down * down
    one_real = (-down * real_part - across * imag_part) * scale
    one_imag = (across * real_part - down * imag_part) * scale
    kernel_real = -cube_imag / safe_power
    kernel_imag = cube_real / safe_power
    three_real = (kernel_real * real_part - kernel_imag * imag_part) * scale
    three_imag = (kernel_real * imag_part + kernel_imag * real_part) * scale
    spectra = jnp.concatenate([one_real, three_real, one_imag, three_imag], axis=1).astype(
        jnp.bfloat16
    )
    by_cos = dot32(cosine, spectra)
    by_sin = dot32(sine, spectra)
    columns_done = jnp.concatenate(
        [
            by_cos[:, : 2 * n] - by_sin[:, 2 * n :],
            by_sin[:, : 2 * n] + by_cos[:, 2 * n :],
        ],
        axis=1,
    ).astype(jnp.bfloat16)
    arranged = jnp.concatenate(
        [columns_done[:, k * n : (k + 1) * n] for k in range(4)], axis=0
    )
    width = n // 4
    edge_cols = jnp.concatenate(
        [cosine[:, :width], cosine[:, n - width :], sine[:, :width], sine[:, n - width :]], axis=1
    )
    edge = dot32(arranged, edge_cols)
    edge_cos, edge_sin = edge[:, : 2 * width], edge[:, 2 * width :]
    edge_fields = jnp.stack(
        [
            edge_cos[:n] - edge_sin[2 * n : 3 * n],
            edge_sin[:n] + edge_cos[2 * n : 3 * n],
            edge_cos[n : 2 * n] - edge_sin[3 * n :],
            edge_sin[n : 2 * n] + edge_cos[3 * n :],
        ]
    ).astype(jnp.bfloat16)
    middle_cols = jnp.concatenate([cosine[:, width : n - width], sine[:, width : n - width]], axis=1)
    middle = dot32(arranged, middle_cols)
    mid_cos, mid_sin = middle[:, : n - 2 * width], middle[:, n - 2 * width :]
    middle_fields = jnp.stack(
        [
            mid_cos[:n] - mid_sin[2 * n : 3 * n],
            mid_sin[:n] + mid_cos[2 * n : 3 * n],
            mid_cos[n : 2 * n] - mid_sin[3 * n :],
            mid_sin[n : 2 * n] + mid_cos[3 * n :],
        ]
    ).astype(jnp.bfloat16)
    fields = jnp.concatenate(
        [edge_fields[:, :, :width], middle_fields, edge_fields[:, :, width:]], axis=2
    )
    return edge_fields, fields


def blend_edges(extended, has_top, has_bottom, has_left, has_right, width):
    values = extended.astype(jnp.float32)
    row_count = values.shape[1] - 2 * width
    col_count = values.shape[2] - 2 * width
    ramp = (jnp.arange(width, dtype=jnp.float32) + 0.5) / width
    top_weight = jnp.where(has_top, ramp, 1.0)[None, :, None]
    bottom_weight = jnp.where(has_bottom, ramp[::-1], 1.0)[None, :, None]
    middle = values[:, width : width + row_count, :]
    top_band = top_weight * middle[:, :width] + (1.0 - top_weight) * values[:, :width]
    bottom_band = (
        bottom_weight * middle[:, row_count - width :]
        + (1.0 - bottom_weight) * values[:, row_count + width :]
    )
    middle = jnp.concatenate([top_band, middle[:, width : row_count - width], bottom_band], axis=1)
    left_weight = jnp.where(has_left, ramp, 1.0)[None, None, :]
    right_weight = jnp.where(has_right, ramp[::-1], 1.0)[None, None, :]
    inner = middle[:, :, width : width + col_count]
    left_band = left_weight * inner[:, :, :width] + (1.0 - left_weight) * middle[:, :, :width]
    right_band = (
        right_weight * inner[:, :, col_count - width :]
        + (1.0 - right_weight) * middle[:, :, col_count + width :]
    )
    return jnp.concatenate([left_band, inner[:, :, width : col_count - width], right_band], axis=2)


def one_hot_rows(codes, count, values):
    picks = codes[None, :] == jnp.arange(1, count + 1, dtype=jnp.int32)[:, None]
    return jnp.dot(picks.astype(values.dtype), values, preferred_element_type=jnp.float32)


def gathered_rows(table_rows, picks):
    chosen = picks.reshape(-1)[:, None] == jnp.arange(table_rows.shape[0], dtype=jnp.int32)
    values = jnp.dot(chosen.astype(table_rows.dtype), table_rows, preferred_element_type=jnp.float32)
    return values.astype(table_rows.dtype).reshape(picks.shape + table_rows.shape[1:])


CODE_SPLIT = 64
CODE_ROWS = 16


def with_codes(values, codes):
    depth, width = values.shape[1], values.shape[2]
    halves = jnp.concatenate([codes // CODE_SPLIT, codes % CODE_SPLIT], axis=1)
    code_rows = halves.reshape(values.shape[0], -1, width).astype(values.dtype)
    pad = jnp.zeros((values.shape[0], CODE_ROWS - code_rows.shape[1], width), values.dtype)
    return jnp.concatenate([values, code_rows, pad], axis=1)


def split_codes(payload, depth):
    width = payload.shape[2]
    used = 2 * depth // width
    halves = payload[:, depth : depth + used].reshape(payload.shape[0], 2 * depth)
    halves = halves.astype(jnp.int32)
    codes = halves[:, :depth] * CODE_SPLIT + halves[:, depth:]
    return payload[:, :depth].reshape(-1, width), codes.reshape(-1)


def sent_block(kappa, lists, slots, counts):
    depth = lists.shape[1]
    live = jnp.arange(depth, dtype=jnp.int32)[None, :] < counts[:, None]
    codes = jnp.where(live, slots + 1, 0)
    return with_codes(gathered_rows(kappa, lists), codes)


def row_blend(own, above, below, top_weight, bottom_weight, width):
    count = own.shape[1]
    top = top_weight * own[:, :width] + (1.0 - top_weight) * above
    bottom = bottom_weight * own[:, count - width :] + (1.0 - bottom_weight) * below
    return jnp.concatenate([top, own[:, width : count - width], bottom], axis=1)


def on_device(kappa, send_list, dest_slot, send_count):
    tile_width = kappa.shape[1]
    rows_axis = lax.axis_size("px")
    cols_axis = lax.axis_size("py")
    band_index = lax.axis_index("px")
    column_index = lax.axis_index("py")
    slot_depth = send_list.shape[2]
    upper_band = jnp.maximum(band_index - 1, 0)
    band_rows = lambda table, band: lax.dynamic_slice_in_dim(table[0], band * cols_axis, cols_axis)
    upper_counts = jnp.where(band_index > 0, band_rows(send_count, upper_band), 0)
    same_sent = sent_block(
        kappa,
        band_rows(send_list, band_index),
        band_rows(dest_slot, band_index),
        band_rows(send_count, band_index),
    )
    rise_sent = sent_block(
        kappa, band_rows(send_list, upper_band), band_rows(dest_slot, upper_band), upper_counts
    )
    arrived = lax.all_to_all(jnp.stack([same_sent, rise_sent], axis=1), "py", 0, 0, tiled=True)
    same_values, same_codes = split_codes(arrived[:, 0], slot_depth)
    rise_values, rise_codes = split_codes(arrived[:, 1], slot_depth)
    rise_total = PATCH_ROWS * PATCH_COLS // tile_width // 4
    rise_live = rise_codes > 0
    rise_place = jnp.where(rise_live, jnp.cumsum(rise_live.astype(jnp.int32)), 0)
    packed_values = one_hot_rows(rise_place, rise_total, rise_values).astype(kappa.dtype)
    packed_picks = rise_place[None, :] == jnp.arange(1, rise_total + 1, dtype=jnp.int32)[:, None]
    packed_codes = jnp.sum(jnp.where(packed_picks, rise_codes[None, :], 0), axis=1)
    packed = with_codes(packed_values.reshape(1, rise_total, tile_width), packed_codes[None])
    raised_values, raised_codes = split_codes(shifted(packed, "px", -1), rise_total)
    slot_total = PATCH_ROWS * PATCH_COLS // tile_width
    patch_tiles = (
        one_hot_rows(same_codes, slot_total, same_values)
        + one_hot_rows(raised_codes, slot_total, raised_values)
    ).astype(kappa.dtype)
    edge_fields, fields = flexion_fields(patch_tiles.reshape(PATCH_ROWS, PATCH_COLS))
    width = tile_width
    last = PATCH_ROWS - width
    left = shifted(edge_fields[:, :, width:], "py", 1)
    right = shifted(edge_fields[:, :, :width], "py", -1)
    above = shifted(fields[:, last:], "px", 1)
    below = shifted(fields[:, :width], "px", -1)
    corners_above = shifted(
        jnp.concatenate([left[:, last:], right[:, last:]], axis=2), "px", 1
    )
    corners_below = shifted(
        jnp.concatenate([left[:, :width], right[:, :width]], axis=2), "px", -1
    )
    above_left, above_right = corners_above[:, :, :width], corners_above[:, :, width:]
    below_left, below_right = corners_below[:, :, :width], corners_below[:, :, width:]
    ramp = (jnp.arange(width, dtype=jnp.float32) + 0.5) / width
    top_weight = jnp.where(band_index > 0, ramp, 1.0)[None, :, None]
    bottom_weight = jnp.where(band_index < rows_axis - 1, ramp[::-1], 1.0)[None, :, None]
    left_weight = jnp.where(column_index > 0, ramp, 1.0)[None, None, :]
    right_weight = jnp.where(column_index < cols_axis - 1, ramp[::-1], 1.0)[None, None, :]
    f32 = lambda x: x.astype(jnp.float32)
    count = fields.shape[1]
    ones = jnp.ones((count - 2 * width,), jnp.float32)
    row_weight = jnp.concatenate([top_weight[0, :, 0], ones, bottom_weight[0, :, 0]])[:, None]
    col_weight = jnp.concatenate([left_weight[0, 0], ones, right_weight[0, 0]])[None, :]
    zero_rows = jnp.zeros((fields.shape[0], count - 2 * width, 1), jnp.float32)
    vertical = jnp.concatenate(
        [f32(above), jnp.broadcast_to(zero_rows, (fields.shape[0], count - 2 * width, count)),
         f32(below)], axis=1
    )
    rows_done = row_weight * f32(fields) + (1.0 - row_weight) * vertical
    side = lambda strip, upper, lower: row_weight * f32(strip) + (1.0 - row_weight) * jnp.concatenate(
        [f32(upper), jnp.broadcast_to(zero_rows, (fields.shape[0], count - 2 * width, width)),
         f32(lower)], axis=1
    )
    left_rows = side(left, above_left, below_left)
    right_rows = side(right, above_right, below_right)
    horizontal = jnp.concatenate(
        [left_rows, jnp.broadcast_to(zero_rows[:, :1], (fields.shape[0], count, count - 2 * width)),
         right_rows], axis=2
    )
    return col_weight * rows_done + (1.0 - col_weight) * horizontal


def solution(mesh):
    placed = (
        P(("px", "py"), None),
        P(("px", "py"), None, None),
        P(("px", "py"), None, None),
        P(("px", "py"), None),
    )
    return jax.shard_map(
        on_device, mesh=mesh, in_specs=placed, out_specs=P(None, "px", "py"), check_vma=False
    )
```

```python
import math

import jax
import ml_dtypes
import numpy as np
import jax.numpy as jnp
from jax import lax
from jax.sharding import PartitionSpec as P

PATCH_ROWS = 512
PATCH_COLS = 512


def shifted(shard, axis, by):
    size = lax.axis_size(axis)
    pairs = [(i, i + by) for i in range(size) if 0 <= i + by < size]
    return lax.ppermute(shard, axis, pairs)


def padded(block, sides, width):
    for axis, dim in sides:
        count = lax.axis_size(axis)
        forward = [(i, i + 1) for i in range(count - 1)]
        backward = [(target, source) for source, target in forward]
        low = lax.ppermute(
            lax.slice_in_dim(block, block.shape[dim] - width, None, axis=dim), axis, forward
        )
        high = lax.ppermute(lax.slice_in_dim(block, 0, width, axis=dim), axis, backward)
        block = jnp.concatenate([low, block, high], axis=dim)
    return block


def dft_tables(length):
    positions = np.arange(length, dtype=np.int64)
    phases = positions[:, None] * positions[None, :] % length
    angles = phases.astype(np.float32) * np.float32(2.0 * math.pi / length)
    return (np.cos(angles).astype(np.float32), np.sin(angles).astype(np.float32))


def table(values):
    return jnp.asarray(values.astype(ml_dtypes.bfloat16))


def wavenumbers(length):
    positions = jnp.arange(length, dtype=jnp.int32)
    signed = positions - length * (positions >= (length + 1) // 2).astype(jnp.int32)
    return signed.astype(jnp.float32) * (2.0 / length)


def dot32(a, b):
    return jnp.dot(a, b, preferred_element_type=jnp.float32)


def flexion_fields(pixels):
    row_count = pixels.shape[0]
    col_count = pixels.shape[1]
    assert row_count == col_count
    cos_np, sin_np = dft_tables(row_count)
    cosine, sine = table(cos_np), table(sin_np)
    n = row_count
    halves = jnp.concatenate([dot32(pixels, cosine), dot32(pixels, sine)], axis=1).astype(
        jnp.bfloat16
    )
    by_cos = dot32(cosine, halves)
    by_sin = dot32(sine, halves)
    real_part = by_cos[:, :n] - by_sin[:, n:]
    imag_part = -(by_sin[:, :n] + by_cos[:, n:])
    across = wavenumbers(col_count)[None, :]
    down = wavenumbers(row_count)[:, None]
    scale = 1.0 / (row_count * col_count)
    power = across * across + down * down
    safe_power = jnp.where(power > 0, power, 1.0)
    cube_real = across * across * across - 3.0 * across * down * down
    cube_imag = 3.0 * across * across * down - down * down * down
    one_real = (-down * real_part - across * imag_part) * scale
    one_imag = (across * real_part - down * imag_part) * scale
    kernel_real = -cube_imag / safe_power
    kernel_imag = cube_real / safe_power
    three_real = (kernel_real * real_part - kernel_imag * imag_part) * scale
    three_imag = (kernel_real * imag_part + kernel_imag * real_part) * scale
    spectra = jnp.concatenate([one_real, three_real, one_imag, three_imag], axis=1).astype(
        jnp.bfloat16
    )
    by_cos = dot32(cosine, spectra)
    by_sin = dot32(sine, spectra)
    columns_done = jnp.concatenate(
        [
            by_cos[:, : 2 * n] - by_sin[:, 2 * n :],
            by_sin[:, : 2 * n] + by_cos[:, 2 * n :],
        ],
        axis=1,
    ).astype(jnp.bfloat16)
    arranged = jnp.concatenate(
        [columns_done[:, k * n : (k + 1) * n] for k in range(4)], axis=0
    )
    width = n // 4
    edge_cols = jnp.concatenate(
        [cosine[:, :width], cosine[:, n - width :], sine[:, :width], sine[:, n - width :]], axis=1
    )
    edge = dot32(arranged, edge_cols)
    edge_cos, edge_sin = edge[:, : 2 * width], edge[:, 2 * width :]
    edge_fields = jnp.stack(
        [
            edge_cos[:n] - edge_sin[2 * n : 3 * n],
            edge_sin[:n] + edge_cos[2 * n : 3 * n],
            edge_cos[n : 2 * n] - edge_sin[3 * n :],
            edge_sin[n : 2 * n] + edge_cos[3 * n :],
        ]
    ).astype(jnp.bfloat16)
    by_cos = dot32(arranged, cosine)
    by_sin = dot32(arranged, sine)
    return edge_fields, jnp.stack(
        [
            by_cos[:n] - by_sin[2 * n : 3 * n],
            by_sin[:n] + by_cos[2 * n : 3 * n],
            by_cos[n : 2 * n] - by_sin[3 * n :],
            by_sin[n : 2 * n] + by_cos[3 * n :],
        ]
    ).astype(jnp.bfloat16)


def blend_edges(extended, has_top, has_bottom, has_left, has_right, width):
    values = extended.astype(jnp.float32)
    row_count = values.shape[1] - 2 * width
    col_count = values.shape[2] - 2 * width
    ramp = (jnp.arange(width, dtype=jnp.float32) + 0.5) / width
    top_weight = jnp.where(has_top, ramp, 1.0)[None, :, None]
    bottom_weight = jnp.where(has_bottom, ramp[::-1], 1.0)[None, :, None]
    middle = values[:, width : width + row_count, :]
    top_band = top_weight * middle[:, :width] + (1.0 - top_weight) * values[:, :width]
    bottom_band = (
        bottom_weight * middle[:, row_count - width :]
        + (1.0 - bottom_weight) * values[:, row_count + width :]
    )
    middle = jnp.concatenate([top_band, middle[:, width : row_count - width], bottom_band], axis=1)
    left_weight = jnp.where(has_left, ramp, 1.0)[None, None, :]
    right_weight = jnp.where(has_right, ramp[::-1], 1.0)[None, None, :]
    inner = middle[:, :, width : width + col_count]
    left_band = left_weight * inner[:, :, :width] + (1.0 - left_weight) * middle[:, :, :width]
    right_band = (
        right_weight * inner[:, :, col_count - width :]
        + (1.0 - right_weight) * middle[:, :, col_count + width :]
    )
    return jnp.concatenate([left_band, inner[:, :, width : col_count - width], right_band], axis=2)


def one_hot_rows(codes, count, values):
    picks = codes[None, :] == jnp.arange(1, count + 1, dtype=jnp.int32)[:, None]
    return jnp.dot(picks.astype(values.dtype), values, preferred_element_type=jnp.float32)


def gathered_rows(table_rows, picks):
    chosen = picks.reshape(-1)[:, None] == jnp.arange(table_rows.shape[0], dtype=jnp.int32)
    values = jnp.dot(chosen.astype(table_rows.dtype), table_rows, preferred_element_type=jnp.float32)
    return values.astype(table_rows.dtype).reshape(picks.shape + table_rows.shape[1:])


CODE_SPLIT = 64
CODE_ROWS = 16


def with_codes(values, codes):
    depth, width = values.shape[1], values.shape[2]
    halves = jnp.concatenate([codes // CODE_SPLIT, codes % CODE_SPLIT], axis=1)
    code_rows = halves.reshape(values.shape[0], -1, width).astype(values.dtype)
    pad = jnp.zeros((values.shape[0], CODE_ROWS - code_rows.shape[1], width), values.dtype)
    return jnp.concatenate([values, code_rows, pad], axis=1)


def split_codes(payload, depth):
    width = payload.shape[2]
    used = 2 * depth // width
    halves = payload[:, depth : depth + used].reshape(payload.shape[0], 2 * depth)
    halves = halves.astype(jnp.int32)
    codes = halves[:, :depth] * CODE_SPLIT + halves[:, depth:]
    return payload[:, :depth].reshape(-1, width), codes.reshape(-1)


def sent_block(kappa, lists, slots, counts):
    depth = lists.shape[1]
    live = jnp.arange(depth, dtype=jnp.int32)[None, :] < counts[:, None]
    codes = jnp.where(live, slots + 1, 0)
    return with_codes(gathered_rows(kappa, lists), codes)


def row_blend(own, above, below, top_weight, bottom_weight, width):
    count = own.shape[1]
    top = top_weight * own[:, :width] + (1.0 - top_weight) * above
    bottom = bottom_weight * own[:, count - width :] + (1.0 - bottom_weight) * below
    return jnp.concatenate([top, own[:, width : count - width], bottom], axis=1)


def on_device(kappa, send_list, dest_slot, send_count):
    tile_width = kappa.shape[1]
    rows_axis = lax.axis_size("px")
    cols_axis = lax.axis_size("py")
    band_index = lax.axis_index("px")
    column_index = lax.axis_index("py")
    slot_depth = send_list.shape[2]
    upper_band = jnp.maximum(band_index - 1, 0)
    band_rows = lambda table, band: lax.dynamic_slice_in_dim(table[0], band * cols_axis, cols_axis)
    upper_counts = jnp.where(band_index > 0, band_rows(send_count, upper_band), 0)
    same_sent = sent_block(
        kappa,
        band_rows(send_list, band_index),
        band_rows(dest_slot, band_index),
        band_rows(send_count, band_index),
    )
    rise_sent = sent_block(
        kappa, band_rows(send_list, upper_band), band_rows(dest_slot, upper_band), upper_counts
    )
    arrived = lax.all_to_all(jnp.stack([same_sent, rise_sent], axis=1), "py", 0, 0, tiled=True)
    same_values, same_codes = split_codes(arrived[:, 0], slot_depth)
    rise_values, rise_codes = split_codes(arrived[:, 1], slot_depth)
    rise_total = PATCH_ROWS * PATCH_COLS // tile_width // 4
    rise_live = rise_codes > 0
    rise_place = jnp.where(rise_live, jnp.cumsum(rise_live.astype(jnp.int32)), 0)
    packed_values = one_hot_rows(rise_place, rise_total, rise_values).astype(kappa.dtype)
    packed_picks = rise_place[None, :] == jnp.arange(1, rise_total + 1, dtype=jnp.int32)[:, None]
    packed_codes = jnp.sum(jnp.where(packed_picks, rise_codes[None, :], 0), axis=1)
    packed = with_codes(packed_values.reshape(1, rise_total, tile_width), packed_codes[None])
    raised_values, raised_codes = split_codes(shifted(packed, "px", -1), rise_total)
    slot_total = PATCH_ROWS * PATCH_COLS // tile_width
    patch_tiles = (
        one_hot_rows(same_codes, slot_total, same_values)
        + one_hot_rows(raised_codes, slot_total, raised_values)
    ).astype(kappa.dtype)
    edge_fields, fields = flexion_fields(patch_tiles.reshape(PATCH_ROWS, PATCH_COLS))
    width = tile_width
    last = PATCH_ROWS - width
    left = shifted(edge_fields[:, :, width:], "py", 1)
    right = shifted(edge_fields[:, :, :width], "py", -1)
    above = shifted(fields[:, last:], "px", 1)
    below = shifted(fields[:, :width], "px", -1)
    corners_above = shifted(
        jnp.concatenate([left[:, last:], right[:, last:]], axis=2), "px", 1
    )
    corners_below = shifted(
        jnp.concatenate([left[:, :width], right[:, :width]], axis=2), "px", -1
    )
    above_left, above_right = corners_above[:, :, :width], corners_above[:, :, width:]
    below_left, below_right = corners_below[:, :, :width], corners_below[:, :, width:]
    ramp = (jnp.arange(width, dtype=jnp.float32) + 0.5) / width
    top_weight = jnp.where(band_index > 0, ramp, 1.0)[None, :, None]
    bottom_weight = jnp.where(band_index < rows_axis - 1, ramp[::-1], 1.0)[None, :, None]
    left_weight = jnp.where(column_index > 0, ramp, 1.0)[None, None, :]
    right_weight = jnp.where(column_index < cols_axis - 1, ramp[::-1], 1.0)[None, None, :]
    f32 = lambda x: x.astype(jnp.float32)
    count = fields.shape[1]
    ones = jnp.ones((count - 2 * width,), jnp.float32)
    row_weight = jnp.concatenate([top_weight[0, :, 0], ones, bottom_weight[0, :, 0]])[:, None]
    col_weight = jnp.concatenate([left_weight[0, 0], ones, right_weight[0, 0]])[None, :]
    zero_rows = jnp.zeros((fields.shape[0], count - 2 * width, 1), jnp.float32)
    vertical = jnp.concatenate(
        [f32(above), jnp.broadcast_to(zero_rows, (fields.shape[0], count - 2 * width, count)),
         f32(below)], axis=1
    )
    rows_done = row_weight * f32(fields) + (1.0 - row_weight) * vertical
    side = lambda strip, upper, lower: row_weight * f32(strip) + (1.0 - row_weight) * jnp.concatenate(
        [f32(upper), jnp.broadcast_to(zero_rows, (fields.shape[0], count - 2 * width, width)),
         f32(lower)], axis=1
    )
    no_corner = jnp.zeros_like(f32(above_left))
    left_rows = side(left, no_corner, no_corner)
    right_rows = side(right, no_corner, no_corner)
    horizontal = jnp.concatenate(
        [left_rows, jnp.broadcast_to(zero_rows[:, :1], (fields.shape[0], count, count - 2 * width)),
         right_rows], axis=2
    )
    result = col_weight * rows_done + (1.0 - col_weight) * horizontal
    last = count - width
    for rows, row_w, vert, pieces in (
        (slice(0, width), top_weight[0], above, ((left, above_left), (right, above_right))),
        (slice(last, count), bottom_weight[0], below, ((left, below_left), (right, below_right))),
    ):
        for (strip, corner), cols, col_w in zip(
            pieces, (slice(0, width), slice(last, count)), (left_weight[0], right_weight[0])
        ):
            own_rows = row_w * f32(fields[:, rows, cols]) + (1.0 - row_w) * f32(vert[:, :, cols])
            strip_rows = row_w * f32(strip[:, rows]) + (1.0 - row_w) * f32(corner)
            result = result.at[:, rows, cols].set(col_w * own_rows + (1.0 - col_w) * strip_rows)
    return result


def solution(mesh):
    placed = (
        P(("px", "py"), None),
        P(("px", "py"), None, None),
        P(("px", "py"), None, None),
        P(("px", "py"), None),
    )
    return jax.shard_map(
        on_device, mesh=mesh, in_specs=placed, out_specs=P(None, "px", "py"), check_vma=False
    )
```

```python
import math

import jax
import ml_dtypes
import numpy as np
import jax.numpy as jnp
from jax import lax
from jax.sharding import PartitionSpec as P

PATCH_ROWS = 512
PATCH_COLS = 512


def shifted(shard, axis, by):
    size = lax.axis_size(axis)
    pairs = [(i, i + by) for i in range(size) if 0 <= i + by < size]
    return lax.ppermute(shard, axis, pairs)


def padded(block, sides, width):
    for axis, dim in sides:
        count = lax.axis_size(axis)
        forward = [(i, i + 1) for i in range(count - 1)]
        backward = [(target, source) for source, target in forward]
        low = lax.ppermute(
            lax.slice_in_dim(block, block.shape[dim] - width, None, axis=dim), axis, forward
        )
        high = lax.ppermute(lax.slice_in_dim(block, 0, width, axis=dim), axis, backward)
        block = jnp.concatenate([low, block, high], axis=dim)
    return block


def dft_tables(length):
    positions = np.arange(length, dtype=np.int64)
    phases = positions[:, None] * positions[None, :] % length
    angles = phases.astype(np.float32) * np.float32(2.0 * math.pi / length)
    return (np.cos(angles).astype(np.float32), np.sin(angles).astype(np.float32))


def table(values):
    return jnp.asarray(values.astype(ml_dtypes.bfloat16))


def wavenumbers(length):
    positions = jnp.arange(length, dtype=jnp.int32)
    signed = positions - length * (positions >= (length + 1) // 2).astype(jnp.int32)
    return signed.astype(jnp.float32) * (2.0 / length)


def dot32(a, b):
    return jnp.dot(a, b, preferred_element_type=jnp.float32)


def flexion_fields(pixels):
    row_count = pixels.shape[0]
    col_count = pixels.shape[1]
    assert row_count == col_count
    cos_np, sin_np = dft_tables(row_count)
    cosine, sine = table(cos_np), table(sin_np)
    n = row_count
    halves = jnp.concatenate([dot32(pixels, cosine), dot32(pixels, sine)], axis=1).astype(
        jnp.bfloat16
    )
    by_cos = dot32(cosine, halves)
    by_sin = dot32(sine, halves)
    real_part = by_cos[:, :n] - by_sin[:, n:]
    imag_part = -(by_sin[:, :n] + by_cos[:, n:])
    across = wavenumbers(col_count)[None, :]
    down = wavenumbers(row_count)[:, None]
    scale = 1.0 / (row_count * col_count)
    power = across * across + down * down
    safe_power = jnp.where(power > 0, power, 1.0)
    cube_real = across * across * across - 3.0 * across * down * down
    cube_imag = 3.0 * across * across * down - down * down * down
    one_real = (-down * real_part - across * imag_part) * scale
    one_imag = (across * real_part - down * imag_part) * scale
    kernel_real = -cube_imag / safe_power
    kernel_imag = cube_real / safe_power
    three_real = (kernel_real * real_part - kernel_imag * imag_part) * scale
    three_imag = (kernel_real * imag_part + kernel_imag * real_part) * scale
    spectra = jnp.concatenate([one_real, three_real, one_imag, three_imag], axis=1).astype(
        jnp.bfloat16
    )
    by_cos = dot32(cosine, spectra)
    by_sin = dot32(sine, spectra)
    columns_done = jnp.concatenate(
        [
            by_cos[:, : 2 * n] - by_sin[:, 2 * n :],
            by_sin[:, : 2 * n] + by_cos[:, 2 * n :],
        ],
        axis=1,
    ).astype(jnp.bfloat16)
    arranged = jnp.concatenate(
        [columns_done[:, k * n : (k + 1) * n] for k in range(4)], axis=0
    )
    width = n // 4
    edge_cols = jnp.concatenate(
        [cosine[:, :width], cosine[:, n - width :], sine[:, :width], sine[:, n - width :]], axis=1
    )
    edge = dot32(arranged, edge_cols)
    edge_cos, edge_sin = edge[:, : 2 * width], edge[:, 2 * width :]
    edge_fields = jnp.stack(
        [
            edge_cos[:n] - edge_sin[2 * n : 3 * n],
            edge_sin[:n] + edge_cos[2 * n : 3 * n],
            edge_cos[n : 2 * n] - edge_sin[3 * n :],
            edge_sin[n : 2 * n] + edge_cos[3 * n :],
        ]
    ).astype(jnp.bfloat16)
    by_cos = dot32(arranged, cosine)
    by_sin = dot32(arranged, sine)
    return edge_fields, jnp.stack(
        [
            by_cos[:n] - by_sin[2 * n : 3 * n],
            by_sin[:n] + by_cos[2 * n : 3 * n],
            by_cos[n : 2 * n] - by_sin[3 * n :],
            by_sin[n : 2 * n] + by_cos[3 * n :],
        ]
    ).astype(jnp.bfloat16)


def blend_edges(extended, has_top, has_bottom, has_left, has_right, width):
    values = extended.astype(jnp.float32)
    row_count = values.shape[1] - 2 * width
    col_count = values.shape[2] - 2 * width
    ramp = (jnp.arange(width, dtype=jnp.float32) + 0.5) / width
    top_weight = jnp.where(has_top, ramp, 1.0)[None, :, None]
    bottom_weight = jnp.where(has_bottom, ramp[::-1], 1.0)[None, :, None]
    middle = values[:, width : width + row_count, :]
    top_band = top_weight * middle[:, :width] + (1.0 - top_weight) * values[:, :width]
    bottom_band = (
        bottom_weight * middle[:, row_count - width :]
        + (1.0 - bottom_weight) * values[:, row_count + width :]
    )
    middle = jnp.concatenate([top_band, middle[:, width : row_count - width], bottom_band], axis=1)
    left_weight = jnp.where(has_left, ramp, 1.0)[None, None, :]
    right_weight = jnp.where(has_right, ramp[::-1], 1.0)[None, None, :]
    inner = middle[:, :, width : width + col_count]
    left_band = left_weight * inner[:, :, :width] + (1.0 - left_weight) * middle[:, :, :width]
    right_band = (
        right_weight * inner[:, :, col_count - width :]
        + (1.0 - right_weight) * middle[:, :, col_count + width :]
    )
    return jnp.concatenate([left_band, inner[:, :, width : col_count - width], right_band], axis=2)


def one_hot_rows(codes, count, values):
    picks = codes[None, :] == jnp.arange(1, count + 1, dtype=jnp.int32)[:, None]
    return jnp.dot(picks.astype(values.dtype), values, preferred_element_type=jnp.float32)


def gathered_rows(table_rows, picks):
    rows, width = table_rows.shape
    paired = table_rows.reshape(rows // 2, 2 * width)
    flat = picks.reshape(-1)
    chosen = (flat // 2)[:, None] == jnp.arange(rows // 2, dtype=jnp.int32)
    both = jnp.dot(chosen.astype(table_rows.dtype), paired, preferred_element_type=jnp.float32)
    both = both.astype(table_rows.dtype)
    values = jnp.where((flat % 2 == 0)[:, None], both[:, :width], both[:, width:])
    return values.reshape(picks.shape + (width,))


CODE_SPLIT = 64
CODE_ROWS = 16


def with_codes(values, codes):
    depth, width = values.shape[1], values.shape[2]
    halves = jnp.concatenate([codes // CODE_SPLIT, codes % CODE_SPLIT], axis=1)
    code_rows = halves.reshape(values.shape[0], -1, width).astype(values.dtype)
    pad = jnp.zeros((values.shape[0], CODE_ROWS - code_rows.shape[1], width), values.dtype)
    return jnp.concatenate([values, code_rows, pad], axis=1)


def split_codes(payload, depth):
    width = payload.shape[2]
    used = 2 * depth // width
    halves = payload[:, depth : depth + used].reshape(payload.shape[0], 2 * depth)
    halves = halves.astype(jnp.int32)
    codes = halves[:, :depth] * CODE_SPLIT + halves[:, depth:]
    return payload[:, :depth].reshape(-1, width), codes.reshape(-1)


def sent_block(kappa, lists, slots, counts):
    depth = lists.shape[1]
    live = jnp.arange(depth, dtype=jnp.int32)[None, :] < counts[:, None]
    codes = jnp.where(live, slots + 1, 0)
    return with_codes(gathered_rows(kappa, lists), codes)


def row_blend(own, above, below, top_weight, bottom_weight, width):
    count = own.shape[1]
    top = top_weight * own[:, :width] + (1.0 - top_weight) * above
    bottom = bottom_weight * own[:, count - width :] + (1.0 - bottom_weight) * below
    return jnp.concatenate([top, own[:, width : count - width], bottom], axis=1)


def on_device(kappa, send_list, dest_slot, send_count):
    tile_width = kappa.shape[1]
    rows_axis = lax.axis_size("px")
    cols_axis = lax.axis_size("py")
    band_index = lax.axis_index("px")
    column_index = lax.axis_index("py")
    slot_depth = send_list.shape[2]
    upper_band = jnp.maximum(band_index - 1, 0)
    band_rows = lambda table, band: lax.dynamic_slice_in_dim(table[0], band * cols_axis, cols_axis)
    upper_counts = jnp.where(band_index > 0, band_rows(send_count, upper_band), 0)
    same_sent = sent_block(
        kappa,
        band_rows(send_list, band_index),
        band_rows(dest_slot, band_index),
        band_rows(send_count, band_index),
    )
    rise_sent = sent_block(
        kappa, band_rows(send_list, upper_band), band_rows(dest_slot, upper_band), upper_counts
    )
    arrived = lax.all_to_all(jnp.stack([same_sent, rise_sent], axis=1), "py", 0, 0, tiled=True)
    same_values, same_codes = split_codes(arrived[:, 0], slot_depth)
    rise_values, rise_codes = split_codes(arrived[:, 1], slot_depth)
    rise_total = PATCH_ROWS * PATCH_COLS // tile_width // 4
    rise_live = rise_codes > 0
    rise_place = jnp.where(rise_live, jnp.cumsum(rise_live.astype(jnp.int32)), 0)
    packed_values = one_hot_rows(rise_place, rise_total, rise_values).astype(kappa.dtype)
    packed_picks = rise_place[None, :] == jnp.arange(1, rise_total + 1, dtype=jnp.int32)[:, None]
    packed_codes = jnp.sum(jnp.where(packed_picks, rise_codes[None, :], 0), axis=1)
    packed = with_codes(packed_values.reshape(1, rise_total, tile_width), packed_codes[None])
    raised_values, raised_codes = split_codes(shifted(packed, "px", -1), rise_total)
    slot_total = PATCH_ROWS * PATCH_COLS // tile_width
    patch_tiles = (
        one_hot_rows(same_codes, slot_total, same_values)
        + one_hot_rows(raised_codes, slot_total, raised_values)
    ).astype(kappa.dtype)
    edge_fields, fields = flexion_fields(patch_tiles.reshape(PATCH_ROWS, PATCH_COLS))
    width = tile_width
    last = PATCH_ROWS - width
    left = shifted(edge_fields[:, :, width:], "py", 1)
    right = shifted(edge_fields[:, :, :width], "py", -1)
    above = shifted(fields[:, last:], "px", 1)
    below = shifted(fields[:, :width], "px", -1)
    corners_above = shifted(
        jnp.concatenate([left[:, last:], right[:, last:]], axis=2), "px", 1
    )
    corners_below = shifted(
        jnp.concatenate([left[:, :width], right[:, :width]], axis=2), "px", -1
    )
    above_left, above_right = corners_above[:, :, :width], corners_above[:, :, width:]
    below_left, below_right = corners_below[:, :, :width], corners_below[:, :, width:]
    ramp = (jnp.arange(width, dtype=jnp.float32) + 0.5) / width
    top_weight = jnp.where(band_index > 0, ramp, 1.0)[None, :, None]
    bottom_weight = jnp.where(band_index < rows_axis - 1, ramp[::-1], 1.0)[None, :, None]
    left_weight = jnp.where(column_index > 0, ramp, 1.0)[None, None, :]
    right_weight = jnp.where(column_index < cols_axis - 1, ramp[::-1], 1.0)[None, None, :]
    f32 = lambda x: x.astype(jnp.float32)
    count = fields.shape[1]
    ones = jnp.ones((count - 2 * width,), jnp.float32)
    row_weight = jnp.concatenate([top_weight[0, :, 0], ones, bottom_weight[0, :, 0]])[:, None]
    col_weight = jnp.concatenate([left_weight[0, 0], ones, right_weight[0, 0]])[None, :]
    zero_rows = jnp.zeros((fields.shape[0], count - 2 * width, 1), jnp.float32)
    vertical = jnp.concatenate(
        [f32(above), jnp.broadcast_to(zero_rows, (fields.shape[0], count - 2 * width, count)),
         f32(below)], axis=1
    )
    rows_done = row_weight * f32(fields) + (1.0 - row_weight) * vertical
    side = lambda strip, upper, lower: row_weight * f32(strip) + (1.0 - row_weight) * jnp.concatenate(
        [f32(upper), jnp.broadcast_to(zero_rows, (fields.shape[0], count - 2 * width, width)),
         f32(lower)], axis=1
    )
    left_rows = side(left, above_left, below_left)
    right_rows = side(right, above_right, below_right)
    horizontal = jnp.concatenate(
        [left_rows, jnp.broadcast_to(zero_rows[:, :1], (fields.shape[0], count, count - 2 * width)),
         right_rows], axis=2
    )
    return col_weight * rows_done + (1.0 - col_weight) * horizontal


def solution(mesh):
    placed = (
        P(("px", "py"), None),
        P(("px", "py"), None, None),
        P(("px", "py"), None, None),
        P(("px", "py"), None),
    )
    return jax.shard_map(
        on_device, mesh=mesh, in_specs=placed, out_specs=P(None, "px", "py"), check_vma=False
    )
```

```python
import math

import jax
import ml_dtypes
import numpy as np
import jax.numpy as jnp
from jax import lax
from jax.sharding import PartitionSpec as P

PATCH_ROWS = 512
PATCH_COLS = 512


def shifted(shard, axis, by):
    size = lax.axis_size(axis)
    pairs = [(i, i + by) for i in range(size) if 0 <= i + by < size]
    return lax.ppermute(shard, axis, pairs)


def padded(block, sides, width):
    for axis, dim in sides:
        count = lax.axis_size(axis)
        forward = [(i, i + 1) for i in range(count - 1)]
        backward = [(target, source) for source, target in forward]
        low = lax.ppermute(
            lax.slice_in_dim(block, block.shape[dim] - width, None, axis=dim), axis, forward
        )
        high = lax.ppermute(lax.slice_in_dim(block, 0, width, axis=dim), axis, backward)
        block = jnp.concatenate([low, block, high], axis=dim)
    return block


def dft_tables(length):
    positions = np.arange(length, dtype=np.int64)
    phases = positions[:, None] * positions[None, :] % length
    angles = phases.astype(np.float32) * np.float32(2.0 * math.pi / length)
    return (np.cos(angles).astype(np.float32), np.sin(angles).astype(np.float32))


def table(values):
    return jnp.asarray(values.astype(ml_dtypes.bfloat16))


def wavenumbers(length):
    positions = jnp.arange(length, dtype=jnp.int32)
    signed = positions - length * (positions >= (length + 1) // 2).astype(jnp.int32)
    return signed.astype(jnp.float32) * (2.0 / length)


def dot32(a, b):
    return jnp.dot(a, b, preferred_element_type=jnp.float32)


def flexion_fields(pixels):
    row_count = pixels.shape[0]
    col_count = pixels.shape[1]
    assert row_count == col_count
    cos_np, sin_np = dft_tables(row_count)
    cosine, sine = table(cos_np), table(sin_np)
    n = row_count
    halves = jnp.concatenate([dot32(pixels, cosine), dot32(pixels, sine)], axis=1).astype(
        jnp.bfloat16
    )
    by_cos = dot32(cosine, halves)
    by_sin = dot32(sine, halves)
    real_part = by_cos[:, :n] - by_sin[:, n:]
    imag_part = -(by_sin[:, :n] + by_cos[:, n:])
    across = wavenumbers(col_count)[None, :]
    down = wavenumbers(row_count)[:, None]
    scale = 1.0 / (row_count * col_count)
    power = across * across + down * down
    safe_power = jnp.where(power > 0, power, 1.0)
    cube_real = across * across * across - 3.0 * across * down * down
    cube_imag = 3.0 * across * across * down - down * down * down
    one_real = (-down * real_part - across * imag_part) * scale
    one_imag = (across * real_part - down * imag_part) * scale
    kernel_real = -cube_imag / safe_power
    kernel_imag = cube_real / safe_power
    three_real = (kernel_real * real_part - kernel_imag * imag_part) * scale
    three_imag = (kernel_real * imag_part + kernel_imag * real_part) * scale
    spectra = jnp.concatenate([one_real, three_real, one_imag, three_imag], axis=1).astype(
        jnp.bfloat16
    )
    by_cos = dot32(cosine, spectra)
    by_sin = dot32(sine, spectra)
    columns_done = jnp.concatenate(
        [
            by_cos[:, : 2 * n] - by_sin[:, 2 * n :],
            by_sin[:, : 2 * n] + by_cos[:, 2 * n :],
        ],
        axis=1,
    ).astype(jnp.bfloat16)
    arranged = jnp.concatenate(
        [columns_done[:, k * n : (k + 1) * n] for k in range(4)], axis=0
    )
    width = n // 4
    edge_cols = jnp.concatenate(
        [cosine[:, :width], cosine[:, n - width :], sine[:, :width], sine[:, n - width :]], axis=1
    )
    edge = dot32(arranged, edge_cols)
    edge_cos, edge_sin = edge[:, : 2 * width], edge[:, 2 * width :]
    edge_fields = jnp.stack(
        [
            edge_cos[:n] - edge_sin[2 * n : 3 * n],
            edge_sin[:n] + edge_cos[2 * n : 3 * n],
            edge_cos[n : 2 * n] - edge_sin[3 * n :],
            edge_sin[n : 2 * n] + edge_cos[3 * n :],
        ]
    ).astype(jnp.bfloat16)
    by_cos = dot32(arranged, cosine)
    by_sin = dot32(arranged, sine)
    return edge_fields, jnp.stack(
        [
            by_cos[:n] - by_sin[2 * n : 3 * n],
            by_sin[:n] + by_cos[2 * n : 3 * n],
            by_cos[n : 2 * n] - by_sin[3 * n :],
            by_sin[n : 2 * n] + by_cos[3 * n :],
        ]
    ).astype(jnp.bfloat16)


def blend_edges(extended, has_top, has_bottom, has_left, has_right, width):
    values = extended.astype(jnp.float32)
    row_count = values.shape[1] - 2 * width
    col_count = values.shape[2] - 2 * width
    ramp = (jnp.arange(width, dtype=jnp.float32) + 0.5) / width
    top_weight = jnp.where(has_top, ramp, 1.0)[None, :, None]
    bottom_weight = jnp.where(has_bottom, ramp[::-1], 1.0)[None, :, None]
    middle = values[:, width : width + row_count, :]
    top_band = top_weight * middle[:, :width] + (1.0 - top_weight) * values[:, :width]
    bottom_band = (
        bottom_weight * middle[:, row_count - width :]
        + (1.0 - bottom_weight) * values[:, row_count + width :]
    )
    middle = jnp.concatenate([top_band, middle[:, width : row_count - width], bottom_band], axis=1)
    left_weight = jnp.where(has_left, ramp, 1.0)[None, None, :]
    right_weight = jnp.where(has_right, ramp[::-1], 1.0)[None, None, :]
    inner = middle[:, :, width : width + col_count]
    left_band = left_weight * inner[:, :, :width] + (1.0 - left_weight) * middle[:, :, :width]
    right_band = (
        right_weight * inner[:, :, col_count - width :]
        + (1.0 - right_weight) * middle[:, :, col_count + width :]
    )
    return jnp.concatenate([left_band, inner[:, :, width : col_count - width], right_band], axis=2)


def one_hot_rows(codes, count, values):
    picks = codes[None, :] == jnp.arange(1, count + 1, dtype=jnp.int32)[:, None]
    return jnp.dot(picks.astype(values.dtype), values, preferred_element_type=jnp.float32)


def placed_rows(codes, row_count, values):
    width = values.shape[1]
    per_row = PATCH_COLS // width
    slots = codes - 1
    quarter = slots % per_row
    spread = jnp.where(
        quarter[:, None, None] == jnp.arange(per_row, dtype=jnp.int32)[None, :, None],
        values[:, None, :],
        jnp.zeros((), values.dtype),
    ).reshape(values.shape[0], per_row * width)
    picks = (slots // per_row)[None, :] == jnp.arange(row_count, dtype=jnp.int32)[:, None]
    return jnp.dot(picks.astype(values.dtype), spread, preferred_element_type=jnp.float32)


def gathered_rows(table_rows, picks):
    chosen = picks.reshape(-1)[:, None] == jnp.arange(table_rows.shape[0], dtype=jnp.int32)
    values = jnp.dot(chosen.astype(table_rows.dtype), table_rows, preferred_element_type=jnp.float32)
    return values.astype(table_rows.dtype).reshape(picks.shape + table_rows.shape[1:])


CODE_SPLIT = 64
CODE_ROWS = 16


def with_codes(values, codes):
    depth, width = values.shape[1], values.shape[2]
    halves = jnp.concatenate([codes // CODE_SPLIT, codes % CODE_SPLIT], axis=1)
    code_rows = halves.reshape(values.shape[0], -1, width).astype(values.dtype)
    pad = jnp.zeros((values.shape[0], CODE_ROWS - code_rows.shape[1], width), values.dtype)
    return jnp.concatenate([values, code_rows, pad], axis=1)


def split_codes(payload, depth):
    width = payload.shape[2]
    used = 2 * depth // width
    halves = payload[:, depth : depth + used].reshape(payload.shape[0], 2 * depth)
    halves = halves.astype(jnp.int32)
    codes = halves[:, :depth] * CODE_SPLIT + halves[:, depth:]
    return payload[:, :depth].reshape(-1, width), codes.reshape(-1)


def sent_block(kappa, lists, slots, counts):
    depth = lists.shape[1]
    live = jnp.arange(depth, dtype=jnp.int32)[None, :] < counts[:, None]
    codes = jnp.where(live, slots + 1, 0)
    return with_codes(gathered_rows(kappa, lists), codes)


def row_blend(own, above, below, top_weight, bottom_weight, width):
    count = own.shape[1]
    top = top_weight * own[:, :width] + (1.0 - top_weight) * above
    bottom = bottom_weight * own[:, count - width :] + (1.0 - bottom_weight) * below
    return jnp.concatenate([top, own[:, width : count - width], bottom], axis=1)


def on_device(kappa, send_list, dest_slot, send_count):
    tile_width = kappa.shape[1]
    rows_axis = lax.axis_size("px")
    cols_axis = lax.axis_size("py")
    band_index = lax.axis_index("px")
    column_index = lax.axis_index("py")
    slot_depth = send_list.shape[2]
    upper_band = jnp.maximum(band_index - 1, 0)
    band_rows = lambda table, band: lax.dynamic_slice_in_dim(table[0], band * cols_axis, cols_axis)
    upper_counts = jnp.where(band_index > 0, band_rows(send_count, upper_band), 0)
    same_sent = sent_block(
        kappa,
        band_rows(send_list, band_index),
        band_rows(dest_slot, band_index),
        band_rows(send_count, band_index),
    )
    rise_sent = sent_block(
        kappa, band_rows(send_list, upper_band), band_rows(dest_slot, upper_band), upper_counts
    )
    arrived = lax.all_to_all(jnp.stack([same_sent, rise_sent], axis=1), "py", 0, 0, tiled=True)
    same_values, same_codes = split_codes(arrived[:, 0], slot_depth)
    rise_values, rise_codes = split_codes(arrived[:, 1], slot_depth)
    rise_total = PATCH_ROWS * PATCH_COLS // tile_width // 4
    rise_live = rise_codes > 0
    rise_place = jnp.where(rise_live, jnp.cumsum(rise_live.astype(jnp.int32)), 0)
    packed_values = one_hot_rows(rise_place, rise_total, rise_values).astype(kappa.dtype)
    packed_picks = rise_place[None, :] == jnp.arange(1, rise_total + 1, dtype=jnp.int32)[:, None]
    packed_codes = jnp.sum(jnp.where(packed_picks, rise_codes[None, :], 0), axis=1)
    packed = with_codes(packed_values.reshape(1, rise_total, tile_width), packed_codes[None])
    raised_values, raised_codes = split_codes(shifted(packed, "px", -1), rise_total)
    slot_total = PATCH_ROWS * PATCH_COLS // tile_width
    pixels = (
        placed_rows(same_codes, PATCH_ROWS, same_values)
        + placed_rows(raised_codes, PATCH_ROWS, raised_values)
    ).astype(kappa.dtype)
    edge_fields, fields = flexion_fields(pixels)
    width = tile_width
    last = PATCH_ROWS - width
    left = shifted(edge_fields[:, :, width:], "py", 1)
    right = shifted(edge_fields[:, :, :width], "py", -1)
    above = shifted(fields[:, last:], "px", 1)
    below = shifted(fields[:, :width], "px", -1)
    corners_above = shifted(
        jnp.concatenate([left[:, last:], right[:, last:]], axis=2), "px", 1
    )
    corners_below = shifted(
        jnp.concatenate([left[:, :width], right[:, :width]], axis=2), "px", -1
    )
    above_left, above_right = corners_above[:, :, :width], corners_above[:, :, width:]
    below_left, below_right = corners_below[:, :, :width], corners_below[:, :, width:]
    ramp = (jnp.arange(width, dtype=jnp.float32) + 0.5) / width
    top_weight = jnp.where(band_index > 0, ramp, 1.0)[None, :, None]
    bottom_weight = jnp.where(band_index < rows_axis - 1, ramp[::-1], 1.0)[None, :, None]
    left_weight = jnp.where(column_index > 0, ramp, 1.0)[None, None, :]
    right_weight = jnp.where(column_index < cols_axis - 1, ramp[::-1], 1.0)[None, None, :]
    f32 = lambda x: x.astype(jnp.float32)
    count = fields.shape[1]
    ones = jnp.ones((count - 2 * width,), jnp.float32)
    row_weight = jnp.concatenate([top_weight[0, :, 0], ones, bottom_weight[0, :, 0]])[:, None]
    col_weight = jnp.concatenate([left_weight[0, 0], ones, right_weight[0, 0]])[None, :]
    zero_rows = jnp.zeros((fields.shape[0], count - 2 * width, 1), jnp.float32)
    vertical = jnp.concatenate(
        [f32(above), jnp.broadcast_to(zero_rows, (fields.shape[0], count - 2 * width, count)),
         f32(below)], axis=1
    )
    rows_done = row_weight * f32(fields) + (1.0 - row_weight) * vertical
    side = lambda strip, upper, lower: row_weight * f32(strip) + (1.0 - row_weight) * jnp.concatenate(
        [f32(upper), jnp.broadcast_to(zero_rows, (fields.shape[0], count - 2 * width, width)),
         f32(lower)], axis=1
    )
    left_rows = side(left, above_left, below_left)
    right_rows = side(right, above_right, below_right)
    horizontal = jnp.concatenate(
        [left_rows, jnp.broadcast_to(zero_rows[:, :1], (fields.shape[0], count, count - 2 * width)),
         right_rows], axis=2
    )
    return col_weight * rows_done + (1.0 - col_weight) * horizontal


def solution(mesh):
    placed = (
        P(("px", "py"), None),
        P(("px", "py"), None, None),
        P(("px", "py"), None, None),
        P(("px", "py"), None),
    )
    return jax.shard_map(
        on_device, mesh=mesh, in_specs=placed, out_specs=P(None, "px", "py"), check_vma=False
    )
```

```python
import math

import jax
import ml_dtypes
import numpy as np
import jax.numpy as jnp
from jax import lax
from jax.sharding import PartitionSpec as P

PATCH_ROWS = 512
PATCH_COLS = 512


def shifted(shard, axis, by):
    size = lax.axis_size(axis)
    pairs = [(i, i + by) for i in range(size) if 0 <= i + by < size]
    return lax.ppermute(shard, axis, pairs)


def padded(block, sides, width):
    for axis, dim in sides:
        count = lax.axis_size(axis)
        forward = [(i, i + 1) for i in range(count - 1)]
        backward = [(target, source) for source, target in forward]
        low = lax.ppermute(
            lax.slice_in_dim(block, block.shape[dim] - width, None, axis=dim), axis, forward
        )
        high = lax.ppermute(lax.slice_in_dim(block, 0, width, axis=dim), axis, backward)
        block = jnp.concatenate([low, block, high], axis=dim)
    return block


def dft_tables(length):
    positions = np.arange(length, dtype=np.int64)
    phases = positions[:, None] * positions[None, :] % length
    angles = phases.astype(np.float32) * np.float32(2.0 * math.pi / length)
    return (np.cos(angles).astype(np.float32), np.sin(angles).astype(np.float32))


def table(values):
    return jnp.asarray(values.astype(ml_dtypes.bfloat16))


def wavenumbers(length):
    positions = jnp.arange(length, dtype=jnp.int32)
    signed = positions - length * (positions >= (length + 1) // 2).astype(jnp.int32)
    return signed.astype(jnp.float32) * (2.0 / length)


def dot32(a, b):
    return jnp.dot(a, b, preferred_element_type=jnp.float32)


def flexion_fields(pixels):
    row_count = pixels.shape[0]
    col_count = pixels.shape[1]
    assert row_count == col_count
    cos_np, sin_np = dft_tables(row_count)
    cosine, sine = table(cos_np), table(sin_np)
    n = row_count
    halves = jnp.concatenate([dot32(pixels, cosine), dot32(pixels, sine)], axis=1).astype(
        jnp.bfloat16
    )
    by_cos = dot32(cosine, halves)
    by_sin = dot32(sine, halves)
    real_part = by_cos[:, :n] - by_sin[:, n:]
    imag_part = -(by_sin[:, :n] + by_cos[:, n:])
    across = wavenumbers(col_count)[None, :]
    down = wavenumbers(row_count)[:, None]
    scale = 1.0 / (row_count * col_count)
    power = across * across + down * down
    safe_power = jnp.where(power > 0, power, 1.0)
    cube_real = across * across * across - 3.0 * across * down * down
    cube_imag = 3.0 * across * across * down - down * down * down
    one_real = (-down * real_part - across * imag_part) * scale
    one_imag = (across * real_part - down * imag_part) * scale
    kernel_real = -cube_imag / safe_power
    kernel_imag = cube_real / safe_power
    three_real = (kernel_real * real_part - kernel_imag * imag_part) * scale
    three_imag = (kernel_real * imag_part + kernel_imag * real_part) * scale
    spectra = jnp.concatenate([one_real, three_real, one_imag, three_imag], axis=1).astype(
        jnp.bfloat16
    )
    by_cos = dot32(cosine, spectra)
    by_sin = dot32(sine, spectra)
    columns_done = jnp.concatenate(
        [
            by_cos[:, : 2 * n] - by_sin[:, 2 * n :],
            by_sin[:, : 2 * n] + by_cos[:, 2 * n :],
        ],
        axis=1,
    ).astype(jnp.bfloat16)
    arranged = jnp.concatenate(
        [columns_done[:, k * n : (k + 1) * n] for k in range(4)], axis=0
    )
    width = n // 4
    edge_cols = jnp.concatenate(
        [cosine[:, :width], cosine[:, n - width :], sine[:, :width], sine[:, n - width :]], axis=1
    )
    edge = dot32(arranged, edge_cols)
    edge_cos, edge_sin = edge[:, : 2 * width], edge[:, 2 * width :]
    edge_fields = jnp.stack(
        [
            edge_cos[:n] - edge_sin[2 * n : 3 * n],
            edge_sin[:n] + edge_cos[2 * n : 3 * n],
            edge_cos[n : 2 * n] - edge_sin[3 * n :],
            edge_sin[n : 2 * n] + edge_cos[3 * n :],
        ]
    ).astype(jnp.bfloat16)
    by_cos = dot32(arranged, cosine)
    by_sin = dot32(arranged, sine)
    return edge_fields, jnp.stack(
        [
            by_cos[:n] - by_sin[2 * n : 3 * n],
            by_sin[:n] + by_cos[2 * n : 3 * n],
            by_cos[n : 2 * n] - by_sin[3 * n :],
            by_sin[n : 2 * n] + by_cos[3 * n :],
        ]
    ).astype(jnp.bfloat16)


def blend_edges(extended, has_top, has_bottom, has_left, has_right, width):
    values = extended.astype(jnp.float32)
    row_count = values.shape[1] - 2 * width
    col_count = values.shape[2] - 2 * width
    ramp = (jnp.arange(width, dtype=jnp.float32) + 0.5) / width
    top_weight = jnp.where(has_top, ramp, 1.0)[None, :, None]
    bottom_weight = jnp.where(has_bottom, ramp[::-1], 1.0)[None, :, None]
    middle = values[:, width : width + row_count, :]
    top_band = top_weight * middle[:, :width] + (1.0 - top_weight) * values[:, :width]
    bottom_band = (
        bottom_weight * middle[:, row_count - width :]
        + (1.0 - bottom_weight) * values[:, row_count + width :]
    )
    middle = jnp.concatenate([top_band, middle[:, width : row_count - width], bottom_band], axis=1)
    left_weight = jnp.where(has_left, ramp, 1.0)[None, None, :]
    right_weight = jnp.where(has_right, ramp[::-1], 1.0)[None, None, :]
    inner = middle[:, :, width : width + col_count]
    left_band = left_weight * inner[:, :, :width] + (1.0 - left_weight) * middle[:, :, :width]
    right_band = (
        right_weight * inner[:, :, col_count - width :]
        + (1.0 - right_weight) * middle[:, :, col_count + width :]
    )
    return jnp.concatenate([left_band, inner[:, :, width : col_count - width], right_band], axis=2)


def one_hot_rows(codes, count, values):
    picks = codes[None, :] == jnp.arange(1, count + 1, dtype=jnp.int32)[:, None]
    return jnp.dot(picks.astype(values.dtype), values, preferred_element_type=jnp.float32)


def gathered_rows(table_rows, picks):
    flat = picks.reshape(-1)
    rows = jnp.arange(table_rows.shape[0], dtype=jnp.int32)
    split = lambda x: ((x // CODE_SPLIT).astype(jnp.bfloat16), (x % CODE_SPLIT).astype(jnp.bfloat16))
    (pick_hi, pick_lo), (row_hi, row_lo) = split(flat), split(rows)
    chosen = (pick_hi[:, None] == row_hi[None, :]) & (pick_lo[:, None] == row_lo[None, :])
    values = jnp.dot(chosen.astype(table_rows.dtype), table_rows, preferred_element_type=jnp.float32)
    return values.astype(table_rows.dtype).reshape(picks.shape + table_rows.shape[1:])


CODE_SPLIT = 64
CODE_ROWS = 16


def with_codes(values, codes):
    depth, width = values.shape[1], values.shape[2]
    halves = jnp.concatenate([codes // CODE_SPLIT, codes % CODE_SPLIT], axis=1)
    code_rows = halves.reshape(values.shape[0], -1, width).astype(values.dtype)
    pad = jnp.zeros((values.shape[0], CODE_ROWS - code_rows.shape[1], width), values.dtype)
    return jnp.concatenate([values, code_rows, pad], axis=1)


def split_codes(payload, depth):
    width = payload.shape[2]
    used = 2 * depth // width
    halves = payload[:, depth : depth + used].reshape(payload.shape[0], 2 * depth)
    halves = halves.astype(jnp.int32)
    codes = halves[:, :depth] * CODE_SPLIT + halves[:, depth:]
    return payload[:, :depth].reshape(-1, width), codes.reshape(-1)


def sent_block(kappa, lists, slots, counts):
    depth = lists.shape[1]
    live = jnp.arange(depth, dtype=jnp.int32)[None, :] < counts[:, None]
    codes = jnp.where(live, slots + 1, 0)
    return with_codes(gathered_rows(kappa, lists), codes)


def row_blend(own, above, below, top_weight, bottom_weight, width):
    count = own.shape[1]
    top = top_weight * own[:, :width] + (1.0 - top_weight) * above
    bottom = bottom_weight * own[:, count - width :] + (1.0 - bottom_weight) * below
    return jnp.concatenate([top, own[:, width : count - width], bottom], axis=1)


def on_device(kappa, send_list, dest_slot, send_count):
    tile_width = kappa.shape[1]
    rows_axis = lax.axis_size("px")
    cols_axis = lax.axis_size("py")
    band_index = lax.axis_index("px")
    column_index = lax.axis_index("py")
    slot_depth = send_list.shape[2]
    upper_band = jnp.maximum(band_index - 1, 0)
    band_rows = lambda table, band: lax.dynamic_slice_in_dim(table[0], band * cols_axis, cols_axis)
    upper_counts = jnp.where(band_index > 0, band_rows(send_count, upper_band), 0)
    same_sent = sent_block(
        kappa,
        band_rows(send_list, band_index),
        band_rows(dest_slot, band_index),
        band_rows(send_count, band_index),
    )
    rise_sent = sent_block(
        kappa, band_rows(send_list, upper_band), band_rows(dest_slot, upper_band), upper_counts
    )
    arrived = lax.all_to_all(jnp.stack([same_sent, rise_sent], axis=1), "py", 0, 0, tiled=True)
    same_values, same_codes = split_codes(arrived[:, 0], slot_depth)
    rise_values, rise_codes = split_codes(arrived[:, 1], slot_depth)
    rise_total = PATCH_ROWS * PATCH_COLS // tile_width // 4
    rise_live = rise_codes > 0
    rise_place = jnp.where(rise_live, jnp.cumsum(rise_live.astype(jnp.int32)), 0)
    packed_values = one_hot_rows(rise_place, rise_total, rise_values).astype(kappa.dtype)
    packed_picks = rise_place[None, :] == jnp.arange(1, rise_total + 1, dtype=jnp.int32)[:, None]
    packed_codes = jnp.sum(jnp.where(packed_picks, rise_codes[None, :], 0), axis=1)
    packed = with_codes(packed_values.reshape(1, rise_total, tile_width), packed_codes[None])
    raised_values, raised_codes = split_codes(shifted(packed, "px", -1), rise_total)
    slot_total = PATCH_ROWS * PATCH_COLS // tile_width
    patch_tiles = (
        one_hot_rows(same_codes, slot_total, same_values)
        + one_hot_rows(raised_codes, slot_total, raised_values)
    ).astype(kappa.dtype)
    edge_fields, fields = flexion_fields(patch_tiles.reshape(PATCH_ROWS, PATCH_COLS))
    width = tile_width
    last = PATCH_ROWS - width
    left = shifted(edge_fields[:, :, width:], "py", 1)
    right = shifted(edge_fields[:, :, :width], "py", -1)
    above = shifted(fields[:, last:], "px", 1)
    below = shifted(fields[:, :width], "px", -1)
    corners_above = shifted(
        jnp.concatenate([left[:, last:], right[:, last:]], axis=2), "px", 1
    )
    corners_below = shifted(
        jnp.concatenate([left[:, :width], right[:, :width]], axis=2), "px", -1
    )
    above_left, above_right = corners_above[:, :, :width], corners_above[:, :, width:]
    below_left, below_right = corners_below[:, :, :width], corners_below[:, :, width:]
    ramp = (jnp.arange(width, dtype=jnp.float32) + 0.5) / width
    top_weight = jnp.where(band_index > 0, ramp, 1.0)[None, :, None]
    bottom_weight = jnp.where(band_index < rows_axis - 1, ramp[::-1], 1.0)[None, :, None]
    left_weight = jnp.where(column_index > 0, ramp, 1.0)[None, None, :]
    right_weight = jnp.where(column_index < cols_axis - 1, ramp[::-1], 1.0)[None, None, :]
    f32 = lambda x: x.astype(jnp.float32)
    count = fields.shape[1]
    ones = jnp.ones((count - 2 * width,), jnp.float32)
    row_weight = jnp.concatenate([top_weight[0, :, 0], ones, bottom_weight[0, :, 0]])[:, None]
    col_weight = jnp.concatenate([left_weight[0, 0], ones, right_weight[0, 0]])[None, :]
    zero_rows = jnp.zeros((fields.shape[0], count - 2 * width, 1), jnp.float32)
    vertical = jnp.concatenate(
        [f32(above), jnp.broadcast_to(zero_rows, (fields.shape[0], count - 2 * width, count)),
         f32(below)], axis=1
    )
    rows_done = row_weight * f32(fields) + (1.0 - row_weight) * vertical
    side = lambda strip, upper, lower: row_weight * f32(strip) + (1.0 - row_weight) * jnp.concatenate(
        [f32(upper), jnp.broadcast_to(zero_rows, (fields.shape[0], count - 2 * width, width)),
         f32(lower)], axis=1
    )
    left_rows = side(left, above_left, below_left)
    right_rows = side(right, above_right, below_right)
    horizontal = jnp.concatenate(
        [left_rows, jnp.broadcast_to(zero_rows[:, :1], (fields.shape[0], count, count - 2 * width)),
         right_rows], axis=2
    )
    return col_weight * rows_done + (1.0 - col_weight) * horizontal


def solution(mesh):
    placed = (
        P(("px", "py"), None),
        P(("px", "py"), None, None),
        P(("px", "py"), None, None),
        P(("px", "py"), None),
    )
    return jax.shard_map(
        on_device, mesh=mesh, in_specs=placed, out_specs=P(None, "px", "py"), check_vma=False
    )
```

```python
import math

import jax
import ml_dtypes
import numpy as np
import jax.numpy as jnp
from jax import lax
from jax.sharding import PartitionSpec as P

PATCH_ROWS = 512
PATCH_COLS = 512


def shifted(shard, axis, by):
    size = lax.axis_size(axis)
    pairs = [(i, i + by) for i in range(size) if 0 <= i + by < size]
    return lax.ppermute(shard, axis, pairs)


def padded(block, sides, width):
    for axis, dim in sides:
        count = lax.axis_size(axis)
        forward = [(i, i + 1) for i in range(count - 1)]
        backward = [(target, source) for source, target in forward]
        low = lax.ppermute(
            lax.slice_in_dim(block, block.shape[dim] - width, None, axis=dim), axis, forward
        )
        high = lax.ppermute(lax.slice_in_dim(block, 0, width, axis=dim), axis, backward)
        block = jnp.concatenate([low, block, high], axis=dim)
    return block


def dft_tables(length):
    positions = np.arange(length, dtype=np.int64)
    phases = positions[:, None] * positions[None, :] % length
    angles = phases.astype(np.float32) * np.float32(2.0 * math.pi / length)
    return (np.cos(angles).astype(np.float32), np.sin(angles).astype(np.float32))


def table(values):
    return jnp.asarray(values.astype(ml_dtypes.bfloat16))


def wavenumbers(length):
    positions = jnp.arange(length, dtype=jnp.int32)
    signed = positions - length * (positions >= (length + 1) // 2).astype(jnp.int32)
    return signed.astype(jnp.float32) * (2.0 / length)


def dot32(a, b):
    return jnp.dot(a, b, preferred_element_type=jnp.float32)


def flexion_fields(pixels):
    row_count = pixels.shape[0]
    col_count = pixels.shape[1]
    assert row_count == col_count
    cos_np, sin_np = dft_tables(row_count)
    cosine, sine = table(cos_np), table(sin_np)
    n = row_count
    halves = jnp.concatenate([dot32(pixels, cosine), dot32(pixels, sine)], axis=1).astype(
        jnp.bfloat16
    )
    by_cos = dot32(cosine, halves)
    by_sin = dot32(sine, halves)
    real_part = by_cos[:, :n] - by_sin[:, n:]
    imag_part = -(by_sin[:, :n] + by_cos[:, n:])
    across = wavenumbers(col_count)[None, :]
    down = wavenumbers(row_count)[:, None]
    scale = 1.0 / (row_count * col_count)
    power = across * across + down * down
    safe_power = jnp.where(power > 0, power, 1.0)
    cube_real = across * across * across - 3.0 * across * down * down
    cube_imag = 3.0 * across * across * down - down * down * down
    one_real = (-down * real_part - across * imag_part) * scale
    one_imag = (across * real_part - down * imag_part) * scale
    kernel_real = -cube_imag / safe_power
    kernel_imag = cube_real / safe_power
    three_real = (kernel_real * real_part - kernel_imag * imag_part) * scale
    three_imag = (kernel_real * imag_part + kernel_imag * real_part) * scale
    spectra = jnp.concatenate([one_real, three_real, one_imag, three_imag], axis=1).astype(
        jnp.bfloat16
    )
    by_cos = dot32(cosine, spectra)
    by_sin = dot32(sine, spectra)
    columns_done = jnp.concatenate(
        [
            by_cos[:, : 2 * n] - by_sin[:, 2 * n :],
            by_sin[:, : 2 * n] + by_cos[:, 2 * n :],
        ],
        axis=1,
    ).astype(jnp.bfloat16)
    arranged = jnp.concatenate(
        [columns_done[:, k * n : (k + 1) * n] for k in range(4)], axis=0
    )
    width = n // 4
    edge_cols = jnp.concatenate(
        [cosine[:, :width], cosine[:, n - width :], sine[:, :width], sine[:, n - width :]], axis=1
    )
    edge = dot32(arranged, edge_cols)
    edge_cos, edge_sin = edge[:, : 2 * width], edge[:, 2 * width :]
    edge_fields = jnp.stack(
        [
            edge_cos[:n] - edge_sin[2 * n : 3 * n],
            edge_sin[:n] + edge_cos[2 * n : 3 * n],
            edge_cos[n : 2 * n] - edge_sin[3 * n :],
            edge_sin[n : 2 * n] + edge_cos[3 * n :],
        ]
    ).astype(jnp.bfloat16)
    by_cos = dot32(arranged, cosine)
    by_sin = dot32(arranged, sine)
    return edge_fields, jnp.stack(
        [
            by_cos[:n] - by_sin[2 * n : 3 * n],
            by_sin[:n] + by_cos[2 * n : 3 * n],
            by_cos[n : 2 * n] - by_sin[3 * n :],
            by_sin[n : 2 * n] + by_cos[3 * n :],
        ]
    ).astype(jnp.bfloat16)


def blend_edges(extended, has_top, has_bottom, has_left, has_right, width):
    values = extended.astype(jnp.float32)
    row_count = values.shape[1] - 2 * width
    col_count = values.shape[2] - 2 * width
    ramp = (jnp.arange(width, dtype=jnp.float32) + 0.5) / width
    top_weight = jnp.where(has_top, ramp, 1.0)[None, :, None]
    bottom_weight = jnp.where(has_bottom, ramp[::-1], 1.0)[None, :, None]
    middle = values[:, width : width + row_count, :]
    top_band = top_weight * middle[:, :width] + (1.0 - top_weight) * values[:, :width]
    bottom_band = (
        bottom_weight * middle[:, row_count - width :]
        + (1.0 - bottom_weight) * values[:, row_count + width :]
    )
    middle = jnp.concatenate([top_band, middle[:, width : row_count - width], bottom_band], axis=1)
    left_weight = jnp.where(has_left, ramp, 1.0)[None, None, :]
    right_weight = jnp.where(has_right, ramp[::-1], 1.0)[None, None, :]
    inner = middle[:, :, width : width + col_count]
    left_band = left_weight * inner[:, :, :width] + (1.0 - left_weight) * middle[:, :, :width]
    right_band = (
        right_weight * inner[:, :, col_count - width :]
        + (1.0 - right_weight) * middle[:, :, col_count + width :]
    )
    return jnp.concatenate([left_band, inner[:, :, width : col_count - width], right_band], axis=2)


def one_hot_rows(codes, count, values):
    picks = codes[None, :] == jnp.arange(1, count + 1, dtype=jnp.int32)[:, None]
    return jnp.dot(picks.astype(values.dtype), values, preferred_element_type=jnp.float32)


def gathered_rows(table_rows, picks):
    chosen = picks.reshape(-1)[:, None] == jnp.arange(table_rows.shape[0], dtype=jnp.int32)
    values = jnp.dot(chosen.astype(table_rows.dtype), table_rows, preferred_element_type=jnp.float32)
    return values.astype(table_rows.dtype).reshape(picks.shape + table_rows.shape[1:])


CODE_SPLIT = 64
CODE_ROWS = 16


def with_codes(values, codes):
    depth, width = values.shape[1], values.shape[2]
    halves = jnp.concatenate([codes // CODE_SPLIT, codes % CODE_SPLIT], axis=1)
    code_rows = halves.reshape(values.shape[0], -1, width).astype(values.dtype)
    pad = jnp.zeros((values.shape[0], CODE_ROWS - code_rows.shape[1], width), values.dtype)
    return jnp.concatenate([values, code_rows, pad], axis=1)


def split_codes(payload, depth):
    width = payload.shape[2]
    used = 2 * depth // width
    halves = payload[:, depth : depth + used].reshape(payload.shape[0], 2 * depth)
    halves = halves.astype(jnp.int32)
    codes = halves[:, :depth] * CODE_SPLIT + halves[:, depth:]
    return payload[:, :depth].reshape(-1, width), codes.reshape(-1)


def sent_block(kappa, lists, slots, counts):
    depth = lists.shape[1]
    live = jnp.arange(depth, dtype=jnp.int32)[None, :] < counts[:, None]
    codes = jnp.where(live, slots + 1, 0)
    return with_codes(gathered_rows(kappa, lists), codes)


def row_blend(own, above, below, top_weight, bottom_weight, width):
    count = own.shape[1]
    top = top_weight * own[:, :width] + (1.0 - top_weight) * above
    bottom = bottom_weight * own[:, count - width :] + (1.0 - bottom_weight) * below
    return jnp.concatenate([top, own[:, width : count - width], bottom], axis=1)


def on_device(kappa, send_list, dest_slot, send_count):
    tile_width = kappa.shape[1]
    rows_axis = lax.axis_size("px")
    cols_axis = lax.axis_size("py")
    band_index = lax.axis_index("px")
    column_index = lax.axis_index("py")
    slot_depth = send_list.shape[2]
    upper_band = jnp.maximum(band_index - 1, 0)
    band_rows = lambda table, band: lax.dynamic_slice_in_dim(table[0], band * cols_axis, cols_axis)
    upper_counts = jnp.where(band_index > 0, band_rows(send_count, upper_band), 0)
    same_sent = sent_block(
        kappa,
        band_rows(send_list, band_index),
        band_rows(dest_slot, band_index),
        band_rows(send_count, band_index),
    )
    rise_sent = sent_block(
        kappa, band_rows(send_list, upper_band), band_rows(dest_slot, upper_band), upper_counts
    )
    same_arrived = lax.all_to_all(same_sent, "py", 0, 0, tiled=True)
    rise_blocks = [rise_sent[column_index]]
    for shift in range(1, cols_axis):
        target = lax.rem(column_index + shift, cols_axis)
        pairs = [(i, (i + shift) % cols_axis) for i in range(cols_axis)]
        rise_blocks.append(lax.ppermute(rise_sent[target], "py", pairs))
    same_values, same_codes = split_codes(same_arrived, slot_depth)
    rise_values, rise_codes = split_codes(jnp.stack(rise_blocks), slot_depth)
    rise_total = PATCH_ROWS * PATCH_COLS // tile_width // 4
    rise_live = rise_codes > 0
    rise_place = jnp.where(rise_live, jnp.cumsum(rise_live.astype(jnp.int32)), 0)
    packed_values = one_hot_rows(rise_place, rise_total, rise_values).astype(kappa.dtype)
    packed_picks = rise_place[None, :] == jnp.arange(1, rise_total + 1, dtype=jnp.int32)[:, None]
    packed_codes = jnp.sum(jnp.where(packed_picks, rise_codes[None, :], 0), axis=1)
    packed = with_codes(packed_values.reshape(1, rise_total, tile_width), packed_codes[None])
    raised_values, raised_codes = split_codes(shifted(packed, "px", -1), rise_total)
    slot_total = PATCH_ROWS * PATCH_COLS // tile_width
    patch_tiles = (
        one_hot_rows(same_codes, slot_total, same_values)
        + one_hot_rows(raised_codes, slot_total, raised_values)
    ).astype(kappa.dtype)
    edge_fields, fields = flexion_fields(patch_tiles.reshape(PATCH_ROWS, PATCH_COLS))
    width = tile_width
    last = PATCH_ROWS - width
    left = shifted(edge_fields[:, :, width:], "py", 1)
    right = shifted(edge_fields[:, :, :width], "py", -1)
    above = shifted(fields[:, last:], "px", 1)
    below = shifted(fields[:, :width], "px", -1)
    corners_above = shifted(
        jnp.concatenate([left[:, last:], right[:, last:]], axis=2), "px", 1
    )
    corners_below = shifted(
        jnp.concatenate([left[:, :width], right[:, :width]], axis=2), "px", -1
    )
    above_left, above_right = corners_above[:, :, :width], corners_above[:, :, width:]
    below_left, below_right = corners_below[:, :, :width], corners_below[:, :, width:]
    ramp = (jnp.arange(width, dtype=jnp.float32) + 0.5) / width
    top_weight = jnp.where(band_index > 0, ramp, 1.0)[None, :, None]
    bottom_weight = jnp.where(band_index < rows_axis - 1, ramp[::-1], 1.0)[None, :, None]
    left_weight = jnp.where(column_index > 0, ramp, 1.0)[None, None, :]
    right_weight = jnp.where(column_index < cols_axis - 1, ramp[::-1], 1.0)[None, None, :]
    f32 = lambda x: x.astype(jnp.float32)
    count = fields.shape[1]
    ones = jnp.ones((count - 2 * width,), jnp.float32)
    row_weight = jnp.concatenate([top_weight[0, :, 0], ones, bottom_weight[0, :, 0]])[:, None]
    col_weight = jnp.concatenate([left_weight[0, 0], ones, right_weight[0, 0]])[None, :]
    zero_rows = jnp.zeros((fields.shape[0], count - 2 * width, 1), jnp.float32)
    vertical = jnp.concatenate(
        [f32(above), jnp.broadcast_to(zero_rows, (fields.shape[0], count - 2 * width, count)),
         f32(below)], axis=1
    )
    rows_done = row_weight * f32(fields) + (1.0 - row_weight) * vertical
    side = lambda strip, upper, lower: row_weight * f32(strip) + (1.0 - row_weight) * jnp.concatenate(
        [f32(upper), jnp.broadcast_to(zero_rows, (fields.shape[0], count - 2 * width, width)),
         f32(lower)], axis=1
    )
    left_rows = side(left, above_left, below_left)
    right_rows = side(right, above_right, below_right)
    horizontal = jnp.concatenate(
        [left_rows, jnp.broadcast_to(zero_rows[:, :1], (fields.shape[0], count, count - 2 * width)),
         right_rows], axis=2
    )
    return col_weight * rows_done + (1.0 - col_weight) * horizontal


def solution(mesh):
    placed = (
        P(("px", "py"), None),
        P(("px", "py"), None, None),
        P(("px", "py"), None, None),
        P(("px", "py"), None),
    )
    return jax.shard_map(
        on_device, mesh=mesh, in_specs=placed, out_specs=P(None, "px", "py"), check_vma=False
    )
```

```python
import math

import jax
import ml_dtypes
import numpy as np
import jax.numpy as jnp
from jax import lax
from jax.sharding import PartitionSpec as P

PATCH_ROWS = 512
PATCH_COLS = 512


def shifted(shard, axis, by):
    size = lax.axis_size(axis)
    pairs = [(i, i + by) for i in range(size) if 0 <= i + by < size]
    return lax.ppermute(shard, axis, pairs)


def padded(block, sides, width):
    for axis, dim in sides:
        count = lax.axis_size(axis)
        forward = [(i, i + 1) for i in range(count - 1)]
        backward = [(target, source) for source, target in forward]
        low = lax.ppermute(
            lax.slice_in_dim(block, block.shape[dim] - width, None, axis=dim), axis, forward
        )
        high = lax.ppermute(lax.slice_in_dim(block, 0, width, axis=dim), axis, backward)
        block = jnp.concatenate([low, block, high], axis=dim)
    return block


def dft_tables(length):
    positions = np.arange(length, dtype=np.int64)
    phases = positions[:, None] * positions[None, :] % length
    angles = phases.astype(np.float32) * np.float32(2.0 * math.pi / length)
    return (np.cos(angles).astype(np.float32), np.sin(angles).astype(np.float32))


def table(values):
    return jnp.asarray(values.astype(ml_dtypes.bfloat16))


def wavenumbers(length):
    positions = jnp.arange(length, dtype=jnp.int32)
    signed = positions - length * (positions >= (length + 1) // 2).astype(jnp.int32)
    return signed.astype(jnp.float32) * (2.0 / length)


def dot32(a, b):
    return jnp.dot(a, b, preferred_element_type=jnp.float32)


def row_products(cosine, sine, values):
    n = cosine.shape[0]
    half = n // 2
    top = half + 8
    by_cos = dot32(cosine[:top], values)
    by_sin = dot32(sine[:top], values)
    by_cos = jnp.concatenate([by_cos[: half + 1], jnp.flip(by_cos[1:half], axis=0)], axis=0)
    by_sin = jnp.concatenate([by_sin[: half + 1], -jnp.flip(by_sin[1:half], axis=0)], axis=0)
    return by_cos, by_sin


def flexion_fields(pixels):
    row_count = pixels.shape[0]
    col_count = pixels.shape[1]
    assert row_count == col_count
    cos_np, sin_np = dft_tables(row_count)
    cosine, sine = table(cos_np), table(sin_np)
    n = row_count
    halves = jnp.concatenate([dot32(pixels, cosine), dot32(pixels, sine)], axis=1).astype(
        jnp.bfloat16
    )
    by_cos, by_sin = row_products(cosine, sine, halves)
    real_part = by_cos[:, :n] - by_sin[:, n:]
    imag_part = -(by_sin[:, :n] + by_cos[:, n:])
    across = wavenumbers(col_count)[None, :]
    down = wavenumbers(row_count)[:, None]
    scale = 1.0 / (row_count * col_count)
    power = across * across + down * down
    safe_power = jnp.where(power > 0, power, 1.0)
    cube_real = across * across * across - 3.0 * across * down * down
    cube_imag = 3.0 * across * across * down - down * down * down
    one_real = (-down * real_part - across * imag_part) * scale
    one_imag = (across * real_part - down * imag_part) * scale
    kernel_real = -cube_imag / safe_power
    kernel_imag = cube_real / safe_power
    three_real = (kernel_real * real_part - kernel_imag * imag_part) * scale
    three_imag = (kernel_real * imag_part + kernel_imag * real_part) * scale
    spectra = jnp.concatenate([one_real, three_real, one_imag, three_imag], axis=1).astype(
        jnp.bfloat16
    )
    by_cos, by_sin = row_products(cosine, sine, spectra)
    columns_done = jnp.concatenate(
        [
            by_cos[:, : 2 * n] - by_sin[:, 2 * n :],
            by_sin[:, : 2 * n] + by_cos[:, 2 * n :],
        ],
        axis=1,
    ).astype(jnp.bfloat16)
    arranged = jnp.concatenate(
        [columns_done[:, k * n : (k + 1) * n] for k in range(4)], axis=0
    )
    width = n // 4
    edge_cols = jnp.concatenate(
        [cosine[:, :width], cosine[:, n - width :], sine[:, :width], sine[:, n - width :]], axis=1
    )
    edge = dot32(arranged, edge_cols)
    edge_cos, edge_sin = edge[:, : 2 * width], edge[:, 2 * width :]
    edge_fields = jnp.stack(
        [
            edge_cos[:n] - edge_sin[2 * n : 3 * n],
            edge_sin[:n] + edge_cos[2 * n : 3 * n],
            edge_cos[n : 2 * n] - edge_sin[3 * n :],
            edge_sin[n : 2 * n] + edge_cos[3 * n :],
        ]
    ).astype(jnp.bfloat16)
    by_cos = dot32(arranged, cosine)
    by_sin = dot32(arranged, sine)
    return edge_fields, jnp.stack(
        [
            by_cos[:n] - by_sin[2 * n : 3 * n],
            by_sin[:n] + by_cos[2 * n : 3 * n],
            by_cos[n : 2 * n] - by_sin[3 * n :],
            by_sin[n : 2 * n] + by_cos[3 * n :],
        ]
    ).astype(jnp.bfloat16)


def blend_edges(extended, has_top, has_bottom, has_left, has_right, width):
    values = extended.astype(jnp.float32)
    row_count = values.shape[1] - 2 * width
    col_count = values.shape[2] - 2 * width
    ramp = (jnp.arange(width, dtype=jnp.float32) + 0.5) / width
    top_weight = jnp.where(has_top, ramp, 1.0)[None, :, None]
    bottom_weight = jnp.where(has_bottom, ramp[::-1], 1.0)[None, :, None]
    middle = values[:, width : width + row_count, :]
    top_band = top_weight * middle[:, :width] + (1.0 - top_weight) * values[:, :width]
    bottom_band = (
        bottom_weight * middle[:, row_count - width :]
        + (1.0 - bottom_weight) * values[:, row_count + width :]
    )
    middle = jnp.concatenate([top_band, middle[:, width : row_count - width], bottom_band], axis=1)
    left_weight = jnp.where(has_left, ramp, 1.0)[None, None, :]
    right_weight = jnp.where(has_right, ramp[::-1], 1.0)[None, None, :]
    inner = middle[:, :, width : width + col_count]
    left_band = left_weight * inner[:, :, :width] + (1.0 - left_weight) * middle[:, :, :width]
    right_band = (
        right_weight * inner[:, :, col_count - width :]
        + (1.0 - right_weight) * middle[:, :, col_count + width :]
    )
    return jnp.concatenate([left_band, inner[:, :, width : col_count - width], right_band], axis=2)


def one_hot_rows(codes, count, values):
    picks = codes[None, :] == jnp.arange(1, count + 1, dtype=jnp.int32)[:, None]
    return jnp.dot(picks.astype(values.dtype), values, preferred_element_type=jnp.float32)


def gathered_rows(table_rows, picks):
    chosen = picks.reshape(-1)[:, None] == jnp.arange(table_rows.shape[0], dtype=jnp.int32)
    values = jnp.dot(chosen.astype(table_rows.dtype), table_rows, preferred_element_type=jnp.float32)
    return values.astype(table_rows.dtype).reshape(picks.shape + table_rows.shape[1:])


CODE_SPLIT = 64
CODE_ROWS = 16


def with_codes(values, codes):
    depth, width = values.shape[1], values.shape[2]
    halves = jnp.concatenate([codes // CODE_SPLIT, codes % CODE_SPLIT], axis=1)
    code_rows = halves.reshape(values.shape[0], -1, width).astype(values.dtype)
    pad = jnp.zeros((values.shape[0], CODE_ROWS - code_rows.shape[1], width), values.dtype)
    return jnp.concatenate([values, code_rows, pad], axis=1)


def split_codes(payload, depth):
    width = payload.shape[2]
    used = 2 * depth // width
    halves = payload[:, depth : depth + used].reshape(payload.shape[0], 2 * depth)
    halves = halves.astype(jnp.int32)
    codes = halves[:, :depth] * CODE_SPLIT + halves[:, depth:]
    return payload[:, :depth].reshape(-1, width), codes.reshape(-1)


def sent_block(kappa, lists, slots, counts):
    depth = lists.shape[1]
    live = jnp.arange(depth, dtype=jnp.int32)[None, :] < counts[:, None]
    codes = jnp.where(live, slots + 1, 0)
    return with_codes(gathered_rows(kappa, lists), codes)


def row_blend(own, above, below, top_weight, bottom_weight, width):
    count = own.shape[1]
    top = top_weight * own[:, :width] + (1.0 - top_weight) * above
    bottom = bottom_weight * own[:, count - width :] + (1.0 - bottom_weight) * below
    return jnp.concatenate([top, own[:, width : count - width], bottom], axis=1)


def on_device(kappa, send_list, dest_slot, send_count):
    tile_width = kappa.shape[1]
    rows_axis = lax.axis_size("px")
    cols_axis = lax.axis_size("py")
    band_index = lax.axis_index("px")
    column_index = lax.axis_index("py")
    slot_depth = send_list.shape[2]
    upper_band = jnp.maximum(band_index - 1, 0)
    band_rows = lambda table, band: lax.dynamic_slice_in_dim(table[0], band * cols_axis, cols_axis)
    upper_counts = jnp.where(band_index > 0, band_rows(send_count, upper_band), 0)
    same_sent = sent_block(
        kappa,
        band_rows(send_list, band_index),
        band_rows(dest_slot, band_index),
        band_rows(send_count, band_index),
    )
    rise_sent = sent_block(
        kappa, band_rows(send_list, upper_band), band_rows(dest_slot, upper_band), upper_counts
    )
    arrived = lax.all_to_all(jnp.stack([same_sent, rise_sent], axis=1), "py", 0, 0, tiled=True)
    same_values, same_codes = split_codes(arrived[:, 0], slot_depth)
    rise_values, rise_codes = split_codes(arrived[:, 1], slot_depth)
    rise_total = PATCH_ROWS * PATCH_COLS // tile_width // 4
    rise_live = rise_codes > 0
    rise_place = jnp.where(rise_live, jnp.cumsum(rise_live.astype(jnp.int32)), 0)
    packed_values = one_hot_rows(rise_place, rise_total, rise_values).astype(kappa.dtype)
    packed_picks = rise_place[None, :] == jnp.arange(1, rise_total + 1, dtype=jnp.int32)[:, None]
    packed_codes = jnp.sum(jnp.where(packed_picks, rise_codes[None, :], 0), axis=1)
    packed = with_codes(packed_values.reshape(1, rise_total, tile_width), packed_codes[None])
    raised_values, raised_codes = split_codes(shifted(packed, "px", -1), rise_total)
    slot_total = PATCH_ROWS * PATCH_COLS // tile_width
    patch_tiles = (
        one_hot_rows(same_codes, slot_total, same_values)
        + one_hot_rows(raised_codes, slot_total, raised_values)
    ).astype(kappa.dtype)
    edge_fields, fields = flexion_fields(patch_tiles.reshape(PATCH_ROWS, PATCH_COLS))
    width = tile_width
    last = PATCH_ROWS - width
    left = shifted(edge_fields[:, :, width:], "py", 1)
    right = shifted(edge_fields[:, :, :width], "py", -1)
    above = shifted(fields[:, last:], "px", 1)
    below = shifted(fields[:, :width], "px", -1)
    corners_above = shifted(
        jnp.concatenate([left[:, last:], right[:, last:]], axis=2), "px", 1
    )
    corners_below = shifted(
        jnp.concatenate([left[:, :width], right[:, :width]], axis=2), "px", -1
    )
    above_left, above_right = corners_above[:, :, :width], corners_above[:, :, width:]
    below_left, below_right = corners_below[:, :, :width], corners_below[:, :, width:]
    ramp = (jnp.arange(width, dtype=jnp.float32) + 0.5) / width
    top_weight = jnp.where(band_index > 0, ramp, 1.0)[None, :, None]
    bottom_weight = jnp.where(band_index < rows_axis - 1, ramp[::-1], 1.0)[None, :, None]
    left_weight = jnp.where(column_index > 0, ramp, 1.0)[None, None, :]
    right_weight = jnp.where(column_index < cols_axis - 1, ramp[::-1], 1.0)[None, None, :]
    f32 = lambda x: x.astype(jnp.float32)
    count = fields.shape[1]
    ones = jnp.ones((count - 2 * width,), jnp.float32)
    row_weight = jnp.concatenate([top_weight[0, :, 0], ones, bottom_weight[0, :, 0]])[:, None]
    col_weight = jnp.concatenate([left_weight[0, 0], ones, right_weight[0, 0]])[None, :]
    zero_rows = jnp.zeros((fields.shape[0], count - 2 * width, 1), jnp.float32)
    vertical = jnp.concatenate(
        [f32(above), jnp.broadcast_to(zero_rows, (fields.shape[0], count - 2 * width, count)),
         f32(below)], axis=1
    )
    rows_done = row_weight * f32(fields) + (1.0 - row_weight) * vertical
    side = lambda strip, upper, lower: row_weight * f32(strip) + (1.0 - row_weight) * jnp.concatenate(
        [f32(upper), jnp.broadcast_to(zero_rows, (fields.shape[0], count - 2 * width, width)),
         f32(lower)], axis=1
    )
    left_rows = side(left, above_left, below_left)
    right_rows = side(right, above_right, below_right)
    horizontal = jnp.concatenate(
        [left_rows, jnp.broadcast_to(zero_rows[:, :1], (fields.shape[0], count, count - 2 * width)),
         right_rows], axis=2
    )
    return col_weight * rows_done + (1.0 - col_weight) * horizontal


def solution(mesh):
    placed = (
        P(("px", "py"), None),
        P(("px", "py"), None, None),
        P(("px", "py"), None, None),
        P(("px", "py"), None),
    )
    return jax.shard_map(
        on_device, mesh=mesh, in_specs=placed, out_specs=P(None, "px", "py"), check_vma=False
    )
```

```python
import math

import jax
import ml_dtypes
import numpy as np
import jax.numpy as jnp
from jax import lax
from jax.sharding import PartitionSpec as P

PATCH_ROWS = 512
PATCH_COLS = 512


def shifted(shard, axis, by):
    size = lax.axis_size(axis)
    pairs = [(i, i + by) for i in range(size) if 0 <= i + by < size]
    return lax.ppermute(shard, axis, pairs)


def padded(block, sides, width):
    for axis, dim in sides:
        count = lax.axis_size(axis)
        forward = [(i, i + 1) for i in range(count - 1)]
        backward = [(target, source) for source, target in forward]
        low = lax.ppermute(
            lax.slice_in_dim(block, block.shape[dim] - width, None, axis=dim), axis, forward
        )
        high = lax.ppermute(lax.slice_in_dim(block, 0, width, axis=dim), axis, backward)
        block = jnp.concatenate([low, block, high], axis=dim)
    return block


def dft_tables(length):
    positions = np.arange(length, dtype=np.int64)
    phases = positions[:, None] * positions[None, :] % length
    angles = phases.astype(np.float32) * np.float32(2.0 * math.pi / length)
    return (np.cos(angles).astype(np.float32), np.sin(angles).astype(np.float32))


def table(values):
    return jnp.asarray(values.astype(ml_dtypes.bfloat16))


def wavenumbers(length):
    positions = jnp.arange(length, dtype=jnp.int32)
    signed = positions - length * (positions >= (length + 1) // 2).astype(jnp.int32)
    return signed.astype(jnp.float32) * (2.0 / length)


def dot32(a, b):
    return jnp.dot(a, b, preferred_element_type=jnp.float32)


def flexion_fields(pixels):
    row_count = pixels.shape[0]
    col_count = pixels.shape[1]
    assert row_count == col_count
    cos_np, sin_np = dft_tables(row_count)
    cosine, sine = table(cos_np), table(sin_np)
    n = row_count
    halves = jnp.concatenate([dot32(pixels, cosine), dot32(pixels, sine)], axis=1).astype(
        jnp.bfloat16
    )
    by_cos = dot32(cosine, halves)
    by_sin = dot32(sine, halves)
    real_part = by_cos[:, :n] - by_sin[:, n:]
    imag_part = -(by_sin[:, :n] + by_cos[:, n:])
    across = wavenumbers(col_count)[None, :]
    down = wavenumbers(row_count)[:, None]
    scale = 1.0 / (row_count * col_count)
    power = across * across + down * down
    safe_power = jnp.where(power > 0, power, 1.0)
    cube_real = across * across * across - 3.0 * across * down * down
    cube_imag = 3.0 * across * across * down - down * down * down
    one_real = (-down * real_part - across * imag_part) * scale
    one_imag = (across * real_part - down * imag_part) * scale
    kernel_real = -cube_imag / safe_power
    kernel_imag = cube_real / safe_power
    three_real = (kernel_real * real_part - kernel_imag * imag_part) * scale
    three_imag = (kernel_real * imag_part + kernel_imag * real_part) * scale
    spectra = jnp.concatenate([one_real, three_real, one_imag, three_imag], axis=1).astype(
        jnp.bfloat16
    )
    by_cos = dot32(cosine, spectra)
    by_sin = dot32(sine, spectra)
    columns_done = jnp.concatenate(
        [
            by_cos[:, : 2 * n] - by_sin[:, 2 * n :],
            by_sin[:, : 2 * n] + by_cos[:, 2 * n :],
        ],
        axis=1,
    ).astype(jnp.bfloat16)
    arranged = jnp.concatenate(
        [columns_done[:, k * n : (k + 1) * n] for k in range(4)], axis=0
    )
    width = n // 4
    edge_cols = jnp.concatenate(
        [cosine[:, :width], cosine[:, n - width :], sine[:, :width], sine[:, n - width :]], axis=1
    )
    edge = dot32(arranged, edge_cols)
    edge_cos, edge_sin = edge[:, : 2 * width], edge[:, 2 * width :]
    edge_fields = jnp.stack(
        [
            edge_cos[:n] - edge_sin[2 * n : 3 * n],
            edge_sin[:n] + edge_cos[2 * n : 3 * n],
            edge_cos[n : 2 * n] - edge_sin[3 * n :],
            edge_sin[n : 2 * n] + edge_cos[3 * n :],
        ]
    ).astype(jnp.bfloat16)
    by_cos = dot32(arranged, cosine)
    by_sin = dot32(arranged, sine)
    return edge_fields, jnp.stack(
        [
            by_cos[:n] - by_sin[2 * n : 3 * n],
            by_sin[:n] + by_cos[2 * n : 3 * n],
            by_cos[n : 2 * n] - by_sin[3 * n :],
            by_sin[n : 2 * n] + by_cos[3 * n :],
        ]
    ).astype(jnp.bfloat16)


def blend_edges(extended, has_top, has_bottom, has_left, has_right, width):
    values = extended.astype(jnp.float32)
    row_count = values.shape[1] - 2 * width
    col_count = values.shape[2] - 2 * width
    ramp = (jnp.arange(width, dtype=jnp.float32) + 0.5) / width
    top_weight = jnp.where(has_top, ramp, 1.0)[None, :, None]
    bottom_weight = jnp.where(has_bottom, ramp[::-1], 1.0)[None, :, None]
    middle = values[:, width : width + row_count, :]
    top_band = top_weight * middle[:, :width] + (1.0 - top_weight) * values[:, :width]
    bottom_band = (
        bottom_weight * middle[:, row_count - width :]
        + (1.0 - bottom_weight) * values[:, row_count + width :]
    )
    middle = jnp.concatenate([top_band, middle[:, width : row_count - width], bottom_band], axis=1)
    left_weight = jnp.where(has_left, ramp, 1.0)[None, None, :]
    right_weight = jnp.where(has_right, ramp[::-1], 1.0)[None, None, :]
    inner = middle[:, :, width : width + col_count]
    left_band = left_weight * inner[:, :, :width] + (1.0 - left_weight) * middle[:, :, :width]
    right_band = (
        right_weight * inner[:, :, col_count - width :]
        + (1.0 - right_weight) * middle[:, :, col_count + width :]
    )
    return jnp.concatenate([left_band, inner[:, :, width : col_count - width], right_band], axis=2)


def one_hot_rows(codes, count, values):
    picks = codes[None, :] == jnp.arange(1, count + 1, dtype=jnp.int32)[:, None]
    return jnp.dot(picks.astype(values.dtype), values, preferred_element_type=values.dtype)


def gathered_rows(table_rows, picks):
    chosen = picks.reshape(-1)[:, None] == jnp.arange(table_rows.shape[0], dtype=jnp.int32)
    values = jnp.dot(chosen.astype(table_rows.dtype), table_rows, preferred_element_type=jnp.float32)
    return values.astype(table_rows.dtype).reshape(picks.shape + table_rows.shape[1:])


CODE_SPLIT = 64
CODE_ROWS = 16


def with_codes(values, codes):
    depth, width = values.shape[1], values.shape[2]
    halves = jnp.concatenate([codes // CODE_SPLIT, codes % CODE_SPLIT], axis=1)
    code_rows = halves.reshape(values.shape[0], -1, width).astype(values.dtype)
    pad = jnp.zeros((values.shape[0], CODE_ROWS - code_rows.shape[1], width), values.dtype)
    return jnp.concatenate([values, code_rows, pad], axis=1)


def split_codes(payload, depth):
    width = payload.shape[2]
    used = 2 * depth // width
    halves = payload[:, depth : depth + used].reshape(payload.shape[0], 2 * depth)
    halves = halves.astype(jnp.int32)
    codes = halves[:, :depth] * CODE_SPLIT + halves[:, depth:]
    return payload[:, :depth].reshape(-1, width), codes.reshape(-1)


def sent_block(kappa, lists, slots, counts):
    depth = lists.shape[1]
    live = jnp.arange(depth, dtype=jnp.int32)[None, :] < counts[:, None]
    codes = jnp.where(live, slots + 1, 0)
    return with_codes(gathered_rows(kappa, lists), codes)


def row_blend(own, above, below, top_weight, bottom_weight, width):
    count = own.shape[1]
    top = top_weight * own[:, :width] + (1.0 - top_weight) * above
    bottom = bottom_weight * own[:, count - width :] + (1.0 - bottom_weight) * below
    return jnp.concatenate([top, own[:, width : count - width], bottom], axis=1)


def on_device(kappa, send_list, dest_slot, send_count):
    tile_width = kappa.shape[1]
    rows_axis = lax.axis_size("px")
    cols_axis = lax.axis_size("py")
    band_index = lax.axis_index("px")
    column_index = lax.axis_index("py")
    slot_depth = send_list.shape[2]
    upper_band = jnp.maximum(band_index - 1, 0)
    band_rows = lambda table, band: lax.dynamic_slice_in_dim(table[0], band * cols_axis, cols_axis)
    upper_counts = jnp.where(band_index > 0, band_rows(send_count, upper_band), 0)
    same_sent = sent_block(
        kappa,
        band_rows(send_list, band_index),
        band_rows(dest_slot, band_index),
        band_rows(send_count, band_index),
    )
    rise_sent = sent_block(
        kappa, band_rows(send_list, upper_band), band_rows(dest_slot, upper_band), upper_counts
    )
    arrived = lax.all_to_all(jnp.stack([same_sent, rise_sent], axis=1), "py", 0, 0, tiled=True)
    same_values, same_codes = split_codes(arrived[:, 0], slot_depth)
    rise_values, rise_codes = split_codes(arrived[:, 1], slot_depth)
    rise_total = PATCH_ROWS * PATCH_COLS // tile_width // 4
    rise_live = rise_codes > 0
    rise_place = jnp.where(rise_live, jnp.cumsum(rise_live.astype(jnp.int32)), 0)
    packed_values = one_hot_rows(rise_place, rise_total, rise_values).astype(kappa.dtype)
    packed_picks = rise_place[None, :] == jnp.arange(1, rise_total + 1, dtype=jnp.int32)[:, None]
    packed_codes = jnp.sum(jnp.where(packed_picks, rise_codes[None, :], 0), axis=1)
    packed = with_codes(packed_values.reshape(1, rise_total, tile_width), packed_codes[None])
    raised_values, raised_codes = split_codes(shifted(packed, "px", -1), rise_total)
    slot_total = PATCH_ROWS * PATCH_COLS // tile_width
    patch_tiles = (
        one_hot_rows(same_codes, slot_total, same_values)
        + one_hot_rows(raised_codes, slot_total, raised_values)
    ).astype(kappa.dtype)
    edge_fields, fields = flexion_fields(patch_tiles.reshape(PATCH_ROWS, PATCH_COLS))
    width = tile_width
    last = PATCH_ROWS - width
    left = shifted(edge_fields[:, :, width:], "py", 1)
    right = shifted(edge_fields[:, :, :width], "py", -1)
    above = shifted(fields[:, last:], "px", 1)
    below = shifted(fields[:, :width], "px", -1)
    corners_above = shifted(
        jnp.concatenate([left[:, last:], right[:, last:]], axis=2), "px", 1
    )
    corners_below = shifted(
        jnp.concatenate([left[:, :width], right[:, :width]], axis=2), "px", -1
    )
    above_left, above_right = corners_above[:, :, :width], corners_above[:, :, width:]
    below_left, below_right = corners_below[:, :, :width], corners_below[:, :, width:]
    ramp = (jnp.arange(width, dtype=jnp.float32) + 0.5) / width
    top_weight = jnp.where(band_index > 0, ramp, 1.0)[None, :, None]
    bottom_weight = jnp.where(band_index < rows_axis - 1, ramp[::-1], 1.0)[None, :, None]
    left_weight = jnp.where(column_index > 0, ramp, 1.0)[None, None, :]
    right_weight = jnp.where(column_index < cols_axis - 1, ramp[::-1], 1.0)[None, None, :]
    f32 = lambda x: x.astype(jnp.float32)
    count = fields.shape[1]
    ones = jnp.ones((count - 2 * width,), jnp.float32)
    row_weight = jnp.concatenate([top_weight[0, :, 0], ones, bottom_weight[0, :, 0]])[:, None]
    col_weight = jnp.concatenate([left_weight[0, 0], ones, right_weight[0, 0]])[None, :]
    zero_rows = jnp.zeros((fields.shape[0], count - 2 * width, 1), jnp.float32)
    vertical = jnp.concatenate(
        [f32(above), jnp.broadcast_to(zero_rows, (fields.shape[0], count - 2 * width, count)),
         f32(below)], axis=1
    )
    rows_done = row_weight * f32(fields) + (1.0 - row_weight) * vertical
    side = lambda strip, upper, lower: row_weight * f32(strip) + (1.0 - row_weight) * jnp.concatenate(
        [f32(upper), jnp.broadcast_to(zero_rows, (fields.shape[0], count - 2 * width, width)),
         f32(lower)], axis=1
    )
    left_rows = side(left, above_left, below_left)
    right_rows = side(right, above_right, below_right)
    horizontal = jnp.concatenate(
        [left_rows, jnp.broadcast_to(zero_rows[:, :1], (fields.shape[0], count, count - 2 * width)),
         right_rows], axis=2
    )
    return col_weight * rows_done + (1.0 - col_weight) * horizontal


def solution(mesh):
    placed = (
        P(("px", "py"), None),
        P(("px", "py"), None, None),
        P(("px", "py"), None, None),
        P(("px", "py"), None),
    )
    return jax.shard_map(
        on_device, mesh=mesh, in_specs=placed, out_specs=P(None, "px", "py"), check_vma=False
    )
```

```python
import math

import jax
import ml_dtypes
import numpy as np
import jax.numpy as jnp
from jax import lax
from jax.sharding import PartitionSpec as P

PATCH_ROWS = 512
PATCH_COLS = 512


def shifted(shard, axis, by):
    size = lax.axis_size(axis)
    pairs = [(i, i + by) for i in range(size) if 0 <= i + by < size]
    return lax.ppermute(shard, axis, pairs)


def padded(block, sides, width):
    for axis, dim in sides:
        count = lax.axis_size(axis)
        forward = [(i, i + 1) for i in range(count - 1)]
        backward = [(target, source) for source, target in forward]
        low = lax.ppermute(
            lax.slice_in_dim(block, block.shape[dim] - width, None, axis=dim), axis, forward
        )
        high = lax.ppermute(lax.slice_in_dim(block, 0, width, axis=dim), axis, backward)
        block = jnp.concatenate([low, block, high], axis=dim)
    return block


def dft_tables(length):
    positions = np.arange(length, dtype=np.int64)
    phases = positions[:, None] * positions[None, :] % length
    angles = phases.astype(np.float32) * np.float32(2.0 * math.pi / length)
    return (np.cos(angles).astype(np.float32), np.sin(angles).astype(np.float32))


def table(values):
    return jnp.asarray(values.astype(ml_dtypes.bfloat16))


def wavenumbers(length):
    positions = jnp.arange(length, dtype=jnp.int32)
    signed = positions - length * (positions >= (length + 1) // 2).astype(jnp.int32)
    return signed.astype(jnp.float32) * (2.0 / length)


def dot32(a, b):
    return jnp.dot(a, b, preferred_element_type=jnp.float32)


def flexion_fields(pixels):
    row_count = pixels.shape[0]
    col_count = pixels.shape[1]
    assert row_count == col_count
    cos_np, sin_np = dft_tables(row_count)
    cosine, sine = table(cos_np), table(sin_np)
    n = row_count
    halves = jnp.concatenate([dot32(pixels, cosine), dot32(pixels, sine)], axis=1).astype(
        jnp.bfloat16
    )
    by_cos = dot32(cosine, halves)
    by_sin = dot32(sine, halves)
    real_part = by_cos[:, :n] - by_sin[:, n:]
    imag_part = -(by_sin[:, :n] + by_cos[:, n:])
    across = wavenumbers(col_count)[None, :]
    down = wavenumbers(row_count)[:, None]
    scale = 1.0 / (row_count * col_count)
    power = across * across + down * down
    safe_power = jnp.where(power > 0, power, 1.0)
    cube_real = across * across * across - 3.0 * across * down * down
    cube_imag = 3.0 * across * across * down - down * down * down
    one_real = (-down * real_part - across * imag_part) * scale
    one_imag = (across * real_part - down * imag_part) * scale
    kernel_real = -cube_imag / safe_power
    kernel_imag = cube_real / safe_power
    three_real = (kernel_real * real_part - kernel_imag * imag_part) * scale
    three_imag = (kernel_real * imag_part + kernel_imag * real_part) * scale
    spectra = jnp.concatenate([one_real, three_real, one_imag, three_imag], axis=1).astype(
        jnp.bfloat16
    )
    by_cos = dot32(cosine, spectra)
    by_sin = dot32(sine, spectra)
    columns_done = jnp.concatenate(
        [
            by_cos[:, : 2 * n] - by_sin[:, 2 * n :],
            by_sin[:, : 2 * n] + by_cos[:, 2 * n :],
        ],
        axis=1,
    ).astype(jnp.bfloat16)
    arranged = jnp.concatenate(
        [columns_done[:, k * n : (k + 1) * n] for k in range(4)], axis=0
    )
    width = n // 4
    edge_cols = jnp.concatenate(
        [cosine[:, :width], cosine[:, n - width :], sine[:, :width], sine[:, n - width :]], axis=1
    )
    edge = dot32(arranged, edge_cols)
    edge_cos, edge_sin = edge[:, : 2 * width], edge[:, 2 * width :]
    edge_fields = jnp.stack(
        [
            edge_cos[:n] - edge_sin[2 * n : 3 * n],
            edge_sin[:n] + edge_cos[2 * n : 3 * n],
            edge_cos[n : 2 * n] - edge_sin[3 * n :],
            edge_sin[n : 2 * n] + edge_cos[3 * n :],
        ]
    ).astype(jnp.bfloat16)
    by_cos = dot32(arranged, cosine)
    by_sin = dot32(arranged, sine)
    return edge_fields, jnp.stack(
        [
            by_cos[:n] - by_sin[2 * n : 3 * n],
            by_sin[:n] + by_cos[2 * n : 3 * n],
            by_cos[n : 2 * n] - by_sin[3 * n :],
            by_sin[n : 2 * n] + by_cos[3 * n :],
        ]
    ).astype(jnp.bfloat16)


def blend_edges(extended, has_top, has_bottom, has_left, has_right, width):
    values = extended.astype(jnp.float32)
    row_count = values.shape[1] - 2 * width
    col_count = values.shape[2] - 2 * width
    ramp = (jnp.arange(width, dtype=jnp.float32) + 0.5) / width
    top_weight = jnp.where(has_top, ramp, 1.0)[None, :, None]
    bottom_weight = jnp.where(has_bottom, ramp[::-1], 1.0)[None, :, None]
    middle = values[:, width : width + row_count, :]
    top_band = top_weight * middle[:, :width] + (1.0 - top_weight) * values[:, :width]
    bottom_band = (
        bottom_weight * middle[:, row_count - width :]
        + (1.0 - bottom_weight) * values[:, row_count + width :]
    )
    middle = jnp.concatenate([top_band, middle[:, width : row_count - width], bottom_band], axis=1)
    left_weight = jnp.where(has_left, ramp, 1.0)[None, None, :]
    right_weight = jnp.where(has_right, ramp[::-1], 1.0)[None, None, :]
    inner = middle[:, :, width : width + col_count]
    left_band = left_weight * inner[:, :, :width] + (1.0 - left_weight) * middle[:, :, :width]
    right_band = (
        right_weight * inner[:, :, col_count - width :]
        + (1.0 - right_weight) * middle[:, :, col_count + width :]
    )
    return jnp.concatenate([left_band, inner[:, :, width : col_count - width], right_band], axis=2)


def one_hot_rows(codes, count, values):
    picks = codes[None, :] == jnp.arange(1, count + 1, dtype=jnp.int32)[:, None]
    return jnp.dot(picks.astype(values.dtype), values, preferred_element_type=values.dtype)


def gathered_rows(table_rows, picks):
    chosen = picks.reshape(-1)[:, None] == jnp.arange(table_rows.shape[0], dtype=jnp.int32)
    values = jnp.dot(chosen.astype(table_rows.dtype), table_rows, preferred_element_type=jnp.float32)
    return values.astype(table_rows.dtype).reshape(picks.shape + table_rows.shape[1:])


CODE_SPLIT = 64
CODE_ROWS = 16


def with_codes(values, codes):
    depth, width = values.shape[1], values.shape[2]
    halves = jnp.concatenate([codes // CODE_SPLIT, codes % CODE_SPLIT], axis=1)
    code_rows = halves.reshape(values.shape[0], -1, width).astype(values.dtype)
    pad = jnp.zeros((values.shape[0], CODE_ROWS - code_rows.shape[1], width), values.dtype)
    return jnp.concatenate([values, code_rows, pad], axis=1)


def split_codes(payload, depth):
    width = payload.shape[2]
    used = 2 * depth // width
    halves = payload[:, depth : depth + used].reshape(payload.shape[0], 2 * depth)
    halves = halves.astype(jnp.int32)
    codes = halves[:, :depth] * CODE_SPLIT + halves[:, depth:]
    return payload[:, :depth].reshape(-1, width), codes.reshape(-1)


def sent_block(kappa, lists, slots, counts):
    depth = lists.shape[1]
    live = jnp.arange(depth, dtype=jnp.int32)[None, :] < counts[:, None]
    codes = jnp.where(live, slots + 1, 0)
    return with_codes(gathered_rows(kappa, lists), codes)


def row_blend(own, above, below, top_weight, bottom_weight, width):
    count = own.shape[1]
    top = top_weight * own[:, :width] + (1.0 - top_weight) * above
    bottom = bottom_weight * own[:, count - width :] + (1.0 - bottom_weight) * below
    return jnp.concatenate([top, own[:, width : count - width], bottom], axis=1)


def on_device(kappa, send_list, dest_slot, send_count):
    tile_width = kappa.shape[1]
    rows_axis = lax.axis_size("px")
    cols_axis = lax.axis_size("py")
    band_index = lax.axis_index("px")
    column_index = lax.axis_index("py")
    slot_depth = send_list.shape[2]
    upper_band = jnp.maximum(band_index - 1, 0)
    band_rows = lambda table, band: lax.dynamic_slice_in_dim(table[0], band * cols_axis, cols_axis)
    upper_counts = jnp.where(band_index > 0, band_rows(send_count, upper_band), 0)
    same_sent = sent_block(
        kappa,
        band_rows(send_list, band_index),
        band_rows(dest_slot, band_index),
        band_rows(send_count, band_index),
    )
    rise_sent = sent_block(
        kappa, band_rows(send_list, upper_band), band_rows(dest_slot, upper_band), upper_counts
    )
    arrived = lax.all_to_all(jnp.stack([same_sent, rise_sent], axis=1), "py", 0, 0, tiled=True)
    same_values, same_codes = split_codes(arrived[:, 0], slot_depth)
    rise_values, rise_codes = split_codes(arrived[:, 1], slot_depth)
    rise_total = PATCH_ROWS * PATCH_COLS // tile_width // 4
    rise_live = rise_codes > 0
    rise_place = jnp.where(rise_live, jnp.cumsum(rise_live.astype(jnp.int32)), 0)
    packed_values = one_hot_rows(rise_place, rise_total, rise_values).astype(kappa.dtype)
    code_parts = jnp.stack([rise_codes // CODE_SPLIT, rise_codes % CODE_SPLIT], axis=1)
    packed_parts = one_hot_rows(rise_place, rise_total, code_parts.astype(kappa.dtype))
    packed_parts = packed_parts.astype(jnp.int32)
    packed_codes = packed_parts[:, 0] * CODE_SPLIT + packed_parts[:, 1]
    packed = with_codes(packed_values.reshape(1, rise_total, tile_width), packed_codes[None])
    raised_values, raised_codes = split_codes(shifted(packed, "px", -1), rise_total)
    slot_total = PATCH_ROWS * PATCH_COLS // tile_width
    patch_tiles = (
        one_hot_rows(same_codes, slot_total, same_values)
        + one_hot_rows(raised_codes, slot_total, raised_values)
    ).astype(kappa.dtype)
    edge_fields, fields = flexion_fields(patch_tiles.reshape(PATCH_ROWS, PATCH_COLS))
    width = tile_width
    last = PATCH_ROWS - width
    left = shifted(edge_fields[:, :, width:], "py", 1)
    right = shifted(edge_fields[:, :, :width], "py", -1)
    above = shifted(fields[:, last:], "px", 1)
    below = shifted(fields[:, :width], "px", -1)
    corners_above = shifted(
        jnp.concatenate([left[:, last:], right[:, last:]], axis=2), "px", 1
    )
    corners_below = shifted(
        jnp.concatenate([left[:, :width], right[:, :width]], axis=2), "px", -1
    )
    above_left, above_right = corners_above[:, :, :width], corners_above[:, :, width:]
    below_left, below_right = corners_below[:, :, :width], corners_below[:, :, width:]
    ramp = (jnp.arange(width, dtype=jnp.float32) + 0.5) / width
    top_weight = jnp.where(band_index > 0, ramp, 1.0)[None, :, None]
    bottom_weight = jnp.where(band_index < rows_axis - 1, ramp[::-1], 1.0)[None, :, None]
    left_weight = jnp.where(column_index > 0, ramp, 1.0)[None, None, :]
    right_weight = jnp.where(column_index < cols_axis - 1, ramp[::-1], 1.0)[None, None, :]
    f32 = lambda x: x.astype(jnp.float32)
    count = fields.shape[1]
    ones = jnp.ones((count - 2 * width,), jnp.float32)
    row_weight = jnp.concatenate([top_weight[0, :, 0], ones, bottom_weight[0, :, 0]])[:, None]
    col_weight = jnp.concatenate([left_weight[0, 0], ones, right_weight[0, 0]])[None, :]
    zero_rows = jnp.zeros((fields.shape[0], count - 2 * width, 1), jnp.float32)
    vertical = jnp.concatenate(
        [f32(above), jnp.broadcast_to(zero_rows, (fields.shape[0], count - 2 * width, count)),
         f32(below)], axis=1
    )
    rows_done = row_weight * f32(fields) + (1.0 - row_weight) * vertical
    side = lambda strip, upper, lower: row_weight * f32(strip) + (1.0 - row_weight) * jnp.concatenate(
        [f32(upper), jnp.broadcast_to(zero_rows, (fields.shape[0], count - 2 * width, width)),
         f32(lower)], axis=1
    )
    left_rows = side(left, above_left, below_left)
    right_rows = side(right, above_right, below_right)
    horizontal = jnp.concatenate(
        [left_rows, jnp.broadcast_to(zero_rows[:, :1], (fields.shape[0], count, count - 2 * width)),
         right_rows], axis=2
    )
    return col_weight * rows_done + (1.0 - col_weight) * horizontal


def solution(mesh):
    placed = (
        P(("px", "py"), None),
        P(("px", "py"), None, None),
        P(("px", "py"), None, None),
        P(("px", "py"), None),
    )
    return jax.shard_map(
        on_device, mesh=mesh, in_specs=placed, out_specs=P(None, "px", "py"), check_vma=False
    )
```

```python
import math

import jax
import ml_dtypes
import numpy as np
import jax.numpy as jnp
from jax import lax
from jax.sharding import PartitionSpec as P

PATCH_ROWS = 512
PATCH_COLS = 512


def shifted(shard, axis, by):
    size = lax.axis_size(axis)
    pairs = [(i, i + by) for i in range(size) if 0 <= i + by < size]
    return lax.ppermute(shard, axis, pairs)


def padded(block, sides, width):
    for axis, dim in sides:
        count = lax.axis_size(axis)
        forward = [(i, i + 1) for i in range(count - 1)]
        backward = [(target, source) for source, target in forward]
        low = lax.ppermute(
            lax.slice_in_dim(block, block.shape[dim] - width, None, axis=dim), axis, forward
        )
        high = lax.ppermute(lax.slice_in_dim(block, 0, width, axis=dim), axis, backward)
        block = jnp.concatenate([low, block, high], axis=dim)
    return block


def dft_tables(length):
    positions = np.arange(length, dtype=np.int64)
    phases = positions[:, None] * positions[None, :] % length
    angles = phases.astype(np.float32) * np.float32(2.0 * math.pi / length)
    return (np.cos(angles).astype(np.float32), np.sin(angles).astype(np.float32))


def table(values):
    return jnp.asarray(values.astype(ml_dtypes.bfloat16))


def wavenumbers(length):
    positions = jnp.arange(length, dtype=jnp.int32)
    signed = positions - length * (positions >= (length + 1) // 2).astype(jnp.int32)
    return signed.astype(jnp.float32) * (2.0 / length)


def dot32(a, b):
    return jnp.dot(a, b, preferred_element_type=jnp.float32)


def flexion_fields(pixels):
    row_count = pixels.shape[0]
    col_count = pixels.shape[1]
    assert row_count == col_count
    cos_np, sin_np = dft_tables(row_count)
    cosine, sine = table(cos_np), table(sin_np)
    n = row_count
    halves = jnp.dot(pixels, jnp.concatenate([cosine, sine], axis=1), preferred_element_type=jnp.float32)
    halves = halves.astype(jnp.bfloat16)
    by_cos = dot32(cosine, halves)
    by_sin = dot32(sine, halves)
    real_part = by_cos[:, :n] - by_sin[:, n:]
    imag_part = -(by_sin[:, :n] + by_cos[:, n:])
    across = wavenumbers(col_count)[None, :]
    down = wavenumbers(row_count)[:, None]
    scale = 1.0 / (row_count * col_count)
    power = across * across + down * down
    safe_power = jnp.where(power > 0, power, 1.0)
    cube_real = across * across * across - 3.0 * across * down * down
    cube_imag = 3.0 * across * across * down - down * down * down
    one_real = (-down * real_part - across * imag_part) * scale
    one_imag = (across * real_part - down * imag_part) * scale
    kernel_real = -cube_imag / safe_power
    kernel_imag = cube_real / safe_power
    three_real = (kernel_real * real_part - kernel_imag * imag_part) * scale
    three_imag = (kernel_real * imag_part + kernel_imag * real_part) * scale
    spectra = jnp.concatenate([one_real, three_real, one_imag, three_imag], axis=1).astype(
        jnp.bfloat16
    )
    by_cos = dot32(cosine, spectra)
    by_sin = dot32(sine, spectra)
    columns_done = jnp.concatenate(
        [
            by_cos[:, : 2 * n] - by_sin[:, 2 * n :],
            by_sin[:, : 2 * n] + by_cos[:, 2 * n :],
        ],
        axis=1,
    ).astype(jnp.bfloat16)
    arranged = jnp.concatenate(
        [columns_done[:, k * n : (k + 1) * n] for k in range(4)], axis=0
    )
    width = n // 4
    edge_cols = jnp.concatenate(
        [cosine[:, :width], cosine[:, n - width :], sine[:, :width], sine[:, n - width :]], axis=1
    )
    edge = dot32(arranged, edge_cols)
    edge_cos, edge_sin = edge[:, : 2 * width], edge[:, 2 * width :]
    edge_fields = jnp.stack(
        [
            edge_cos[:n] - edge_sin[2 * n : 3 * n],
            edge_sin[:n] + edge_cos[2 * n : 3 * n],
            edge_cos[n : 2 * n] - edge_sin[3 * n :],
            edge_sin[n : 2 * n] + edge_cos[3 * n :],
        ]
    ).astype(jnp.bfloat16)
    by_cos = dot32(arranged, cosine)
    by_sin = dot32(arranged, sine)
    return edge_fields, jnp.stack(
        [
            by_cos[:n] - by_sin[2 * n : 3 * n],
            by_sin[:n] + by_cos[2 * n : 3 * n],
            by_cos[n : 2 * n] - by_sin[3 * n :],
            by_sin[n : 2 * n] + by_cos[3 * n :],
        ]
    ).astype(jnp.bfloat16)


def blend_edges(extended, has_top, has_bottom, has_left, has_right, width):
    values = extended.astype(jnp.float32)
    row_count = values.shape[1] - 2 * width
    col_count = values.shape[2] - 2 * width
    ramp = (jnp.arange(width, dtype=jnp.float32) + 0.5) / width
    top_weight = jnp.where(has_top, ramp, 1.0)[None, :, None]
    bottom_weight = jnp.where(has_bottom, ramp[::-1], 1.0)[None, :, None]
    middle = values[:, width : width + row_count, :]
    top_band = top_weight * middle[:, :width] + (1.0 - top_weight) * values[:, :width]
    bottom_band = (
        bottom_weight * middle[:, row_count - width :]
        + (1.0 - bottom_weight) * values[:, row_count + width :]
    )
    middle = jnp.concatenate([top_band, middle[:, width : row_count - width], bottom_band], axis=1)
    left_weight = jnp.where(has_left, ramp, 1.0)[None, None, :]
    right_weight = jnp.where(has_right, ramp[::-1], 1.0)[None, None, :]
    inner = middle[:, :, width : width + col_count]
    left_band = left_weight * inner[:, :, :width] + (1.0 - left_weight) * middle[:, :, :width]
    right_band = (
        right_weight * inner[:, :, col_count - width :]
        + (1.0 - right_weight) * middle[:, :, col_count + width :]
    )
    return jnp.concatenate([left_band, inner[:, :, width : col_count - width], right_band], axis=2)


def one_hot_rows(codes, count, values):
    picks = codes[None, :] == jnp.arange(1, count + 1, dtype=jnp.int32)[:, None]
    return jnp.dot(picks.astype(values.dtype), values, preferred_element_type=values.dtype)


def gathered_rows(table_rows, picks):
    chosen = picks.reshape(-1)[:, None] == jnp.arange(table_rows.shape[0], dtype=jnp.int32)
    values = jnp.dot(chosen.astype(table_rows.dtype), table_rows, preferred_element_type=jnp.float32)
    return values.astype(table_rows.dtype).reshape(picks.shape + table_rows.shape[1:])


CODE_SPLIT = 64
CODE_ROWS = 16


def with_codes(values, codes):
    depth, width = values.shape[1], values.shape[2]
    halves = jnp.concatenate([codes // CODE_SPLIT, codes % CODE_SPLIT], axis=1)
    code_rows = halves.reshape(values.shape[0], -1, width).astype(values.dtype)
    pad = jnp.zeros((values.shape[0], CODE_ROWS - code_rows.shape[1], width), values.dtype)
    return jnp.concatenate([values, code_rows, pad], axis=1)


def split_codes(payload, depth):
    width = payload.shape[2]
    used = 2 * depth // width
    halves = payload[:, depth : depth + used].reshape(payload.shape[0], 2 * depth)
    halves = halves.astype(jnp.int32)
    codes = halves[:, :depth] * CODE_SPLIT + halves[:, depth:]
    return payload[:, :depth].reshape(-1, width), codes.reshape(-1)


def sent_block(kappa, lists, slots, counts):
    depth = lists.shape[1]
    live = jnp.arange(depth, dtype=jnp.int32)[None, :] < counts[:, None]
    codes = jnp.where(live, slots + 1, 0)
    return with_codes(gathered_rows(kappa, lists), codes)


def row_blend(own, above, below, top_weight, bottom_weight, width):
    count = own.shape[1]
    top = top_weight * own[:, :width] + (1.0 - top_weight) * above
    bottom = bottom_weight * own[:, count - width :] + (1.0 - bottom_weight) * below
    return jnp.concatenate([top, own[:, width : count - width], bottom], axis=1)


def on_device(kappa, send_list, dest_slot, send_count):
    tile_width = kappa.shape[1]
    rows_axis = lax.axis_size("px")
    cols_axis = lax.axis_size("py")
    band_index = lax.axis_index("px")
    column_index = lax.axis_index("py")
    slot_depth = send_list.shape[2]
    upper_band = jnp.maximum(band_index - 1, 0)
    band_rows = lambda table, band: lax.dynamic_slice_in_dim(table[0], band * cols_axis, cols_axis)
    upper_counts = jnp.where(band_index > 0, band_rows(send_count, upper_band), 0)
    same_sent = sent_block(
        kappa,
        band_rows(send_list, band_index),
        band_rows(dest_slot, band_index),
        band_rows(send_count, band_index),
    )
    rise_sent = sent_block(
        kappa, band_rows(send_list, upper_band), band_rows(dest_slot, upper_band), upper_counts
    )
    arrived = lax.all_to_all(jnp.stack([same_sent, rise_sent], axis=1), "py", 0, 0, tiled=True)
    same_values, same_codes = split_codes(arrived[:, 0], slot_depth)
    rise_values, rise_codes = split_codes(arrived[:, 1], slot_depth)
    rise_total = PATCH_ROWS * PATCH_COLS // tile_width // 4
    rise_live = rise_codes > 0
    rise_place = jnp.where(rise_live, jnp.cumsum(rise_live.astype(jnp.int32)), 0)
    packed_values = one_hot_rows(rise_place, rise_total, rise_values).astype(kappa.dtype)
    packed_picks = rise_place[None, :] == jnp.arange(1, rise_total + 1, dtype=jnp.int32)[:, None]
    packed_codes = jnp.sum(jnp.where(packed_picks, rise_codes[None, :], 0), axis=1)
    packed = with_codes(packed_values.reshape(1, rise_total, tile_width), packed_codes[None])
    raised_values, raised_codes = split_codes(shifted(packed, "px", -1), rise_total)
    slot_total = PATCH_ROWS * PATCH_COLS // tile_width
    patch_tiles = (
        one_hot_rows(same_codes, slot_total, same_values)
        + one_hot_rows(raised_codes, slot_total, raised_values)
    ).astype(kappa.dtype)
    edge_fields, fields = flexion_fields(patch_tiles.reshape(PATCH_ROWS, PATCH_COLS))
    width = tile_width
    last = PATCH_ROWS - width
    left = shifted(edge_fields[:, :, width:], "py", 1)
    right = shifted(edge_fields[:, :, :width], "py", -1)
    above = shifted(fields[:, last:], "px", 1)
    below = shifted(fields[:, :width], "px", -1)
    corners_above = shifted(
        jnp.concatenate([left[:, last:], right[:, last:]], axis=2), "px", 1
    )
    corners_below = shifted(
        jnp.concatenate([left[:, :width], right[:, :width]], axis=2), "px", -1
    )
    above_left, above_right = corners_above[:, :, :width], corners_above[:, :, width:]
    below_left, below_right = corners_below[:, :, :width], corners_below[:, :, width:]
    ramp = (jnp.arange(width, dtype=jnp.float32) + 0.5) / width
    top_weight = jnp.where(band_index > 0, ramp, 1.0)[None, :, None]
    bottom_weight = jnp.where(band_index < rows_axis - 1, ramp[::-1], 1.0)[None, :, None]
    left_weight = jnp.where(column_index > 0, ramp, 1.0)[None, None, :]
    right_weight = jnp.where(column_index < cols_axis - 1, ramp[::-1], 1.0)[None, None, :]
    f32 = lambda x: x.astype(jnp.float32)
    count = fields.shape[1]
    ones = jnp.ones((count - 2 * width,), jnp.float32)
    row_weight = jnp.concatenate([top_weight[0, :, 0], ones, bottom_weight[0, :, 0]])[:, None]
    col_weight = jnp.concatenate([left_weight[0, 0], ones, right_weight[0, 0]])[None, :]
    zero_rows = jnp.zeros((fields.shape[0], count - 2 * width, 1), jnp.float32)
    vertical = jnp.concatenate(
        [f32(above), jnp.broadcast_to(zero_rows, (fields.shape[0], count - 2 * width, count)),
         f32(below)], axis=1
    )
    rows_done = row_weight * f32(fields) + (1.0 - row_weight) * vertical
    side = lambda strip, upper, lower: row_weight * f32(strip) + (1.0 - row_weight) * jnp.concatenate(
        [f32(upper), jnp.broadcast_to(zero_rows, (fields.shape[0], count - 2 * width, width)),
         f32(lower)], axis=1
    )
    left_rows = side(left, above_left, below_left)
    right_rows = side(right, above_right, below_right)
    horizontal = jnp.concatenate(
        [left_rows, jnp.broadcast_to(zero_rows[:, :1], (fields.shape[0], count, count - 2 * width)),
         right_rows], axis=2
    )
    return col_weight * rows_done + (1.0 - col_weight) * horizontal


def solution(mesh):
    placed = (
        P(("px", "py"), None),
        P(("px", "py"), None, None),
        P(("px", "py"), None, None),
        P(("px", "py"), None),
    )
    return jax.shard_map(
        on_device, mesh=mesh, in_specs=placed, out_specs=P(None, "px", "py"), check_vma=False
    )
```

```python
import math

import jax
import ml_dtypes
import numpy as np
import jax.numpy as jnp
from jax import lax
from jax.sharding import PartitionSpec as P

PATCH_ROWS = 512
PATCH_COLS = 512


def shifted(shard, axis, by):
    size = lax.axis_size(axis)
    pairs = [(i, i + by) for i in range(size) if 0 <= i + by < size]
    return lax.ppermute(shard, axis, pairs)


def padded(block, sides, width):
    for axis, dim in sides:
        count = lax.axis_size(axis)
        forward = [(i, i + 1) for i in range(count - 1)]
        backward = [(target, source) for source, target in forward]
        low = lax.ppermute(
            lax.slice_in_dim(block, block.shape[dim] - width, None, axis=dim), axis, forward
        )
        high = lax.ppermute(lax.slice_in_dim(block, 0, width, axis=dim), axis, backward)
        block = jnp.concatenate([low, block, high], axis=dim)
    return block


def dft_tables(length):
    positions = np.arange(length, dtype=np.int64)
    phases = positions[:, None] * positions[None, :] % length
    angles = phases.astype(np.float32) * np.float32(2.0 * math.pi / length)
    return (np.cos(angles).astype(np.float32), np.sin(angles).astype(np.float32))


def table(values):
    return jnp.asarray(values.astype(ml_dtypes.bfloat16))


def wavenumbers(length):
    positions = jnp.arange(length, dtype=jnp.int32)
    signed = positions - length * (positions >= (length + 1) // 2).astype(jnp.int32)
    return signed.astype(jnp.float32) * (2.0 / length)


def dot32(a, b):
    return jnp.dot(a, b, preferred_element_type=jnp.float32)


def flexion_fields(pixels):
    row_count = pixels.shape[0]
    col_count = pixels.shape[1]
    assert row_count == col_count
    cos_np, sin_np = dft_tables(row_count)
    cosine, sine = table(cos_np), table(sin_np)
    n = row_count
    halves = jnp.dot(pixels, jnp.concatenate([cosine, sine], axis=1), preferred_element_type=jnp.float32)
    halves = halves.astype(jnp.bfloat16)
    by_cos = dot32(cosine, halves)
    by_sin = dot32(sine, halves)
    real_part = by_cos[:, :n] - by_sin[:, n:]
    imag_part = -(by_sin[:, :n] + by_cos[:, n:])
    across = wavenumbers(col_count)[None, :]
    down = wavenumbers(row_count)[:, None]
    scale = 1.0 / (row_count * col_count)
    power = across * across + down * down
    safe_power = jnp.where(power > 0, power, 1.0)
    cube_real = across * across * across - 3.0 * across * down * down
    cube_imag = 3.0 * across * across * down - down * down * down
    one_real = (-down * real_part - across * imag_part) * scale
    one_imag = (across * real_part - down * imag_part) * scale
    kernel_real = -cube_imag / safe_power
    kernel_imag = cube_real / safe_power
    three_real = (kernel_real * real_part - kernel_imag * imag_part) * scale
    three_imag = (kernel_real * imag_part + kernel_imag * real_part) * scale
    spectra = jnp.concatenate([one_real, three_real, one_imag, three_imag], axis=1).astype(
        jnp.bfloat16
    )
    by_cos = dot32(cosine, spectra)
    by_sin = dot32(sine, spectra)
    columns_done = jnp.concatenate(
        [
            by_cos[:, : 2 * n] - by_sin[:, 2 * n :],
            by_sin[:, : 2 * n] + by_cos[:, 2 * n :],
        ],
        axis=1,
    ).astype(jnp.bfloat16)
    arranged = jnp.concatenate(
        [columns_done[:, k * n : (k + 1) * n] for k in range(4)], axis=0
    )
    width = n // 4
    edge_cols = jnp.concatenate(
        [cosine[:, :width], cosine[:, n - width :], sine[:, :width], sine[:, n - width :]], axis=1
    )
    edge = dot32(arranged, edge_cols)
    edge_cos, edge_sin = edge[:, : 2 * width], edge[:, 2 * width :]
    edge_fields = jnp.stack(
        [
            edge_cos[:n] - edge_sin[2 * n : 3 * n],
            edge_sin[:n] + edge_cos[2 * n : 3 * n],
            edge_cos[n : 2 * n] - edge_sin[3 * n :],
            edge_sin[n : 2 * n] + edge_cos[3 * n :],
        ]
    ).astype(jnp.bfloat16)
    both = dot32(arranged, jnp.concatenate([cosine, sine], axis=1))
    by_cos, by_sin = both[:, :n], both[:, n:]
    return edge_fields, jnp.stack(
        [
            by_cos[:n] - by_sin[2 * n : 3 * n],
            by_sin[:n] + by_cos[2 * n : 3 * n],
            by_cos[n : 2 * n] - by_sin[3 * n :],
            by_sin[n : 2 * n] + by_cos[3 * n :],
        ]
    ).astype(jnp.bfloat16)


def blend_edges(extended, has_top, has_bottom, has_left, has_right, width):
    values = extended.astype(jnp.float32)
    row_count = values.shape[1] - 2 * width
    col_count = values.shape[2] - 2 * width
    ramp = (jnp.arange(width, dtype=jnp.float32) + 0.5) / width
    top_weight = jnp.where(has_top, ramp, 1.0)[None, :, None]
    bottom_weight = jnp.where(has_bottom, ramp[::-1], 1.0)[None, :, None]
    middle = values[:, width : width + row_count, :]
    top_band = top_weight * middle[:, :width] + (1.0 - top_weight) * values[:, :width]
    bottom_band = (
        bottom_weight * middle[:, row_count - width :]
        + (1.0 - bottom_weight) * values[:, row_count + width :]
    )
    middle = jnp.concatenate([top_band, middle[:, width : row_count - width], bottom_band], axis=1)
    left_weight = jnp.where(has_left, ramp, 1.0)[None, None, :]
    right_weight = jnp.where(has_right, ramp[::-1], 1.0)[None, None, :]
    inner = middle[:, :, width : width + col_count]
    left_band = left_weight * inner[:, :, :width] + (1.0 - left_weight) * middle[:, :, :width]
    right_band = (
        right_weight * inner[:, :, col_count - width :]
        + (1.0 - right_weight) * middle[:, :, col_count + width :]
    )
    return jnp.concatenate([left_band, inner[:, :, width : col_count - width], right_band], axis=2)


def one_hot_rows(codes, count, values):
    picks = codes[None, :] == jnp.arange(1, count + 1, dtype=jnp.int32)[:, None]
    return jnp.dot(picks.astype(values.dtype), values, preferred_element_type=values.dtype)


def gathered_rows(table_rows, picks):
    chosen = picks.reshape(-1)[:, None] == jnp.arange(table_rows.shape[0], dtype=jnp.int32)
    values = jnp.dot(chosen.astype(table_rows.dtype), table_rows, preferred_element_type=jnp.float32)
    return values.astype(table_rows.dtype).reshape(picks.shape + table_rows.shape[1:])


CODE_SPLIT = 64
CODE_ROWS = 16


def with_codes(values, codes):
    depth, width = values.shape[1], values.shape[2]
    halves = jnp.concatenate([codes // CODE_SPLIT, codes % CODE_SPLIT], axis=1)
    code_rows = halves.reshape(values.shape[0], -1, width).astype(values.dtype)
    pad = jnp.zeros((values.shape[0], CODE_ROWS - code_rows.shape[1], width), values.dtype)
    return jnp.concatenate([values, code_rows, pad], axis=1)


def split_codes(payload, depth):
    width = payload.shape[2]
    used = 2 * depth // width
    halves = payload[:, depth : depth + used].reshape(payload.shape[0], 2 * depth)
    halves = halves.astype(jnp.int32)
    codes = halves[:, :depth] * CODE_SPLIT + halves[:, depth:]
    return payload[:, :depth].reshape(-1, width), codes.reshape(-1)


def sent_block(kappa, lists, slots, counts):
    depth = lists.shape[1]
    live = jnp.arange(depth, dtype=jnp.int32)[None, :] < counts[:, None]
    codes = jnp.where(live, slots + 1, 0)
    return with_codes(gathered_rows(kappa, lists), codes)


def row_blend(own, above, below, top_weight, bottom_weight, width):
    count = own.shape[1]
    top = top_weight * own[:, :width] + (1.0 - top_weight) * above
    bottom = bottom_weight * own[:, count - width :] + (1.0 - bottom_weight) * below
    return jnp.concatenate([top, own[:, width : count - width], bottom], axis=1)


def on_device(kappa, send_list, dest_slot, send_count):
    tile_width = kappa.shape[1]
    rows_axis = lax.axis_size("px")
    cols_axis = lax.axis_size("py")
    band_index = lax.axis_index("px")
    column_index = lax.axis_index("py")
    slot_depth = send_list.shape[2]
    upper_band = jnp.maximum(band_index - 1, 0)
    band_rows = lambda table, band: lax.dynamic_slice_in_dim(table[0], band * cols_axis, cols_axis)
    upper_counts = jnp.where(band_index > 0, band_rows(send_count, upper_band), 0)
    same_sent = sent_block(
        kappa,
        band_rows(send_list, band_index),
        band_rows(dest_slot, band_index),
        band_rows(send_count, band_index),
    )
    rise_sent = sent_block(
        kappa, band_rows(send_list, upper_band), band_rows(dest_slot, upper_band), upper_counts
    )
    arrived = lax.all_to_all(jnp.stack([same_sent, rise_sent], axis=1), "py", 0, 0, tiled=True)
    same_values, same_codes = split_codes(arrived[:, 0], slot_depth)
    rise_values, rise_codes = split_codes(arrived[:, 1], slot_depth)
    rise_total = PATCH_ROWS * PATCH_COLS // tile_width // 4
    rise_live = rise_codes > 0
    rise_place = jnp.where(rise_live, jnp.cumsum(rise_live.astype(jnp.int32)), 0)
    packed_values = one_hot_rows(rise_place, rise_total, rise_values).astype(kappa.dtype)
    packed_picks = rise_place[None, :] == jnp.arange(1, rise_total + 1, dtype=jnp.int32)[:, None]
    packed_codes = jnp.sum(jnp.where(packed_picks, rise_codes[None, :], 0), axis=1)
    packed = with_codes(packed_values.reshape(1, rise_total, tile_width), packed_codes[None])
    raised_values, raised_codes = split_codes(shifted(packed, "px", -1), rise_total)
    slot_total = PATCH_ROWS * PATCH_COLS // tile_width
    patch_tiles = (
        one_hot_rows(same_codes, slot_total, same_values)
        + one_hot_rows(raised_codes, slot_total, raised_values)
    ).astype(kappa.dtype)
    edge_fields, fields = flexion_fields(patch_tiles.reshape(PATCH_ROWS, PATCH_COLS))
    width = tile_width
    last = PATCH_ROWS - width
    left = shifted(edge_fields[:, :, width:], "py", 1)
    right = shifted(edge_fields[:, :, :width], "py", -1)
    above = shifted(fields[:, last:], "px", 1)
    below = shifted(fields[:, :width], "px", -1)
    corners_above = shifted(
        jnp.concatenate([left[:, last:], right[:, last:]], axis=2), "px", 1
    )
    corners_below = shifted(
        jnp.concatenate([left[:, :width], right[:, :width]], axis=2), "px", -1
    )
    above_left, above_right = corners_above[:, :, :width], corners_above[:, :, width:]
    below_left, below_right = corners_below[:, :, :width], corners_below[:, :, width:]
    ramp = (jnp.arange(width, dtype=jnp.float32) + 0.5) / width
    top_weight = jnp.where(band_index > 0, ramp, 1.0)[None, :, None]
    bottom_weight = jnp.where(band_index < rows_axis - 1, ramp[::-1], 1.0)[None, :, None]
    left_weight = jnp.where(column_index > 0, ramp, 1.0)[None, None, :]
    right_weight = jnp.where(column_index < cols_axis - 1, ramp[::-1], 1.0)[None, None, :]
    f32 = lambda x: x.astype(jnp.float32)
    count = fields.shape[1]
    ones = jnp.ones((count - 2 * width,), jnp.float32)
    row_weight = jnp.concatenate([top_weight[0, :, 0], ones, bottom_weight[0, :, 0]])[:, None]
    col_weight = jnp.concatenate([left_weight[0, 0], ones, right_weight[0, 0]])[None, :]
    zero_rows = jnp.zeros((fields.shape[0], count - 2 * width, 1), jnp.float32)
    vertical = jnp.concatenate(
        [f32(above), jnp.broadcast_to(zero_rows, (fields.shape[0], count - 2 * width, count)),
         f32(below)], axis=1
    )
    rows_done = row_weight * f32(fields) + (1.0 - row_weight) * vertical
    side = lambda strip, upper, lower: row_weight * f32(strip) + (1.0 - row_weight) * jnp.concatenate(
        [f32(upper), jnp.broadcast_to(zero_rows, (fields.shape[0], count - 2 * width, width)),
         f32(lower)], axis=1
    )
    left_rows = side(left, above_left, below_left)
    right_rows = side(right, above_right, below_right)
    horizontal = jnp.concatenate(
        [left_rows, jnp.broadcast_to(zero_rows[:, :1], (fields.shape[0], count, count - 2 * width)),
         right_rows], axis=2
    )
    return col_weight * rows_done + (1.0 - col_weight) * horizontal


def solution(mesh):
    placed = (
        P(("px", "py"), None),
        P(("px", "py"), None, None),
        P(("px", "py"), None, None),
        P(("px", "py"), None),
    )
    return jax.shard_map(
        on_device, mesh=mesh, in_specs=placed, out_specs=P(None, "px", "py"), check_vma=False
    )
```
